32 devices in a mesh: slab: 4 (over y, core), rot: 8 (over z, x).
Axes of the slice: x: 2, y: 2, z: 4, core: 2. Of those that a mesh axis runs over, the one named last changes fastest.
Arguments:
- receptor: float32 [2, 128, 128, 128], P(None, 'slab'), may hold values from -6 to 6
- ligand_box: float32 [2, 8, 2, 32, 32, 32], P(None, 'rot', None, 'slab'), may hold values from -0.0234375 to 0.0234375
- channel_weight: float32 [2], replicated, may hold values from 0.3 to 3
- rotation_table: float32 [9, 16], replicated, may hold values from -1 to 1, as said below
- ligand_atoms: float32 [3, 128], replicated, may hold values from -0.12 to 0.12
- cluster_center: float32 [64, 3, 128], P('rot'), may hold values from -1.5 to 1.5
- pose_rotation: int32 [8192], P(('slab', 'rot')), may hold values from 0 to 15
- pose_translation: int32 [8192], P(('slab', 'rot')), may hold values from 0 to 2097151
- pose_owner: int32 [8192, 1], P(('slab', 'rot')), may hold values from 0 to 7; in each aligned block of 256 rows (0 to 255, 256 to 511, ...) at most 64 rows name the same one
- pose_member: int32 [8192], P(('slab', 'rot')), may hold values from 0 to 7
Outputs:
- scores: float32 [2, 8, 128, 128, 128], P(None, 'rot', 'slab')
- pose_stats: float32 [10, 8192], P(None, ('slab', 'rot'))
The draws below stay inside these ranges and needn't reach their ends.
Inputs may be any that keep to these rules, and one draw needn't show every extreme that they name: `pose_owner`: the rows of one device name one owner at most 64 times, and some device's rows name some owner exactly 64 times. `rotation_table`: each column is a proper rotation matrix up to float32 rounding, row-major.
All inputs are finite; a program needn't handle non-finite values.
Results may differ from the reference program's by a relative error of at most 0.0003.
Values sent between devices are 32-bit elements; how exact they have to be, the bound alone decides.
No kernel may reach another device: no remote copies, remote signals or barrier semaphores. Data moves between devices by JAX's collectives and lax.ppermute only.
A program may use at most 128 MiB of HBM per device.

```python
import math
import jax
import jax.numpy as jnp
import numpy as np
from jax import lax

N = 128
CH = 2
LB = 32
SETS = 2
P_DEV = 256
ATOMS = 128
CL_DEV = 8
ROTS = 8
POSES = 8192
CLUSTERS = 64
N_ROT = 8


def draw_rotation_table(key, part):
    quat = jax.random.normal(key, (4, SETS * ROTS), jnp.float32)
    quat = quat / jnp.sqrt(jnp.sum(quat * quat, axis=0, keepdims=True) + 1e-06)
    quat_real = quat[0]
    quat_one = quat[1]
    quat_two = quat[2]
    quat_three = quat[3]
    entries = [quat_real * quat_real + quat_one * quat_one - quat_two * quat_two - quat_three * quat_three, 2.0 * (quat_one * quat_two - quat_real * quat_three), 2.0 * (quat_one * quat_three + quat_real * quat_two), 2.0 * (quat_one * quat_two + quat_real * quat_three), quat_real * quat_real - quat_one * quat_one + quat_two * quat_two - quat_three * quat_three, 2.0 * (quat_two * quat_three - quat_real * quat_one), 2.0 * (quat_one * quat_three - quat_real * quat_two), 2.0 * (quat_two * quat_three + quat_real * quat_one), quat_real * quat_real - quat_one * quat_one - quat_two * quat_two + quat_three * quat_three]
    return jnp.clip(jnp.stack(entries, axis=0), -1.0, 1.0)


def touch_ends(drawn, stream_key, smallest, high):
    dims = drawn.shape
    index_at = [jax.random.randint(jax.random.fold_in(stream_key, axis), (), 0, dims[axis]) for axis in range(len(dims))]
    drawn = drawn.at[tuple(index_at)].set(smallest)
    longest = dims.index(max(dims))
    index_at[longest] = (index_at[longest] + 1) % dims[longest]
    return drawn.at[tuple(index_at)].set(high)


def block_scale(stream_key, extent, split, least, high):
    def one(dim, parts):
        heights = jax.random.uniform(jax.random.fold_in(jax.random.fold_in(stream_key, 6), dim), (parts,), jnp.float32, least / len(split), high / len(split))
        return jnp.repeat(jnp.exp(heights), extent[dim] // parts).reshape((-1,) + (1,) * (len(extent) - dim - 1))

    loudness = one(*split[0])
    for cut in split[1:]:
        loudness = loudness * one(*cut)
    return loudness


def deal_out(rng, own, number, rows, count, top, limit, slope):
    ranking = jax.random.permutation(rng, count)
    packed, common = shares(count, rows * top, limit, slope, True), shares(count, rows * top, limit, slope, False)
    places = jnp.arange(count)

    def named(lengths, turn):
        used = int((lengths > 0).sum())
        fixed = max(1, used // 4)
        passed = fixed + (places - fixed + turn * (used - fixed)) % max(1, count - fixed)
        return jnp.zeros((count,), jnp.int32).at[ranking[jnp.where(places < fixed, places, passed)]].set(jnp.asarray(lengths, jnp.int32))

    lengths = jnp.where(number % 4 == 0, named(packed, number // 4), named(common, number - number // 4 - 1))
    mixed = jax.random.permutation(jax.random.fold_in(own, 3), count)
    giver, sink = mixed[0:count // 2 * 2:2], mixed[1:count // 2 * 2:2]
    room = jnp.minimum(lengths[giver] - 1, limit - lengths[sink]) // 2
    room = jnp.where((giver == ranking[0]) | (sink == ranking[0]) | (lengths[sink] == 0), 0, jnp.maximum(room, 0))
    passed = jax.random.randint(jax.random.fold_in(own, 4), (count // 2,), 0, 1 << 20) % (room + 1)
    lengths = lengths.at[giver].add(-passed).at[sink].add(passed)
    members = jnp.searchsorted(jnp.cumsum(lengths), jnp.arange(rows * top), side="right").astype(jnp.int32)
    grid = members.reshape(top, rows).T
    grid = grid[jax.random.permutation(jax.random.fold_in(own, 1), rows)]
    turn = jax.random.randint(jax.random.fold_in(own, 2), (rows, 1), 0, top)
    return jnp.take_along_axis(grid, (jnp.arange(top)[None, :] + turn) % top, axis=1)


def shares(count, total, most, skew, full):
    loads = [(1 << 20) // math.isqrt(grade ** skew) + 1 for grade in range(1, count + 1)]
    largest = most if full else min(most, max(-(-total // count), total * loads[0] // sum(loads)))
    least = 1 if total - largest >= count - 1 else 0
    holding, rest = [largest] + [least] * (count - 1), total - largest - least * (count - 1)
    while rest > 0:
        movable = [i for i in range(1, count) if holding[i] < largest] or [i for i in range(1, count) if holding[i] < most]
        mass, budget = sum([loads[i] for i in movable]), rest
        for i in movable:
            extra = min(most - holding[i], max(1, budget * loads[i] // mass), rest)
            holding[i] = holding[i] + extra
            rest = rest - extra
    return np.array(holding)


def normal_values(key, shape, scale, reach, pieces=(), held_as=jnp.bfloat16):
    gain = block_scale(key, shape, pieces, -0.22, 0.18) if pieces else 1.0
    drawn = jax.random.normal(key, shape, jnp.float32) * scale * gain
    return jnp.minimum(jnp.maximum(drawn, -reach), reach).astype(held_as)


def setup_inputs(seed: int = 0) -> dict:
    key_list = jax.random.split(jax.random.key(seed), 11)
    receptor = normal_values(key_list[0], (CH, N, N, N), 1.0, 6.0, ((1, 4),), jnp.float32)
    ligand_box = normal_values(key_list[1], (SETS, ROTS, CH, LB, LB, LB), (CH * LB ** 3) ** -0.5, 0.0234375, ((1, 8), (3, 4)), jnp.float32)
    channel_weight = jnp.clip(jnp.exp(jax.random.uniform(key_list[2], (CH,), jnp.float32, math.log(0.3), math.log(3.0))), 0.3, 3.0)
    rotation_table = draw_rotation_table(jax.random.fold_in(key_list[10], 71), 0)
    ligand_atoms = jnp.clip(jax.random.uniform(key_list[4], (3, ATOMS), jnp.float32, -0.12, 0.12), -0.12, 0.12)
    cluster_center = normal_values(key_list[5], (CLUSTERS, 3, ATOMS), 0.3, 1.5, ((0, 8),), jnp.float32)
    pose_rotation = touch_ends(jax.random.randint(key_list[6], (POSES,), 0, SETS * ROTS), jax.random.fold_in(key_list[6], 1), 0, (SETS * ROTS) - 1).astype(jnp.int32)
    pose_translation = touch_ends(jax.random.randint(key_list[7], (POSES,), 0, N ** 3), jax.random.fold_in(key_list[7], 1), 0, (N ** 3) - 1).astype(jnp.int32)
    pose_owner_keys = jax.random.split(jax.random.fold_in(key_list[8], 1), POSES // P_DEV)
    pose_owner_turns = jax.random.permutation(jax.random.fold_in(key_list[8], 3), POSES // P_DEV)
    pose_owner = jax.vmap(lambda own, number: deal_out(jax.random.fold_in(key_list[8], 2), own, number, P_DEV, N_ROT, 1, 2 * P_DEV // N_ROT, 2))(pose_owner_keys, pose_owner_turns).reshape((POSES, 1))
    pose_member = touch_ends(jax.random.randint(key_list[9], (POSES,), 0, CL_DEV), jax.random.fold_in(key_list[9], 1), 0, CL_DEV - 1).astype(jnp.int32)
    return dict(receptor=receptor, ligand_box=ligand_box, channel_weight=channel_weight, rotation_table=rotation_table, ligand_atoms=ligand_atoms, cluster_center=cluster_center, pose_rotation=pose_rotation, pose_translation=pose_translation, pose_owner=pose_owner, pose_member=pose_member)


PRECISE = lax.Precision.HIGHEST


def pose_block(rotation_rows, translation_rows, owner_rows, member_rows, rotation_table, ligand_atoms, cluster_center):
    rotation = rotation_table[:, rotation_rows].T.reshape(-1, 3, 3)
    coords = jnp.stack([translation_rows // (N * N), (translation_rows // N) % N, translation_rows % N], axis=1)
    shifts = ((coords + N // 2) % N - N // 2).astype(jnp.float32) / N
    cluster = (owner_rows * CL_DEV + member_rows).astype(jnp.int32)
    center = cluster_center[cluster]
    moved = jnp.einsum("pjk,ka->pja", rotation, ligand_atoms, precision=PRECISE) + shifts[:, :, None]
    spread = moved - center
    mean_square = jnp.mean(jnp.sum(spread * spread, axis=1), axis=1)
    moved_centred = moved - jnp.mean(moved, axis=2, keepdims=True)
    center_centred = center - jnp.mean(center, axis=2, keepdims=True)
    covariance = jnp.einsum("pja,pka->pjk", moved_centred, center_centred, precision=PRECISE)
    return jnp.concatenate([covariance.reshape(-1, 9), mean_square[:, None]], axis=1)


def reference(receptor, ligand_box, channel_weight, rotation_table, ligand_atoms, cluster_center, pose_rotation, pose_translation, pose_owner, pose_member):
    receptor_hat = jnp.fft.fftn(receptor, axes=(1, 2, 3))
    weights = channel_weight[:, None, None, None]
    boxes = ligand_box.reshape(SETS * ROTS, CH, LB, LB, LB)

    def score_one(ligand):
        padded = jnp.pad(ligand, ((0, 0), (0, N - LB), (0, N - LB), (0, N - LB)))
        ligand_hat = jnp.fft.fftn(padded, axes=(1, 2, 3))
        product = jnp.sum(weights * receptor_hat * jnp.conj(ligand_hat), axis=0)
        return jnp.real(jnp.fft.ifftn(product)).astype(jnp.float32)

    scores = lax.map(score_one, boxes).reshape(SETS, ROTS, N, N, N)
    block_count = pose_rotation.shape[0] // P_DEV

    def stats_one(rows):
        return pose_block(rows[0], rows[1], rows[2], rows[3], rotation_table, ligand_atoms, cluster_center)

    stacked = (pose_rotation.reshape(block_count, P_DEV), pose_translation.reshape(block_count, P_DEV), pose_owner[:, 0].reshape(block_count, P_DEV), pose_member.reshape(block_count, P_DEV))
    stats = lax.map(stats_one, stacked)
    pose_stats = stats.reshape(-1, 10).T
    return scores, pose_stats
```

```python
import functools

import jax
import jax.numpy as jnp
from jax import lax
from jax.experimental import pallas as pl
from jax.experimental.pallas import tpu as pltpu
from jax.sharding import PartitionSpec as P

PRECISE = lax.Precision.HIGHEST
SPLIT3 = lax.Precision.HIGH
TWO_PI = 6.283185307179586
F32 = jnp.float32
BF16 = jnp.bfloat16


def phase_tables(rows, cols, length):
    row_index = lax.broadcasted_iota(jnp.int32, (rows, cols), 0)
    col_index = lax.broadcasted_iota(jnp.int32, (rows, cols), 1)
    phase = (row_index * col_index % length).astype(F32) * (TWO_PI / length)
    return (jnp.cos(phase), jnp.sin(phase))


def block2(top_left, top_right, bottom_left, bottom_right):
    top = jnp.concatenate([top_left, top_right], axis=1)
    bottom = jnp.concatenate([bottom_left, bottom_right], axis=1)
    return jnp.concatenate([top, bottom], axis=0)


def hi_lo(table):
    high = table.astype(BF16)
    low = (table - high.astype(F32)).astype(BF16)
    return high, low


def split_dot(a, b_high, b_low, a_left):
    a_high = a.astype(BF16)
    a_low = (a - a_high.astype(F32)).astype(BF16)
    dot = functools.partial(jnp.dot, preferred_element_type=F32)
    if a_left:
        return dot(a_high, b_high) + (dot(a_low, b_high) + dot(a_high, b_low))
    return dot(b_high, a_high) + (dot(b_high, a_low) + dot(b_low, a_high))


def forward_plane_kernel(in_ref, rz_ref, ly_ref, out_ref):
    planes = in_ref.shape[1]
    size = in_ref.shape[3]
    rz_hi, rz_lo = hi_lo(rz_ref[...])
    ly_hi, ly_lo = hi_lo(ly_ref[...])

    def body(p, carry):
        joined = jnp.concatenate([in_ref[0, p], in_ref[1, p]], axis=1)
        along_z = split_dot(joined, rz_hi, rz_lo, True)
        stacked = jnp.concatenate([along_z[:, :size], along_z[:, size:]], axis=0)
        along_y = split_dot(stacked, ly_hi, ly_lo, False)
        out_ref[0, p] = along_y[:size]
        out_ref[1, p] = along_y[size:]
        return carry

    lax.fori_loop(0, planes, body, 0)


def inverse_plane_kernel(in_ref, ly_ref, rz_ref, out_ref):
    planes = in_ref.shape[2]
    size = in_ref.shape[4]
    ly_hi, ly_lo = hi_lo(ly_ref[...])
    rz_hi, rz_lo = hi_lo(rz_ref[...])

    def body(p, carry):
        stacked = jnp.concatenate([in_ref[0, 0, p], in_ref[0, 1, p]], axis=0)
        along_y = split_dot(stacked, ly_hi, ly_lo, False)
        joined = jnp.concatenate([along_y[:size], along_y[size:]], axis=1)
        out_ref[0, p] = split_dot(joined, rz_hi, rz_lo, True)
        return carry

    lax.fori_loop(0, planes, body, 0)


def forward_planes(block, tables, plane_step):
    planes, size = block.shape[1], block.shape[3]
    table_spec = pl.BlockSpec((2 * size, 2 * size), lambda i: (0, 0))
    data_spec = pl.BlockSpec((2, plane_step, size, size), lambda i: (0, i, 0, 0))
    return pl.pallas_call(
        forward_plane_kernel,
        grid=(planes // plane_step,),
        in_specs=[data_spec, table_spec, table_spec],
        out_specs=data_spec,
        out_shape=jax.ShapeDtypeStruct(block.shape, F32),
    )(block, *tables)


def inverse_planes(spectra, tables, plane_step):
    sets, planes, size = spectra.shape[0], spectra.shape[2], spectra.shape[4]
    ly_spec = pl.BlockSpec((2 * size, 2 * size), lambda s, i: (0, 0))
    rz_spec = pl.BlockSpec((2 * size, size), lambda s, i: (0, 0))
    return pl.pallas_call(
        inverse_plane_kernel,
        grid=(sets, planes // plane_step),
        in_specs=[
            pl.BlockSpec((1, 2, plane_step, size, size), lambda s, i: (s, 0, i, 0, 0)),
            ly_spec,
            rz_spec,
        ],
        out_specs=pl.BlockSpec((1, plane_step, size, size), lambda s, i: (s, i, 0, 0)),
        out_shape=jax.ShapeDtypeStruct((sets, planes, size, size), F32),
    )(spectra, *tables)


def score_grids(receptor, ligand_box, channel_weight):
    size = receptor.shape[2]
    slab_count = lax.axis_size("slab")
    part = receptor.shape[1]
    box = ligand_box.shape[4]
    sets = ligand_box.shape[0]
    extra = -(-(box - 1) // part)
    window = part * (1 + extra)
    plane_step = 8

    blocks = [receptor]
    for hop in range(1, extra + 1):
        pairs = [(i, (i - hop) % slab_count) for i in range(slab_count)]
        blocks.append(lax.ppermute(receptor, "slab", perm=pairs))

    cos_n, sin_n = phase_tables(size, size, size)
    rz = block2(cos_n, -sin_n, sin_n, cos_n)
    ly = block2(cos_n, sin_n, -sin_n, cos_n)
    forward_tables = (rz, ly)

    cos_w, sin_w = phase_tables(window, window, window)
    spectrum = None
    for index, planes in enumerate(blocks):
        along_yz = forward_planes(planes, forward_tables, plane_step)
        cols = slice(index * part, (index + 1) * part)
        gx = block2(cos_w[:, cols], sin_w[:, cols], -sin_w[:, cols], cos_w[:, cols])
        term = jnp.einsum(
            "uc,cjk->ujk", gx, along_yz.reshape(2 * part, size, size), precision=SPLIT3
        )
        spectrum = term if spectrum is None else spectrum + term
    rec_real = spectrum[:window]
    rec_imag = spectrum[window:]

    full_box = lax.all_gather(ligand_box, "slab", axis=3, tiled=True)
    lig_real = full_box[:, 0, 0] * channel_weight[0]
    lig_imag = full_box[:, 0, 1] * channel_weight[1]
    cos_b, sin_b = phase_tables(box, size, size)
    z_real = jnp.einsum("sxyz,zk->sxyk", lig_real, cos_b, precision=SPLIT3) + jnp.einsum(
        "sxyz,zk->sxyk", lig_imag, sin_b, precision=SPLIT3
    )
    z_imag = jnp.einsum("sxyz,zk->sxyk", lig_imag, cos_b, precision=SPLIT3) - jnp.einsum(
        "sxyz,zk->sxyk", lig_real, sin_b, precision=SPLIT3
    )
    cos_xb, sin_xb = phase_tables(window, box, window)
    gl = block2(cos_xb, sin_xb, -sin_xb, cos_xb)
    x_both = jnp.einsum(
        "uc,scyk->suyk",
        gl,
        jnp.concatenate([z_real, z_imag], axis=1),
        precision=SPLIT3,
    )
    x_real = x_both[:, :window]
    x_imag = x_both[:, window:]
    cos_yb = cos_b.T
    sin_yb = sin_b.T
    lig_spec_real = jnp.einsum("jy,suyk->sujk", cos_yb, x_real, precision=SPLIT3) + jnp.einsum(
        "jy,suyk->sujk", sin_yb, x_imag, precision=SPLIT3
    )
    lig_spec_imag = jnp.einsum("jy,suyk->sujk", cos_yb, x_imag, precision=SPLIT3) - jnp.einsum(
        "jy,suyk->sujk", sin_yb, x_real, precision=SPLIT3
    )

    prod_real = rec_real[None] * lig_spec_real + rec_imag[None] * lig_spec_imag
    prod_imag = rec_imag[None] * lig_spec_real - rec_real[None] * lig_spec_imag
    product = jnp.concatenate([prod_real, prod_imag], axis=1)

    cos_t, sin_t = phase_tables(part, window, window)
    scale = 1.0 / float(window * size * size)
    hx = block2(cos_t, -sin_t, sin_t, cos_t) * scale
    back_x = jnp.einsum("tc,scjk->stjk", hx, product, precision=SPLIT3)
    back_x = back_x.reshape(sets, 2, part, size, size)

    lyi = block2(cos_n, -sin_n, sin_n, cos_n)
    rzi = jnp.concatenate([cos_n, -sin_n], axis=0)
    inverse_tables = (lyi, rzi)
    grids = inverse_planes(back_x, inverse_tables, plane_step)
    return grids.reshape(sets, 1, part, size, size)


def pose_statistics(
    rotation_table,
    ligand_atoms,
    cluster_center,
    pose_rotation,
    pose_translation,
    pose_owner,
    pose_member,
    size,
):
    all_centers = lax.all_gather(cluster_center, "rot", axis=0, tiled=True)
    local_count = cluster_center.shape[0]
    cluster = pose_owner[:, 0] * local_count + pose_member
    rotation = jnp.take(rotation_table, pose_rotation, axis=1, mode="clip").T.reshape(-1, 3, 3)
    coords = jnp.stack(
        [
            pose_translation // (size * size),
            pose_translation // size % size,
            pose_translation % size,
        ],
        axis=1,
    )
    shifts = ((coords + size // 2) % size - size // 2).astype(F32) / size
    center = jnp.take(all_centers, cluster, axis=0, mode="clip")
    moved = jnp.einsum("pjk,ka->pja", rotation, ligand_atoms, precision=PRECISE) + shifts[:, :, None]
    spread = moved - center
    mean_square = jnp.mean(jnp.sum(spread * spread, axis=1), axis=1)
    moved_centred = moved - jnp.mean(moved, axis=2, keepdims=True)
    center_centred = center - jnp.mean(center, axis=2, keepdims=True)
    covariance = jnp.einsum("pja,pka->pjk", moved_centred, center_centred, precision=PRECISE)
    stats = jnp.concatenate([covariance.reshape(-1, 9), mean_square[:, None]], axis=1)
    return stats.T


def local(
    receptor,
    ligand_box,
    channel_weight,
    rotation_table,
    ligand_atoms,
    cluster_center,
    pose_rotation,
    pose_translation,
    pose_owner,
    pose_member,
):
    size = receptor.shape[2]
    scores = score_grids(receptor, ligand_box, channel_weight)
    pose_stats = pose_statistics(
        rotation_table,
        ligand_atoms,
        cluster_center,
        pose_rotation,
        pose_translation,
        pose_owner,
        pose_member,
        size,
    )
    return (scores, pose_stats)


def solution(mesh):
    return jax.shard_map(
        local,
        mesh=mesh,
        in_specs=(
            P(None, "slab", None, None),
            P(None, "rot", None, "slab", None, None),
            P(),
            P(),
            P(),
            P("rot", None, None),
            P(("slab", "rot")),
            P(("slab", "rot")),
            P(("slab", "rot"), None),
            P(("slab", "rot")),
        ),
        out_specs=(P(None, "rot", "slab", None, None), P(None, ("slab", "rot"))),
        check_vma=False,
    )
```

```python
import functools

import jax
import jax.numpy as jnp
from jax import lax
from jax.experimental import pallas as pl
from jax.experimental.pallas import tpu as pltpu
from jax.sharding import PartitionSpec as P

PRECISE = lax.Precision.HIGHEST
SPLIT3 = lax.Precision.HIGH
TWO_PI = 6.283185307179586
F32 = jnp.float32
BF16 = jnp.bfloat16


def phase_tables(rows, cols, length):
    row_index = lax.broadcasted_iota(jnp.int32, (rows, cols), 0)
    col_index = lax.broadcasted_iota(jnp.int32, (rows, cols), 1)
    phase = (row_index * col_index % length).astype(F32) * (TWO_PI / length)
    return (jnp.cos(phase), jnp.sin(phase))


def block2(top_left, top_right, bottom_left, bottom_right):
    top = jnp.concatenate([top_left, top_right], axis=1)
    bottom = jnp.concatenate([bottom_left, bottom_right], axis=1)
    return jnp.concatenate([top, bottom], axis=0)


def hi_lo(table):
    high = table.astype(BF16)
    low = (table - high.astype(F32)).astype(BF16)
    return high, low


def split_dot(a, b_high, b_low, a_left):
    a_high = a.astype(BF16)
    a_low = (a - a_high.astype(F32)).astype(BF16)
    dot = functools.partial(jnp.dot, preferred_element_type=F32)
    if a_left:
        return dot(a_high, b_high) + (dot(a_low, b_high) + dot(a_high, b_low))
    return dot(b_high, a_high) + (dot(b_high, a_low) + dot(b_low, a_high))


def forward_plane_kernel(in_ref, rz_ref, ly_ref, out_ref):
    planes = in_ref.shape[1]
    size = in_ref.shape[3]
    rz_hi, rz_lo = hi_lo(rz_ref[...])
    ly_hi, ly_lo = hi_lo(ly_ref[...])

    def body(p, carry):
        joined = jnp.concatenate([in_ref[0, p], in_ref[1, p]], axis=1)
        along_z = split_dot(joined, rz_hi, rz_lo, True)
        stacked = jnp.concatenate([along_z[:, :size], along_z[:, size:]], axis=0)
        along_y = split_dot(stacked, ly_hi, ly_lo, False)
        out_ref[0, p] = along_y[:size]
        out_ref[1, p] = along_y[size:]
        return carry

    lax.fori_loop(0, planes, body, 0)


def inverse_plane_kernel(in_ref, ly_ref, rz_ref, out_ref):
    planes = in_ref.shape[2]
    size = in_ref.shape[4]
    ly_hi, ly_lo = hi_lo(ly_ref[...])
    rz_hi, rz_lo = hi_lo(rz_ref[...])

    def body(p, carry):
        stacked = jnp.concatenate([in_ref[0, 0, p], in_ref[0, 1, p]], axis=0)
        along_y = split_dot(stacked, ly_hi, ly_lo, False)
        joined = jnp.concatenate([along_y[:size], along_y[size:]], axis=1)
        out_ref[0, p] = split_dot(joined, rz_hi, rz_lo, True)
        return carry

    lax.fori_loop(0, planes, body, 0)


def forward_planes(block, tables, plane_step):
    planes, size = block.shape[1], block.shape[3]
    table_spec = pl.BlockSpec((2 * size, 2 * size), lambda i: (0, 0))
    data_spec = pl.BlockSpec((2, plane_step, size, size), lambda i: (0, i, 0, 0))
    return pl.pallas_call(
        forward_plane_kernel,
        grid=(planes // plane_step,),
        in_specs=[data_spec, table_spec, table_spec],
        out_specs=data_spec,
        out_shape=jax.ShapeDtypeStruct(block.shape, F32),
    )(block, *tables)


def inverse_planes(spectra, tables, plane_step):
    sets, planes, size = spectra.shape[0], spectra.shape[2], spectra.shape[4]
    ly_spec = pl.BlockSpec((2 * size, 2 * size), lambda s, i: (0, 0))
    rz_spec = pl.BlockSpec((2 * size, size), lambda s, i: (0, 0))
    return pl.pallas_call(
        inverse_plane_kernel,
        grid=(sets, planes // plane_step),
        in_specs=[
            pl.BlockSpec((1, 2, plane_step, size, size), lambda s, i: (s, 0, i, 0, 0)),
            ly_spec,
            rz_spec,
        ],
        out_specs=pl.BlockSpec((1, plane_step, size, size), lambda s, i: (s, i, 0, 0)),
        out_shape=jax.ShapeDtypeStruct((sets, planes, size, size), F32),
    )(spectra, *tables)


def gather_by_sum(piece, axis_name, dim):
    count = lax.axis_size(axis_name)
    index = lax.axis_index(axis_name)
    width = piece.shape[dim]
    shape = list(piece.shape)
    shape[dim] = width * count
    start = [0] * len(shape)
    start[dim] = index * width
    placed = lax.dynamic_update_slice(jnp.zeros(shape, piece.dtype), piece, start)
    return lax.psum(placed, axis_name)


def score_grids(receptor, ligand_box, channel_weight):
    size = receptor.shape[2]
    slab_count = lax.axis_size("slab")
    part = receptor.shape[1]
    box = ligand_box.shape[4]
    sets = ligand_box.shape[0]
    extra = -(-(box - 1) // part)
    window = part * (1 + extra)
    plane_step = 8

    full_box = gather_by_sum(ligand_box, "slab", 3)
    blocks = [receptor]
    for hop in range(1, extra + 1):
        pairs = [(i, (i - hop) % slab_count) for i in range(slab_count)]
        blocks.append(lax.ppermute(receptor, "slab", perm=pairs))

    cos_n, sin_n = phase_tables(size, size, size)
    rz = block2(cos_n, -sin_n, sin_n, cos_n)
    ly = block2(cos_n, sin_n, -sin_n, cos_n)
    forward_tables = (rz, ly)

    cos_w, sin_w = phase_tables(window, window, window)
    rec_real = None
    rec_imag = None
    for index, planes in enumerate(blocks):
        along_yz = forward_planes(planes, forward_tables, plane_step)
        cols = slice(index * part, (index + 1) * part)
        stacked = along_yz.reshape(2 * part, size, size)
        g_real = jnp.concatenate([cos_w[:, cols], sin_w[:, cols]], axis=1)
        g_imag = jnp.concatenate([-sin_w[:, cols], cos_w[:, cols]], axis=1)
        term_real = jnp.einsum("uc,cjk->ujk", g_real, stacked, precision=SPLIT3)
        term_imag = jnp.einsum("uc,cjk->ujk", g_imag, stacked, precision=SPLIT3)
        rec_real = term_real if rec_real is None else rec_real + term_real
        rec_imag = term_imag if rec_imag is None else rec_imag + term_imag

    lig_real = full_box[:, 0, 0] * channel_weight[0]
    lig_imag = full_box[:, 0, 1] * channel_weight[1]
    cos_b, sin_b = phase_tables(box, size, size)
    z_real = jnp.einsum("sxyz,zk->sxyk", lig_real, cos_b, precision=SPLIT3) + jnp.einsum(
        "sxyz,zk->sxyk", lig_imag, sin_b, precision=SPLIT3
    )
    z_imag = jnp.einsum("sxyz,zk->sxyk", lig_imag, cos_b, precision=SPLIT3) - jnp.einsum(
        "sxyz,zk->sxyk", lig_real, sin_b, precision=SPLIT3
    )
    cos_yb = cos_b.T
    sin_yb = sin_b.T
    wy = block2(cos_yb, sin_yb, -sin_yb, cos_yb)
    along_y = jnp.einsum(
        "jc,sxck->sxjk", wy, jnp.concatenate([z_real, z_imag], axis=2), precision=SPLIT3
    )
    along_y = along_y.reshape(sets, box, 2, size, size)
    cos_xb, sin_xb = phase_tables(window, box, window)
    lx_real = jnp.stack([cos_xb, sin_xb], axis=2)
    lx_imag = jnp.stack([-sin_xb, cos_xb], axis=2)
    lig_spec_real = jnp.einsum("uxc,sxcjk->sujk", lx_real, along_y, precision=SPLIT3)
    lig_spec_imag = jnp.einsum("uxc,sxcjk->sujk", lx_imag, along_y, precision=SPLIT3)

    prod_real = rec_real[None] * lig_spec_real + rec_imag[None] * lig_spec_imag
    prod_imag = rec_imag[None] * lig_spec_real - rec_real[None] * lig_spec_imag

    cos_t, sin_t = phase_tables(part, window, window)
    scale = 1.0 / float(window * size * size)
    h_from_real = jnp.concatenate([cos_t, sin_t], axis=0) * scale
    h_from_imag = jnp.concatenate([-sin_t, cos_t], axis=0) * scale
    back_x = jnp.einsum("tu,sujk->stjk", h_from_real, prod_real, precision=SPLIT3) + jnp.einsum(
        "tu,sujk->stjk", h_from_imag, prod_imag, precision=SPLIT3
    )
    back_x = back_x.reshape(sets, 2, part, size, size)

    lyi = block2(cos_n, -sin_n, sin_n, cos_n)
    rzi = jnp.concatenate([cos_n, -sin_n], axis=0)
    inverse_tables = (lyi, rzi)
    grids = inverse_planes(back_x, inverse_tables, plane_step)
    return grids.reshape(sets, 1, part, size, size)


def pose_statistics(
    rotation_table,
    ligand_atoms,
    cluster_center,
    pose_rotation,
    pose_translation,
    pose_owner,
    pose_member,
    size,
):
    all_centers = gather_by_sum(cluster_center, "rot", 0)
    local_count = cluster_center.shape[0]
    cluster = pose_owner[:, 0] * local_count + pose_member
    rotation = jnp.take(rotation_table, pose_rotation, axis=1, mode="clip").T.reshape(-1, 3, 3)
    coords = jnp.stack(
        [
            pose_translation // (size * size),
            pose_translation // size % size,
            pose_translation % size,
        ],
        axis=1,
    )
    shifts = ((coords + size // 2) % size - size // 2).astype(F32) / size
    center = jnp.take(all_centers, cluster, axis=0, mode="clip")
    moved = jnp.einsum("pjk,ka->pja", rotation, ligand_atoms, precision=PRECISE) + shifts[:, :, None]
    spread = moved - center
    mean_square = jnp.mean(jnp.sum(spread * spread, axis=1), axis=1)
    moved_centred = moved - jnp.mean(moved, axis=2, keepdims=True)
    center_centred = center - jnp.mean(center, axis=2, keepdims=True)
    covariance = jnp.einsum("pja,pka->pjk", moved_centred, center_centred, precision=PRECISE)
    stats = jnp.concatenate([covariance.reshape(-1, 9), mean_square[:, None]], axis=1)
    return stats.T


def local(
    receptor,
    ligand_box,
    channel_weight,
    rotation_table,
    ligand_atoms,
    cluster_center,
    pose_rotation,
    pose_translation,
    pose_owner,
    pose_member,
):
    size = receptor.shape[2]
    scores = score_grids(receptor, ligand_box, channel_weight)
    pose_stats = pose_statistics(
        rotation_table,
        ligand_atoms,
        cluster_center,
        pose_rotation,
        pose_translation,
        pose_owner,
        pose_member,
        size,
    )
    return (scores, pose_stats)


def solution(mesh):
    return jax.shard_map(
        local,
        mesh=mesh,
        in_specs=(
            P(None, "slab", None, None),
            P(None, "rot", None, "slab", None, None),
            P(),
            P(),
            P(),
            P("rot", None, None),
            P(("slab", "rot")),
            P(("slab", "rot")),
            P(("slab", "rot"), None),
            P(("slab", "rot")),
        ),
        out_specs=(P(None, "rot", "slab", None, None), P(None, ("slab", "rot"))),
        check_vma=False,
    )
```

```python
import functools

import jax
import jax.numpy as jnp
from jax import lax
from jax.experimental import pallas as pl
from jax.experimental.pallas import tpu as pltpu
from jax.sharding import PartitionSpec as P

PRECISE = lax.Precision.HIGHEST
SPLIT3 = lax.Precision.HIGH
TWO_PI = 6.283185307179586
F32 = jnp.float32
BF16 = jnp.bfloat16


def phase_tables(rows, cols, length):
    row_index = lax.broadcasted_iota(jnp.int32, (rows, cols), 0)
    col_index = lax.broadcasted_iota(jnp.int32, (rows, cols), 1)
    phase = (row_index * col_index % length).astype(F32) * (TWO_PI / length)
    return (jnp.cos(phase), jnp.sin(phase))


def block2(top_left, top_right, bottom_left, bottom_right):
    top = jnp.concatenate([top_left, top_right], axis=1)
    bottom = jnp.concatenate([bottom_left, bottom_right], axis=1)
    return jnp.concatenate([top, bottom], axis=0)


def hi_lo(table):
    high = table.astype(BF16)
    low = (table - high.astype(F32)).astype(BF16)
    return high, low


def split_dot(a, b_high, b_low, a_left):
    a_high = a.astype(BF16)
    a_low = (a - a_high.astype(F32)).astype(BF16)
    dot = functools.partial(jnp.dot, preferred_element_type=F32)
    if a_left:
        return dot(a_high, b_high) + (dot(a_low, b_high) + dot(a_high, b_low))
    return dot(b_high, a_high) + (dot(b_high, a_low) + dot(b_low, a_high))


def forward_plane_kernel(in_ref, rz_ref, ly_ref, out_ref):
    planes = in_ref.shape[1]
    size = out_ref.shape[3]
    rz_hi, rz_lo = hi_lo(rz_ref[...])
    ly_hi, ly_lo = hi_lo(ly_ref[...])

    def body(p, carry):
        joined = jnp.concatenate([in_ref[0, p], in_ref[1, p]], axis=1)
        along_z = split_dot(joined, rz_hi, rz_lo, True)
        stacked = jnp.concatenate([along_z[:, :size], along_z[:, size:]], axis=0)
        along_y = split_dot(stacked, ly_hi, ly_lo, False)
        out_ref[0, p] = along_y[:size]
        out_ref[1, p] = along_y[size:]
        return carry

    lax.fori_loop(0, planes, body, 0)


def inverse_plane_kernel(in_ref, ly_ref, rz_ref, out_ref):
    planes = in_ref.shape[2]
    size = in_ref.shape[4]
    ly_hi, ly_lo = hi_lo(ly_ref[...])
    rz_hi, rz_lo = hi_lo(rz_ref[...])

    def body(p, carry):
        stacked = jnp.concatenate([in_ref[0, 0, p], in_ref[0, 1, p]], axis=0)
        along_y = split_dot(stacked, ly_hi, ly_lo, False)
        joined = jnp.concatenate([along_y[:size], along_y[size:]], axis=1)
        out_ref[0, p] = split_dot(joined, rz_hi, rz_lo, True)
        return carry

    lax.fori_loop(0, planes, body, 0)


def forward_planes(block, tables, plane_step, size):
    planes, rows, cols = block.shape[1], block.shape[2], block.shape[3]
    table_specs = [pl.BlockSpec(t.shape, lambda i: (0, 0)) for t in tables]
    return pl.pallas_call(
        forward_plane_kernel,
        grid=(planes // plane_step,),
        in_specs=[pl.BlockSpec((2, plane_step, rows, cols), lambda i: (0, i, 0, 0))] + table_specs,
        out_specs=pl.BlockSpec((2, plane_step, size, size), lambda i: (0, i, 0, 0)),
        out_shape=jax.ShapeDtypeStruct((2, planes, size, size), F32),
    )(block, *tables)


def cross_kernel(*refs, blocks, sets, box, window, part):
    rec_refs = refs[:blocks]
    lig_ref = refs[blocks]
    g_tables = [hi_lo(t[...]) for t in refs[blocks + 1 : 2 * blocks + 1]]
    gl_hi, gl_lo = hi_lo(refs[2 * blocks + 1][...])
    h_hi, h_lo = hi_lo(refs[2 * blocks + 2][...])
    out_ref = refs[-1]
    rows = out_ref.shape[3]
    lanes = out_ref.shape[4]

    def body(r, carry):
        rec = None
        for b in range(blocks):
            piece = rec_refs[b][:, :, r, :].reshape(2 * part, lanes)
            term = split_dot(piece, g_tables[b][0], g_tables[b][1], False)
            rec = term if rec is None else rec + term
        rec_real = rec[:window]
        rec_imag = rec[window:]
        for s in range(sets):
            piece = lig_ref[:, s * box : (s + 1) * box, r, :].reshape(2 * box, lanes)
            lig = split_dot(piece, gl_hi, gl_lo, False)
            lig_real = lig[:window]
            lig_imag = lig[window:]
            prod = jnp.concatenate(
                [rec_real * lig_real + rec_imag * lig_imag, rec_imag * lig_real - rec_real * lig_imag],
                axis=0,
            )
            back = split_dot(prod, h_hi, h_lo, False)
            out_ref[s, :, :, r, :] = back.reshape(2, part, lanes)
        return carry

    lax.fori_loop(0, rows, body, 0)


def cross_spectra(rec_blocks, lig_yz, g_tables, gl, hx, sets, box, window, row_step):
    part = rec_blocks[0].shape[1]
    size = rec_blocks[0].shape[2]
    lanes = rec_blocks[0].shape[3]
    blocks = len(rec_blocks)
    tables = list(g_tables) + [gl, hx]
    kernel = functools.partial(
        cross_kernel, blocks=blocks, sets=sets, box=box, window=window, part=part
    )
    return pl.pallas_call(
        kernel,
        grid=(size // row_step,),
        in_specs=[pl.BlockSpec((2, part, row_step, lanes), lambda i: (0, 0, i, 0))] * blocks
        + [pl.BlockSpec((2, sets * box, row_step, lanes), lambda i: (0, 0, i, 0))]
        + [pl.BlockSpec(t.shape, lambda i: (0, 0)) for t in tables],
        out_specs=pl.BlockSpec((sets, 2, part, row_step, lanes), lambda i: (0, 0, 0, i, 0)),
        out_shape=jax.ShapeDtypeStruct((sets, 2, part, size, lanes), F32),
    )(*rec_blocks, lig_yz, *tables)


def inverse_planes(spectra, tables, plane_step):
    sets, planes, size = spectra.shape[0], spectra.shape[2], spectra.shape[4]
    ly_spec = pl.BlockSpec((2 * size, 2 * size), lambda s, i: (0, 0))
    rz_spec = pl.BlockSpec((2 * size, size), lambda s, i: (0, 0))
    return pl.pallas_call(
        inverse_plane_kernel,
        grid=(sets, planes // plane_step),
        in_specs=[
            pl.BlockSpec((1, 2, plane_step, size, size), lambda s, i: (s, 0, i, 0, 0)),
            ly_spec,
            rz_spec,
        ],
        out_specs=pl.BlockSpec((1, plane_step, size, size), lambda s, i: (s, i, 0, 0)),
        out_shape=jax.ShapeDtypeStruct((sets, planes, size, size), F32),
    )(spectra, *tables)


def gather_by_sum(piece, axis_name, dim):
    count = lax.axis_size(axis_name)
    index = lax.axis_index(axis_name)
    width = piece.shape[dim]
    shape = list(piece.shape)
    shape[dim] = width * count
    start = [0] * len(shape)
    start[dim] = index * width
    placed = lax.dynamic_update_slice(jnp.zeros(shape, piece.dtype), piece, start)
    return lax.psum(placed, axis_name)


def gather_pieces(piece, axis_name, dim):
    count = lax.axis_size(axis_name)
    if count & (count - 1):
        return gather_by_sum(piece, axis_name, dim)
    index = lax.axis_index(axis_name)
    held = piece
    step = 1
    while step < count:
        pairs = [(i, i ^ step) for i in range(count)]
        other = lax.ppermute(held, axis_name, perm=pairs)
        low_half = (index // step) % 2 == 0
        held = jnp.where(
            low_half,
            jnp.concatenate([held, other], axis=dim),
            jnp.concatenate([other, held], axis=dim),
        )
        step *= 2
    return held


def score_grids(receptor, ligand_box, channel_weight):
    size = receptor.shape[2]
    slab_count = lax.axis_size("slab")
    part = receptor.shape[1]
    box = ligand_box.shape[4]
    sets = ligand_box.shape[0]
    extra = -(-(box - 1) // part)
    window = part * (1 + extra)
    plane_step = 8
    row_step = 8

    full_box = gather_pieces(ligand_box, "slab", 3)
    blocks = [receptor]
    for hop in range(1, extra + 1):
        pairs = [(i, (i - hop) % slab_count) for i in range(slab_count)]
        blocks.append(lax.ppermute(receptor, "slab", perm=pairs))

    cos_n, sin_n = phase_tables(size, size, size)
    rz = block2(cos_n, -sin_n, sin_n, cos_n)
    ly = block2(cos_n, sin_n, -sin_n, cos_n)
    rec_blocks = [forward_planes(planes, (rz, ly), plane_step, size) for planes in blocks]

    lig = jnp.stack(
        [full_box[:, 0, 0] * channel_weight[0], full_box[:, 0, 1] * channel_weight[1]], axis=0
    ).reshape(2, sets * box, box, box)
    cos_b, sin_b = phase_tables(box, size, size)
    rz_box = block2(cos_b, -sin_b, sin_b, cos_b)
    ly_box = block2(cos_b.T, sin_b.T, -sin_b.T, cos_b.T)
    lig_yz = forward_planes(lig, (rz_box, ly_box), plane_step, size)

    cos_w, sin_w = phase_tables(window, window, window)
    g_tables = []
    for index in range(len(blocks)):
        cols = slice(index * part, (index + 1) * part)
        g_tables.append(block2(cos_w[:, cols], sin_w[:, cols], -sin_w[:, cols], cos_w[:, cols]))
    cos_xb, sin_xb = phase_tables(window, box, window)
    gl = block2(cos_xb, sin_xb, -sin_xb, cos_xb)
    cos_t, sin_t = phase_tables(part, window, window)
    scale = 1.0 / float(window * size * size)
    hx = block2(cos_t, -sin_t, sin_t, cos_t) * scale
    back_x = cross_spectra(rec_blocks, lig_yz, g_tables, gl, hx, sets, box, window, row_step)

    lyi = block2(cos_n, -sin_n, sin_n, cos_n)
    rzi = jnp.concatenate([cos_n, -sin_n], axis=0)
    inverse_tables = (lyi, rzi)
    grids = inverse_planes(back_x, inverse_tables, plane_step)
    return grids.reshape(sets, 1, part, size, size)


def pose_statistics(
    rotation_table,
    ligand_atoms,
    cluster_center,
    pose_rotation,
    pose_translation,
    pose_owner,
    pose_member,
    size,
):
    all_centers = gather_pieces(cluster_center, "rot", 0)
    local_count = cluster_center.shape[0]
    cluster = pose_owner[:, 0] * local_count + pose_member
    rotation = jnp.take(rotation_table, pose_rotation, axis=1, mode="clip").T.reshape(-1, 3, 3)
    coords = jnp.stack(
        [
            pose_translation // (size * size),
            pose_translation // size % size,
            pose_translation % size,
        ],
        axis=1,
    )
    shifts = ((coords + size // 2) % size - size // 2).astype(F32) / size
    center = jnp.take(all_centers, cluster, axis=0, mode="clip")
    moved = jnp.einsum("pjk,ka->pja", rotation, ligand_atoms, precision=PRECISE) + shifts[:, :, None]
    spread = moved - center
    mean_square = jnp.mean(jnp.sum(spread * spread, axis=1), axis=1)
    moved_centred = moved - jnp.mean(moved, axis=2, keepdims=True)
    center_centred = center - jnp.mean(center, axis=2, keepdims=True)
    covariance = jnp.einsum("pja,pka->pjk", moved_centred, center_centred, precision=PRECISE)
    stats = jnp.concatenate([covariance.reshape(-1, 9), mean_square[:, None]], axis=1)
    return stats.T


def local(
    receptor,
    ligand_box,
    channel_weight,
    rotation_table,
    ligand_atoms,
    cluster_center,
    pose_rotation,
    pose_translation,
    pose_owner,
    pose_member,
):
    size = receptor.shape[2]
    scores = score_grids(receptor, ligand_box, channel_weight)
    pose_stats = pose_statistics(
        rotation_table,
        ligand_atoms,
        cluster_center,
        pose_rotation,
        pose_translation,
        pose_owner,
        pose_member,
        size,
    )
    return (scores, pose_stats)


def solution(mesh):
    return jax.shard_map(
        local,
        mesh=mesh,
        in_specs=(
            P(None, "slab", None, None),
            P(None, "rot", None, "slab", None, None),
            P(),
            P(),
            P(),
            P("rot", None, None),
            P(("slab", "rot")),
            P(("slab", "rot")),
            P(("slab", "rot"), None),
            P(("slab", "rot")),
        ),
        out_specs=(P(None, "rot", "slab", None, None), P(None, ("slab", "rot"))),
        check_vma=False,
    )
```

```python
import functools

import jax
import jax.numpy as jnp
from jax import lax
from jax.experimental import pallas as pl
from jax.experimental.pallas import tpu as pltpu
from jax.sharding import PartitionSpec as P

PRECISE = lax.Precision.HIGHEST
SPLIT3 = lax.Precision.HIGH
TWO_PI = 6.283185307179586
F32 = jnp.float32
BF16 = jnp.bfloat16


def phase_tables(rows, cols, length):
    row_index = lax.broadcasted_iota(jnp.int32, (rows, cols), 0)
    col_index = lax.broadcasted_iota(jnp.int32, (rows, cols), 1)
    phase = (row_index * col_index % length).astype(F32) * (TWO_PI / length)
    return (jnp.cos(phase), jnp.sin(phase))


def block2(top_left, top_right, bottom_left, bottom_right):
    top = jnp.concatenate([top_left, top_right], axis=1)
    bottom = jnp.concatenate([bottom_left, bottom_right], axis=1)
    return jnp.concatenate([top, bottom], axis=0)


def hi_lo(table):
    high = table.astype(BF16)
    low = (table - high.astype(F32)).astype(BF16)
    return high, low


def split_dot(a, b_high, b_low, a_left):
    a_high = a.astype(BF16)
    a_low = (a - a_high.astype(F32)).astype(BF16)
    dot = functools.partial(jnp.dot, preferred_element_type=F32)
    if a_left:
        return dot(a_high, b_high) + (dot(a_low, b_high) + dot(a_high, b_low))
    return dot(b_high, a_high) + (dot(b_high, a_low) + dot(b_low, a_high))


def forward_plane_kernel(in_ref, rz_ref, ly_ref, out_ref):
    planes, rows, cols = in_ref.shape[1], in_ref.shape[2], in_ref.shape[3]
    size = out_ref.shape[3]
    rz_hi, rz_lo = hi_lo(rz_ref[...])
    ly_hi, ly_lo = hi_lo(ly_ref[...])
    joined = jnp.concatenate(
        [in_ref[0].reshape(planes * rows, cols), in_ref[1].reshape(planes * rows, cols)], axis=1
    )
    along_z = split_dot(joined, rz_hi, rz_lo, True)
    stacked = jnp.concatenate(
        [
            jnp.concatenate(
                [along_z[p * rows : (p + 1) * rows, :size], along_z[p * rows : (p + 1) * rows, size:]],
                axis=0,
            )
            for p in range(planes)
        ],
        axis=1,
    )
    along_y = split_dot(stacked, ly_hi, ly_lo, False)
    for p in range(planes):
        out_ref[0, p] = along_y[:size, p * size : (p + 1) * size]
        out_ref[1, p] = along_y[size:, p * size : (p + 1) * size]


def inverse_plane_kernel(in_ref, ly_ref, rz_ref, out_ref):
    planes = in_ref.shape[2]
    size = in_ref.shape[4]
    ly_hi, ly_lo = hi_lo(ly_ref[...])
    rz_hi, rz_lo = hi_lo(rz_ref[...])
    stacked = jnp.concatenate(
        [jnp.concatenate([in_ref[0, 0, p], in_ref[0, 1, p]], axis=0) for p in range(planes)], axis=1
    )
    along_y = split_dot(stacked, ly_hi, ly_lo, False)
    joined = jnp.concatenate(
        [
            jnp.concatenate(
                [along_y[:size, p * size : (p + 1) * size], along_y[size:, p * size : (p + 1) * size]],
                axis=1,
            )
            for p in range(planes)
        ],
        axis=0,
    )
    out_ref[0] = split_dot(joined, rz_hi, rz_lo, True).reshape(planes, size, size)


def forward_planes(block, tables, plane_step, size):
    planes, rows, cols = block.shape[1], block.shape[2], block.shape[3]
    table_specs = [pl.BlockSpec(t.shape, lambda i: (0, 0)) for t in tables]
    return pl.pallas_call(
        forward_plane_kernel,
        grid=(planes // plane_step,),
        in_specs=[pl.BlockSpec((2, plane_step, rows, cols), lambda i: (0, i, 0, 0))] + table_specs,
        out_specs=pl.BlockSpec((2, plane_step, size, size), lambda i: (0, i, 0, 0)),
        out_shape=jax.ShapeDtypeStruct((2, planes, size, size), F32),
    )(block, *tables)


def cross_kernel(*refs, blocks, sets, box, window, part):
    rec_refs = refs[:blocks]
    lig_ref = refs[blocks]
    g_tables = [hi_lo(t[...]) for t in refs[blocks + 1 : 2 * blocks + 1]]
    gl_hi, gl_lo = hi_lo(refs[2 * blocks + 1][...])
    h_hi, h_lo = hi_lo(refs[2 * blocks + 2][...])
    out_ref = refs[-1]
    rows = out_ref.shape[3]
    lanes = out_ref.shape[4]

    def gathered(ref, lo, count):
        return jnp.concatenate(
            [ref[:, lo : lo + count, r, :].reshape(2 * count, lanes) for r in range(rows)], axis=1
        )

    rec = None
    for b in range(blocks):
        term = split_dot(gathered(rec_refs[b], 0, part), g_tables[b][0], g_tables[b][1], False)
        rec = term if rec is None else rec + term
    rec_real = rec[:window]
    rec_imag = rec[window:]
    for s in range(sets):
        lig = split_dot(gathered(lig_ref, s * box, box), gl_hi, gl_lo, False)
        lig_real = lig[:window]
        lig_imag = lig[window:]
        prod = jnp.concatenate(
            [rec_real * lig_real + rec_imag * lig_imag, rec_imag * lig_real - rec_real * lig_imag],
            axis=0,
        )
        back = split_dot(prod, h_hi, h_lo, False)
        for r in range(rows):
            out_ref[s, :, :, r, :] = back[:, r * lanes : (r + 1) * lanes].reshape(2, part, lanes)


def cross_spectra(rec_blocks, lig_yz, g_tables, gl, hx, sets, box, window, row_step):
    part = rec_blocks[0].shape[1]
    size = rec_blocks[0].shape[2]
    lanes = rec_blocks[0].shape[3]
    blocks = len(rec_blocks)
    tables = list(g_tables) + [gl, hx]
    kernel = functools.partial(
        cross_kernel, blocks=blocks, sets=sets, box=box, window=window, part=part
    )
    return pl.pallas_call(
        kernel,
        grid=(size // row_step,),
        in_specs=[pl.BlockSpec((2, part, row_step, lanes), lambda i: (0, 0, i, 0))] * blocks
        + [pl.BlockSpec((2, sets * box, row_step, lanes), lambda i: (0, 0, i, 0))]
        + [pl.BlockSpec(t.shape, lambda i: (0, 0)) for t in tables],
        out_specs=pl.BlockSpec((sets, 2, part, row_step, lanes), lambda i: (0, 0, 0, i, 0)),
        out_shape=jax.ShapeDtypeStruct((sets, 2, part, size, lanes), F32),
    )(*rec_blocks, lig_yz, *tables)


def inverse_planes(spectra, tables, plane_step):
    sets, planes, size = spectra.shape[0], spectra.shape[2], spectra.shape[4]
    ly_spec = pl.BlockSpec((2 * size, 2 * size), lambda s, i: (0, 0))
    rz_spec = pl.BlockSpec((2 * size, size), lambda s, i: (0, 0))
    return pl.pallas_call(
        inverse_plane_kernel,
        grid=(sets, planes // plane_step),
        in_specs=[
            pl.BlockSpec((1, 2, plane_step, size, size), lambda s, i: (s, 0, i, 0, 0)),
            ly_spec,
            rz_spec,
        ],
        out_specs=pl.BlockSpec((1, plane_step, size, size), lambda s, i: (s, i, 0, 0)),
        out_shape=jax.ShapeDtypeStruct((sets, planes, size, size), F32),
    )(spectra, *tables)


def gather_by_sum(piece, axis_name, dim):
    count = lax.axis_size(axis_name)
    index = lax.axis_index(axis_name)
    width = piece.shape[dim]
    shape = list(piece.shape)
    shape[dim] = width * count
    start = [0] * len(shape)
    start[dim] = index * width
    placed = lax.dynamic_update_slice(jnp.zeros(shape, piece.dtype), piece, start)
    return lax.psum(placed, axis_name)


def gather_pieces(piece, axis_name, dim):
    count = lax.axis_size(axis_name)
    if count & (count - 1):
        return gather_by_sum(piece, axis_name, dim)
    index = lax.axis_index(axis_name)
    held = piece
    step = 1
    while step < count:
        pairs = [(i, i ^ step) for i in range(count)]
        other = lax.ppermute(held, axis_name, perm=pairs)
        low_half = (index // step) % 2 == 0
        held = jnp.where(
            low_half,
            jnp.concatenate([held, other], axis=dim),
            jnp.concatenate([other, held], axis=dim),
        )
        step *= 2
    return held


def score_grids(receptor, ligand_box, channel_weight):
    size = receptor.shape[2]
    slab_count = lax.axis_size("slab")
    part = receptor.shape[1]
    box = ligand_box.shape[4]
    sets = ligand_box.shape[0]
    extra = -(-(box - 1) // part)
    window = part * (1 + extra)
    plane_step = 8
    row_step = 8

    full_box = gather_pieces(ligand_box, "slab", 3)
    full_box, outgoing = lax.optimization_barrier((full_box, receptor))
    blocks = [receptor]
    for hop in range(1, extra + 1):
        pairs = [(i, (i - hop) % slab_count) for i in range(slab_count)]
        blocks.append(lax.ppermute(outgoing, "slab", perm=pairs))

    cos_n, sin_n = phase_tables(size, size, size)
    rz = block2(cos_n, -sin_n, sin_n, cos_n)
    ly = block2(cos_n, sin_n, -sin_n, cos_n)
    rec_blocks = [forward_planes(planes, (rz, ly), plane_step, size) for planes in blocks]

    lig = jnp.stack(
        [full_box[:, 0, 0] * channel_weight[0], full_box[:, 0, 1] * channel_weight[1]], axis=0
    ).reshape(2, sets * box, box, box)
    cos_b, sin_b = phase_tables(box, size, size)
    rz_box = block2(cos_b, -sin_b, sin_b, cos_b)
    ly_box = block2(cos_b.T, sin_b.T, -sin_b.T, cos_b.T)
    lig_yz = forward_planes(lig, (rz_box, ly_box), plane_step, size)

    cos_w, sin_w = phase_tables(window, window, window)
    g_tables = []
    for index in range(len(blocks)):
        cols = slice(index * part, (index + 1) * part)
        g_tables.append(block2(cos_w[:, cols], sin_w[:, cols], -sin_w[:, cols], cos_w[:, cols]))
    cos_xb, sin_xb = phase_tables(window, box, window)
    gl = block2(cos_xb, sin_xb, -sin_xb, cos_xb)
    cos_t, sin_t = phase_tables(part, window, window)
    scale = 1.0 / float(window * size * size)
    hx = block2(cos_t, -sin_t, sin_t, cos_t) * scale
    back_x = cross_spectra(rec_blocks, lig_yz, g_tables, gl, hx, sets, box, window, row_step)

    lyi = block2(cos_n, -sin_n, sin_n, cos_n)
    rzi = jnp.concatenate([cos_n, -sin_n], axis=0)
    inverse_tables = (lyi, rzi)
    grids = inverse_planes(back_x, inverse_tables, plane_step)
    return grids.reshape(sets, 1, part, size, size)


def pose_statistics(
    rotation_table,
    ligand_atoms,
    cluster_center,
    pose_rotation,
    pose_translation,
    pose_owner,
    pose_member,
    size,
):
    all_centers = gather_pieces(cluster_center, "rot", 0)
    local_count = cluster_center.shape[0]
    cluster = pose_owner[:, 0] * local_count + pose_member
    rotation = jnp.take(rotation_table, pose_rotation, axis=1, mode="clip").T.reshape(-1, 3, 3)
    coords = jnp.stack(
        [
            pose_translation // (size * size),
            pose_translation // size % size,
            pose_translation % size,
        ],
        axis=1,
    )
    shifts = ((coords + size // 2) % size - size // 2).astype(F32) / size
    center = jnp.take(all_centers, cluster, axis=0, mode="clip")
    moved = jnp.einsum("pjk,ka->pja", rotation, ligand_atoms, precision=PRECISE) + shifts[:, :, None]
    spread = moved - center
    mean_square = jnp.mean(jnp.sum(spread * spread, axis=1), axis=1)
    moved_centred = moved - jnp.mean(moved, axis=2, keepdims=True)
    center_centred = center - jnp.mean(center, axis=2, keepdims=True)
    covariance = jnp.einsum("pja,pka->pjk", moved_centred, center_centred, precision=PRECISE)
    stats = jnp.concatenate([covariance.reshape(-1, 9), mean_square[:, None]], axis=1)
    return stats.T


def local(
    receptor,
    ligand_box,
    channel_weight,
    rotation_table,
    ligand_atoms,
    cluster_center,
    pose_rotation,
    pose_translation,
    pose_owner,
    pose_member,
):
    size = receptor.shape[2]
    scores = score_grids(receptor, ligand_box, channel_weight)
    pose_stats = pose_statistics(
        rotation_table,
        ligand_atoms,
        cluster_center,
        pose_rotation,
        pose_translation,
        pose_owner,
        pose_member,
        size,
    )
    return (scores, pose_stats)


def solution(mesh):
    return jax.shard_map(
        local,
        mesh=mesh,
        in_specs=(
            P(None, "slab", None, None),
            P(None, "rot", None, "slab", None, None),
            P(),
            P(),
            P(),
            P("rot", None, None),
            P(("slab", "rot")),
            P(("slab", "rot")),
            P(("slab", "rot"), None),
            P(("slab", "rot")),
        ),
        out_specs=(P(None, "rot", "slab", None, None), P(None, ("slab", "rot"))),
        check_vma=False,
    )
```

```python
import functools

import jax
import jax.numpy as jnp
from jax import lax
from jax.experimental import pallas as pl
from jax.experimental.pallas import tpu as pltpu
from jax.sharding import PartitionSpec as P

PRECISE = lax.Precision.HIGHEST
SPLIT3 = lax.Precision.HIGH
TWO_PI = 6.283185307179586
F32 = jnp.float32
BF16 = jnp.bfloat16


def phase_tables(rows, cols, length):
    row_index = lax.broadcasted_iota(jnp.int32, (rows, cols), 0)
    col_index = lax.broadcasted_iota(jnp.int32, (rows, cols), 1)
    phase = (row_index * col_index % length).astype(F32) * (TWO_PI / length)
    return (jnp.cos(phase), jnp.sin(phase))


def block2(top_left, top_right, bottom_left, bottom_right):
    top = jnp.concatenate([top_left, top_right], axis=1)
    bottom = jnp.concatenate([bottom_left, bottom_right], axis=1)
    return jnp.concatenate([top, bottom], axis=0)


def hi_lo(table):
    high = table.astype(BF16)
    low = (table - high.astype(F32)).astype(BF16)
    return high, low


def split_dot(a, b_high, b_low, a_left):
    a_high = a.astype(BF16)
    a_low = (a - a_high.astype(F32)).astype(BF16)
    dot = functools.partial(jnp.dot, preferred_element_type=F32)
    if a_left:
        return dot(a_high, b_high) + (dot(a_low, b_high) + dot(a_high, b_low))
    return dot(b_high, a_high) + (dot(b_high, a_low) + dot(b_low, a_high))


def forward_plane_kernel(in_ref, rz_ref, ly_ref, out_ref):
    planes, rows, cols = in_ref.shape[1], in_ref.shape[2], in_ref.shape[3]
    size = out_ref.shape[3]
    rz_hi, rz_lo = hi_lo(rz_ref[...])
    ly_hi, ly_lo = hi_lo(ly_ref[...])
    joined = jnp.concatenate(
        [in_ref[0].reshape(planes * rows, cols), in_ref[1].reshape(planes * rows, cols)], axis=1
    )
    along_z = split_dot(joined, rz_hi, rz_lo, True)
    stacked = jnp.concatenate(
        [
            jnp.concatenate(
                [along_z[p * rows : (p + 1) * rows, :size], along_z[p * rows : (p + 1) * rows, size:]],
                axis=0,
            )
            for p in range(planes)
        ],
        axis=1,
    )
    along_y = split_dot(stacked, ly_hi, ly_lo, False)
    for p in range(planes):
        out_ref[0, p] = along_y[:size, p * size : (p + 1) * size]
        out_ref[1, p] = along_y[size:, p * size : (p + 1) * size]


def inverse_plane_kernel(in_ref, ly_ref, rz_ref, out_ref):
    planes = in_ref.shape[2]
    size = in_ref.shape[4]
    ly_hi, ly_lo = hi_lo(ly_ref[...])
    rz_hi, rz_lo = hi_lo(rz_ref[...])
    stacked = jnp.concatenate(
        [jnp.concatenate([in_ref[0, 0, p], in_ref[0, 1, p]], axis=0) for p in range(planes)], axis=1
    )
    along_y = split_dot(stacked, ly_hi, ly_lo, False)
    joined = jnp.concatenate(
        [
            jnp.concatenate(
                [along_y[:size, p * size : (p + 1) * size], along_y[size:, p * size : (p + 1) * size]],
                axis=1,
            )
            for p in range(planes)
        ],
        axis=0,
    )
    out_ref[0] = split_dot(joined, rz_hi, rz_lo, True).reshape(planes, size, size)


def forward_planes(block, tables, plane_step, size):
    planes, rows, cols = block.shape[1], block.shape[2], block.shape[3]
    table_specs = [pl.BlockSpec(t.shape, lambda i: (0, 0)) for t in tables]
    return pl.pallas_call(
        forward_plane_kernel,
        grid=(planes // plane_step,),
        in_specs=[pl.BlockSpec((2, plane_step, rows, cols), lambda i: (0, i, 0, 0))] + table_specs,
        out_specs=pl.BlockSpec((2, plane_step, size, size), lambda i: (0, i, 0, 0)),
        out_shape=jax.ShapeDtypeStruct((2, planes, size, size), F32),
    )(block, *tables)


def cross_kernel(*refs, blocks, sets, box, window, part):
    rec_refs = refs[:blocks]
    lig_ref = refs[blocks]
    g_tables = [hi_lo(t[...]) for t in refs[blocks + 1 : 2 * blocks + 1]]
    gl_hi, gl_lo = hi_lo(refs[2 * blocks + 1][...])
    h_hi, h_lo = hi_lo(refs[2 * blocks + 2][...])
    out_ref = refs[-1]
    rows = out_ref.shape[3]
    lanes = out_ref.shape[4]

    def gathered(ref, lo, count):
        return jnp.concatenate(
            [ref[:, lo : lo + count, r, :].reshape(2 * count, lanes) for r in range(rows)], axis=1
        )

    rec = None
    for b in range(blocks):
        term = split_dot(gathered(rec_refs[b], 0, part), g_tables[b][0], g_tables[b][1], False)
        rec = term if rec is None else rec + term
    rec_real = rec[:window]
    rec_imag = rec[window:]
    for s in range(sets):
        lig = split_dot(gathered(lig_ref, s * box, box), gl_hi, gl_lo, False)
        lig_real = lig[:window]
        lig_imag = lig[window:]
        prod = jnp.concatenate(
            [rec_real * lig_real + rec_imag * lig_imag, rec_imag * lig_real - rec_real * lig_imag],
            axis=0,
        )
        back = split_dot(prod, h_hi, h_lo, False)
        for r in range(rows):
            out_ref[s, :, :, r, :] = back[:, r * lanes : (r + 1) * lanes].reshape(2, part, lanes)


def cross_spectra(rec_blocks, lig_yz, g_tables, gl, hx, sets, box, window, row_step):
    part = rec_blocks[0].shape[1]
    size = rec_blocks[0].shape[2]
    lanes = rec_blocks[0].shape[3]
    blocks = len(rec_blocks)
    tables = list(g_tables) + [gl, hx]
    kernel = functools.partial(
        cross_kernel, blocks=blocks, sets=sets, box=box, window=window, part=part
    )
    return pl.pallas_call(
        kernel,
        grid=(size // row_step,),
        in_specs=[pl.BlockSpec((2, part, row_step, lanes), lambda i: (0, 0, i, 0))] * blocks
        + [pl.BlockSpec((2, sets * box, row_step, lanes), lambda i: (0, 0, i, 0))]
        + [pl.BlockSpec(t.shape, lambda i: (0, 0)) for t in tables],
        out_specs=pl.BlockSpec((sets, 2, part, row_step, lanes), lambda i: (0, 0, 0, i, 0)),
        out_shape=jax.ShapeDtypeStruct((sets, 2, part, size, lanes), F32),
    )(*rec_blocks, lig_yz, *tables)


def inverse_planes(spectra, tables, plane_step):
    sets, planes, size = spectra.shape[0], spectra.shape[2], spectra.shape[4]
    ly_spec = pl.BlockSpec((2 * size, 2 * size), lambda s, i: (0, 0))
    rz_spec = pl.BlockSpec((2 * size, size), lambda s, i: (0, 0))
    return pl.pallas_call(
        inverse_plane_kernel,
        grid=(sets, planes // plane_step),
        in_specs=[
            pl.BlockSpec((1, 2, plane_step, size, size), lambda s, i: (s, 0, i, 0, 0)),
            ly_spec,
            rz_spec,
        ],
        out_specs=pl.BlockSpec((1, plane_step, size, size), lambda s, i: (s, i, 0, 0)),
        out_shape=jax.ShapeDtypeStruct((sets, planes, size, size), F32),
    )(spectra, *tables)


def gather_by_sum(piece, axis_name, dim):
    count = lax.axis_size(axis_name)
    index = lax.axis_index(axis_name)
    width = piece.shape[dim]
    shape = list(piece.shape)
    shape[dim] = width * count
    start = [0] * len(shape)
    start[dim] = index * width
    placed = lax.dynamic_update_slice(jnp.zeros(shape, piece.dtype), piece, start)
    return lax.psum(placed, axis_name)


def gather_pieces(piece, axis_name, dim):
    count = lax.axis_size(axis_name)
    if count & (count - 1):
        return gather_by_sum(piece, axis_name, dim)
    index = lax.axis_index(axis_name)
    held = piece
    step = 1
    while step < count:
        pairs = [(i, i ^ step) for i in range(count)]
        other = lax.ppermute(held, axis_name, perm=pairs)
        low_half = (index // step) % 2 == 0
        held = jnp.where(
            low_half,
            jnp.concatenate([held, other], axis=dim),
            jnp.concatenate([other, held], axis=dim),
        )
        step *= 2
    return held


def score_grids(receptor, ligand_box, channel_weight):
    size = receptor.shape[2]
    slab_count = lax.axis_size("slab")
    part = receptor.shape[1]
    box = ligand_box.shape[4]
    sets = ligand_box.shape[0]
    extra = -(-(box - 1) // part)
    window = part * (1 + extra)
    plane_step = 8
    row_step = 16

    lead = ligand_box.shape[:4]
    dense = ligand_box.reshape(lead + (box * box,))
    full_box = gather_pieces(dense, "slab", 3)
    full_box, outgoing = lax.optimization_barrier((full_box, receptor))
    blocks = [receptor]
    for hop in range(1, extra + 1):
        pairs = [(i, (i - hop) % slab_count) for i in range(slab_count)]
        blocks.append(lax.ppermute(outgoing, "slab", perm=pairs))

    cos_n, sin_n = phase_tables(size, size, size)
    rz = block2(cos_n, -sin_n, sin_n, cos_n)
    ly = block2(cos_n, sin_n, -sin_n, cos_n)
    rec_blocks = [forward_planes(planes, (rz, ly), plane_step, size) for planes in blocks]

    lig = jnp.stack(
        [full_box[:, 0, 0] * channel_weight[0], full_box[:, 0, 1] * channel_weight[1]], axis=0
    ).reshape(2, sets * box, box, box)
    cos_b, sin_b = phase_tables(box, size, size)
    rz_box = block2(cos_b, -sin_b, sin_b, cos_b)
    ly_box = block2(cos_b.T, sin_b.T, -sin_b.T, cos_b.T)
    lig_yz = forward_planes(lig, (rz_box, ly_box), plane_step, size)

    cos_w, sin_w = phase_tables(window, window, window)
    g_tables = []
    for index in range(len(blocks)):
        cols = slice(index * part, (index + 1) * part)
        g_tables.append(block2(cos_w[:, cols], sin_w[:, cols], -sin_w[:, cols], cos_w[:, cols]))
    cos_xb, sin_xb = phase_tables(window, box, window)
    gl = block2(cos_xb, sin_xb, -sin_xb, cos_xb)
    cos_t, sin_t = phase_tables(part, window, window)
    scale = 1.0 / float(window * size * size)
    hx = block2(cos_t, -sin_t, sin_t, cos_t) * scale
    back_x = cross_spectra(rec_blocks, lig_yz, g_tables, gl, hx, sets, box, window, row_step)

    lyi = block2(cos_n, -sin_n, sin_n, cos_n)
    rzi = jnp.concatenate([cos_n, -sin_n], axis=0)
    inverse_tables = (lyi, rzi)
    grids = inverse_planes(back_x, inverse_tables, plane_step)
    return grids.reshape(sets, 1, part, size, size)


def pose_statistics(
    rotation_table,
    ligand_atoms,
    cluster_center,
    pose_rotation,
    pose_translation,
    pose_owner,
    pose_member,
    size,
):
    all_centers = gather_pieces(cluster_center, "rot", 0)
    local_count = cluster_center.shape[0]
    cluster = pose_owner[:, 0] * local_count + pose_member
    rotation = jnp.take(rotation_table, pose_rotation, axis=1, mode="clip").T.reshape(-1, 3, 3)
    coords = jnp.stack(
        [
            pose_translation // (size * size),
            pose_translation // size % size,
            pose_translation % size,
        ],
        axis=1,
    )
    shifts = ((coords + size // 2) % size - size // 2).astype(F32) / size
    center = jnp.take(all_centers, cluster, axis=0, mode="clip")
    moved = jnp.einsum("pjk,ka->pja", rotation, ligand_atoms, precision=PRECISE) + shifts[:, :, None]
    spread = moved - center
    mean_square = jnp.mean(jnp.sum(spread * spread, axis=1), axis=1)
    moved_centred = moved - jnp.mean(moved, axis=2, keepdims=True)
    center_centred = center - jnp.mean(center, axis=2, keepdims=True)
    covariance = jnp.einsum("pja,pka->pjk", moved_centred, center_centred, precision=PRECISE)
    stats = jnp.concatenate([covariance.reshape(-1, 9), mean_square[:, None]], axis=1)
    return stats.T


def local(
    receptor,
    ligand_box,
    channel_weight,
    rotation_table,
    ligand_atoms,
    cluster_center,
    pose_rotation,
    pose_translation,
    pose_owner,
    pose_member,
):
    size = receptor.shape[2]
    scores = score_grids(receptor, ligand_box, channel_weight)
    pose_stats = pose_statistics(
        rotation_table,
        ligand_atoms,
        cluster_center,
        pose_rotation,
        pose_translation,
        pose_owner,
        pose_member,
        size,
    )
    return (scores, pose_stats)


def solution(mesh):
    return jax.shard_map(
        local,
        mesh=mesh,
        in_specs=(
            P(None, "slab", None, None),
            P(None, "rot", None, "slab", None, None),
            P(),
            P(),
            P(),
            P("rot", None, None),
            P(("slab", "rot")),
            P(("slab", "rot")),
            P(("slab", "rot"), None),
            P(("slab", "rot")),
        ),
        out_specs=(P(None, "rot", "slab", None, None), P(None, ("slab", "rot"))),
        check_vma=False,
    )
```

```python
import functools

import jax
import jax.numpy as jnp
from jax import lax
from jax.experimental import pallas as pl
from jax.experimental.pallas import tpu as pltpu
from jax.sharding import PartitionSpec as P

PRECISE = lax.Precision.HIGHEST
SPLIT3 = lax.Precision.HIGH
TWO_PI = 6.283185307179586
F32 = jnp.float32
BF16 = jnp.bfloat16


def phase_tables(rows, cols, length):
    row_index = lax.broadcasted_iota(jnp.int32, (rows, cols), 0)
    col_index = lax.broadcasted_iota(jnp.int32, (rows, cols), 1)
    phase = (row_index * col_index % length).astype(F32) * (TWO_PI / length)
    return (jnp.cos(phase), jnp.sin(phase))


def block2(top_left, top_right, bottom_left, bottom_right):
    top = jnp.concatenate([top_left, top_right], axis=1)
    bottom = jnp.concatenate([bottom_left, bottom_right], axis=1)
    return jnp.concatenate([top, bottom], axis=0)


def hi_lo(table):
    high = table.astype(BF16)
    low = (table - high.astype(F32)).astype(BF16)
    return high, low


def split_dot(a, b_high, b_low, a_left):
    a_high = a.astype(BF16)
    a_low = (a - a_high.astype(F32)).astype(BF16)
    dot = functools.partial(jnp.dot, preferred_element_type=F32)
    if a_left:
        return dot(a_high, b_high) + (dot(a_low, b_high) + dot(a_high, b_low))
    return dot(b_high, a_high) + (dot(b_high, a_low) + dot(b_low, a_high))


def forward_plane_kernel(in_ref, rz_ref, ly_ref, out_ref):
    planes, rows, cols = in_ref.shape[1], in_ref.shape[2], in_ref.shape[3]
    size = out_ref.shape[3]
    rz_hi, rz_lo = hi_lo(rz_ref[...])
    ly_hi, ly_lo = hi_lo(ly_ref[...])
    joined = jnp.concatenate(
        [in_ref[0].reshape(planes * rows, cols), in_ref[1].reshape(planes * rows, cols)], axis=1
    )
    along_z = split_dot(joined, rz_hi, rz_lo, True)
    stacked = jnp.concatenate(
        [
            jnp.concatenate(
                [along_z[p * rows : (p + 1) * rows, :size], along_z[p * rows : (p + 1) * rows, size:]],
                axis=0,
            )
            for p in range(planes)
        ],
        axis=1,
    )
    along_y = split_dot(stacked, ly_hi, ly_lo, False)
    for p in range(planes):
        out_ref[0, p] = along_y[:size, p * size : (p + 1) * size]
        out_ref[1, p] = along_y[size:, p * size : (p + 1) * size]


def inverse_plane_kernel(in_ref, ly_ref, rz_ref, out_ref):
    planes = in_ref.shape[2]
    size = in_ref.shape[4]
    ly_hi, ly_lo = hi_lo(ly_ref[...])
    rz_hi, rz_lo = hi_lo(rz_ref[...])
    stacked = jnp.concatenate(
        [jnp.concatenate([in_ref[0, 0, p], in_ref[0, 1, p]], axis=0) for p in range(planes)], axis=1
    )
    along_y = split_dot(stacked, ly_hi, ly_lo, False)
    joined = jnp.concatenate(
        [
            jnp.concatenate(
                [along_y[:size, p * size : (p + 1) * size], along_y[size:, p * size : (p + 1) * size]],
                axis=1,
            )
            for p in range(planes)
        ],
        axis=0,
    )
    out_ref[0] = split_dot(joined, rz_hi, rz_lo, True).reshape(planes, size, size)


def forward_planes(block, tables, plane_step, size):
    planes, rows, cols = block.shape[1], block.shape[2], block.shape[3]
    table_specs = [pl.BlockSpec(t.shape, lambda i: (0, 0)) for t in tables]
    return pl.pallas_call(
        forward_plane_kernel,
        grid=(planes // plane_step,),
        in_specs=[pl.BlockSpec((2, plane_step, rows, cols), lambda i: (0, i, 0, 0))] + table_specs,
        out_specs=pl.BlockSpec((2, plane_step, size, size), lambda i: (0, i, 0, 0)),
        out_shape=jax.ShapeDtypeStruct((2, planes, size, size), F32),
    )(block, *tables)


def cross_kernel(*refs, blocks, sets, box, window, part):
    rec_refs = refs[:blocks]
    lig_ref = refs[blocks]
    g_hi, g_lo = hi_lo(refs[blocks + 1][...])
    gl_hi, gl_lo = hi_lo(refs[blocks + 2][...])
    h_hi, h_lo = hi_lo(refs[blocks + 3][...])
    out_ref = refs[-1]
    rows = out_ref.shape[3]
    lanes = out_ref.shape[4]

    def gathered(ref, lo, count):
        turned = [jnp.swapaxes(ref[c, lo : lo + count], 0, 1) for c in range(2)]
        return jnp.concatenate(
            [jnp.concatenate([turned[0][r], turned[1][r]], axis=0) for r in range(rows)], axis=1
        )

    rec_in = jnp.concatenate([gathered(rec_refs[b], 0, part) for b in range(blocks)], axis=0)
    rec = split_dot(rec_in, g_hi, g_lo, False)
    rec = jnp.concatenate([rec] * sets, axis=1)
    lig_in = jnp.concatenate([gathered(lig_ref, s * box, box) for s in range(sets)], axis=1)
    lig = split_dot(lig_in, gl_hi, gl_lo, False)
    rec_real = rec[:window]
    rec_imag = rec[window:]
    lig_real = lig[:window]
    lig_imag = lig[window:]
    prod = jnp.concatenate(
        [rec_real * lig_real + rec_imag * lig_imag, rec_imag * lig_real - rec_real * lig_imag],
        axis=0,
    )
    back = split_dot(prod, h_hi, h_lo, False)
    width = rows * lanes
    for s in range(sets):
        for c in range(2):
            pieces = jnp.stack(
                [
                    back[c * part : (c + 1) * part, s * width + r * lanes : s * width + (r + 1) * lanes]
                    for r in range(rows)
                ],
                axis=0,
            )
            out_ref[s, c] = jnp.swapaxes(pieces, 0, 1)


def cross_spectra(rec_blocks, lig_yz, g_tables, gl, hx, sets, box, window, row_step):
    part = rec_blocks[0].shape[1]
    size = rec_blocks[0].shape[2]
    lanes = rec_blocks[0].shape[3]
    blocks = len(rec_blocks)
    tables = [jnp.concatenate(g_tables, axis=1), gl, hx]
    kernel = functools.partial(
        cross_kernel, blocks=blocks, sets=sets, box=box, window=window, part=part
    )
    return pl.pallas_call(
        kernel,
        grid=(size // row_step,),
        in_specs=[pl.BlockSpec((2, part, row_step, lanes), lambda i: (0, 0, i, 0))] * blocks
        + [pl.BlockSpec((2, sets * box, row_step, lanes), lambda i: (0, 0, i, 0))]
        + [pl.BlockSpec(t.shape, lambda i: (0, 0)) for t in tables],
        out_specs=pl.BlockSpec((sets, 2, part, row_step, lanes), lambda i: (0, 0, 0, i, 0)),
        out_shape=jax.ShapeDtypeStruct((sets, 2, part, size, lanes), F32),
    )(*rec_blocks, lig_yz, *tables)


def inverse_planes(spectra, tables, plane_step):
    sets, planes, size = spectra.shape[0], spectra.shape[2], spectra.shape[4]
    ly_spec = pl.BlockSpec((2 * size, 2 * size), lambda s, i: (0, 0))
    rz_spec = pl.BlockSpec((2 * size, size), lambda s, i: (0, 0))
    return pl.pallas_call(
        inverse_plane_kernel,
        grid=(sets, planes // plane_step),
        in_specs=[
            pl.BlockSpec((1, 2, plane_step, size, size), lambda s, i: (s, 0, i, 0, 0)),
            ly_spec,
            rz_spec,
        ],
        out_specs=pl.BlockSpec((1, plane_step, size, size), lambda s, i: (s, i, 0, 0)),
        out_shape=jax.ShapeDtypeStruct((sets, planes, size, size), F32),
    )(spectra, *tables)


def gather_by_sum(piece, axis_name, dim):
    count = lax.axis_size(axis_name)
    index = lax.axis_index(axis_name)
    width = piece.shape[dim]
    shape = list(piece.shape)
    shape[dim] = width * count
    start = [0] * len(shape)
    start[dim] = index * width
    placed = lax.dynamic_update_slice(jnp.zeros(shape, piece.dtype), piece, start)
    return lax.psum(placed, axis_name)


def gather_pieces(piece, axis_name, dim):
    count = lax.axis_size(axis_name)
    if count & (count - 1):
        return gather_by_sum(piece, axis_name, dim)
    index = lax.axis_index(axis_name)
    held = piece
    step = 1
    while step < count:
        pairs = [(i, i ^ step) for i in range(count)]
        other = lax.ppermute(held, axis_name, perm=pairs)
        low_half = (index // step) % 2 == 0
        held = jnp.where(
            low_half,
            jnp.concatenate([held, other], axis=dim),
            jnp.concatenate([other, held], axis=dim),
        )
        step *= 2
    return held


def score_grids(receptor, ligand_box, channel_weight):
    size = receptor.shape[2]
    slab_count = lax.axis_size("slab")
    part = receptor.shape[1]
    box = ligand_box.shape[4]
    sets = ligand_box.shape[0]
    extra = -(-(box - 1) // part)
    window = part * (1 + extra)
    plane_step = 8
    row_step = 16

    lead = ligand_box.shape[:4]
    dense = ligand_box.reshape(lead + (box * box,))
    full_box = gather_pieces(dense, "slab", 3)
    full_box, outgoing = lax.optimization_barrier((full_box, receptor))
    blocks = [receptor]
    for hop in range(1, extra + 1):
        pairs = [(i, (i - hop) % slab_count) for i in range(slab_count)]
        blocks.append(lax.ppermute(outgoing, "slab", perm=pairs))

    cos_n, sin_n = phase_tables(size, size, size)
    rz = block2(cos_n, -sin_n, sin_n, cos_n)
    ly = block2(cos_n, sin_n, -sin_n, cos_n)
    rec_blocks = [forward_planes(planes, (rz, ly), plane_step, size) for planes in blocks]

    lig = jnp.stack(
        [full_box[:, 0, 0] * channel_weight[0], full_box[:, 0, 1] * channel_weight[1]], axis=0
    ).reshape(2, sets * box, box, box)
    cos_b, sin_b = phase_tables(box, size, size)
    rz_box = block2(cos_b, -sin_b, sin_b, cos_b)
    ly_box = block2(cos_b.T, sin_b.T, -sin_b.T, cos_b.T)
    lig_yz = forward_planes(lig, (rz_box, ly_box), plane_step, size)

    cos_w, sin_w = phase_tables(window, window, window)
    g_tables = []
    for index in range(len(blocks)):
        cols = slice(index * part, (index + 1) * part)
        g_tables.append(block2(cos_w[:, cols], sin_w[:, cols], -sin_w[:, cols], cos_w[:, cols]))
    cos_xb, sin_xb = phase_tables(window, box, window)
    gl = block2(cos_xb, sin_xb, -sin_xb, cos_xb)
    cos_t, sin_t = phase_tables(part, window, window)
    scale = 1.0 / float(window * size * size)
    hx = block2(cos_t, -sin_t, sin_t, cos_t) * scale
    back_x = cross_spectra(rec_blocks, lig_yz, g_tables, gl, hx, sets, box, window, row_step)

    lyi = block2(cos_n, -sin_n, sin_n, cos_n)
    rzi = jnp.concatenate([cos_n, -sin_n], axis=0)
    inverse_tables = (lyi, rzi)
    grids = inverse_planes(back_x, inverse_tables, plane_step)
    return grids.reshape(sets, 1, part, size, size)


def pose_statistics(
    rotation_table,
    ligand_atoms,
    cluster_center,
    pose_rotation,
    pose_translation,
    pose_owner,
    pose_member,
    size,
):
    all_centers = gather_pieces(cluster_center, "rot", 0)
    local_count = cluster_center.shape[0]
    cluster = pose_owner[:, 0] * local_count + pose_member
    rotation = jnp.take(rotation_table, pose_rotation, axis=1, mode="clip").T.reshape(-1, 3, 3)
    coords = jnp.stack(
        [
            pose_translation // (size * size),
            pose_translation // size % size,
            pose_translation % size,
        ],
        axis=1,
    )
    shifts = ((coords + size // 2) % size - size // 2).astype(F32) / size
    center = jnp.take(all_centers, cluster, axis=0, mode="clip")
    moved = jnp.einsum("pjk,ka->pja", rotation, ligand_atoms, precision=PRECISE) + shifts[:, :, None]
    spread = moved - center
    mean_square = jnp.mean(jnp.sum(spread * spread, axis=1), axis=1)
    moved_centred = moved - jnp.mean(moved, axis=2, keepdims=True)
    center_centred = center - jnp.mean(center, axis=2, keepdims=True)
    covariance = jnp.einsum("pja,pka->pjk", moved_centred, center_centred, precision=PRECISE)
    stats = jnp.concatenate([covariance.reshape(-1, 9), mean_square[:, None]], axis=1)
    return stats.T


def local(
    receptor,
    ligand_box,
    channel_weight,
    rotation_table,
    ligand_atoms,
    cluster_center,
    pose_rotation,
    pose_translation,
    pose_owner,
    pose_member,
):
    size = receptor.shape[2]
    scores = score_grids(receptor, ligand_box, channel_weight)
    pose_stats = pose_statistics(
        rotation_table,
        ligand_atoms,
        cluster_center,
        pose_rotation,
        pose_translation,
        pose_owner,
        pose_member,
        size,
    )
    return (scores, pose_stats)


def solution(mesh):
    return jax.shard_map(
        local,
        mesh=mesh,
        in_specs=(
            P(None, "slab", None, None),
            P(None, "rot", None, "slab", None, None),
            P(),
            P(),
            P(),
            P("rot", None, None),
            P(("slab", "rot")),
            P(("slab", "rot")),
            P(("slab", "rot"), None),
            P(("slab", "rot")),
        ),
        out_specs=(P(None, "rot", "slab", None, None), P(None, ("slab", "rot"))),
        check_vma=False,
    )
```

```python
import functools

import jax
import jax.numpy as jnp
from jax import lax
from jax.experimental import pallas as pl
from jax.experimental.pallas import tpu as pltpu
from jax.sharding import PartitionSpec as P

PRECISE = lax.Precision.HIGHEST
SPLIT3 = lax.Precision.HIGH
TWO_PI = 6.283185307179586
F32 = jnp.float32
BF16 = jnp.bfloat16


def phase_tables(rows, cols, length):
    row_index = lax.broadcasted_iota(jnp.int32, (rows, cols), 0)
    col_index = lax.broadcasted_iota(jnp.int32, (rows, cols), 1)
    phase = (row_index * col_index % length).astype(F32) * (TWO_PI / length)
    return (jnp.cos(phase), jnp.sin(phase))


def block2(top_left, top_right, bottom_left, bottom_right):
    top = jnp.concatenate([top_left, top_right], axis=1)
    bottom = jnp.concatenate([bottom_left, bottom_right], axis=1)
    return jnp.concatenate([top, bottom], axis=0)


def hi_lo(table):
    high = table.astype(BF16)
    low = (table - high.astype(F32)).astype(BF16)
    return high, low


def split_dot(a, b_high, b_low, a_left):
    a_high = a.astype(BF16)
    a_low = (a - a_high.astype(F32)).astype(BF16)
    dot = functools.partial(jnp.dot, preferred_element_type=F32)
    if a_left:
        return dot(a_high, b_high) + (dot(a_low, b_high) + dot(a_high, b_low))
    return dot(b_high, a_high) + (dot(b_high, a_low) + dot(b_low, a_high))


def forward_plane_kernel(in_ref, rz_ref, ly_ref, out_ref):
    planes, rows, cols = in_ref.shape[1], in_ref.shape[2], in_ref.shape[3]
    size = out_ref.shape[3]
    rz_hi, rz_lo = hi_lo(rz_ref[...])
    ly_hi, ly_lo = hi_lo(ly_ref[...])
    joined = jnp.concatenate(
        [in_ref[0].reshape(planes * rows, cols), in_ref[1].reshape(planes * rows, cols)], axis=1
    )
    along_z = split_dot(joined, rz_hi, rz_lo, True)
    stacked = jnp.concatenate(
        [
            jnp.concatenate(
                [along_z[p * rows : (p + 1) * rows, :size], along_z[p * rows : (p + 1) * rows, size:]],
                axis=0,
            )
            for p in range(planes)
        ],
        axis=1,
    )
    along_y = split_dot(stacked, ly_hi, ly_lo, False)
    for p in range(planes):
        out_ref[0, p] = along_y[:size, p * size : (p + 1) * size]
        out_ref[1, p] = along_y[size:, p * size : (p + 1) * size]


def inverse_plane_kernel(in_ref, ly_ref, rz_ref, out_ref):
    planes = in_ref.shape[2]
    size = in_ref.shape[4]
    ly_hi, ly_lo = hi_lo(ly_ref[...])
    rz_hi, rz_lo = hi_lo(rz_ref[...])
    stacked = jnp.concatenate(
        [jnp.concatenate([in_ref[0, 0, p], in_ref[0, 1, p]], axis=0) for p in range(planes)], axis=1
    )
    along_y = split_dot(stacked, ly_hi, ly_lo, False)
    joined = jnp.concatenate(
        [
            jnp.concatenate(
                [along_y[:size, p * size : (p + 1) * size], along_y[size:, p * size : (p + 1) * size]],
                axis=1,
            )
            for p in range(planes)
        ],
        axis=0,
    )
    out_ref[0] = split_dot(joined, rz_hi, rz_lo, True).reshape(planes, size, size)


def forward_planes(block, tables, plane_step, size):
    planes, rows, cols = block.shape[1], block.shape[2], block.shape[3]
    table_specs = [pl.BlockSpec(t.shape, lambda i: (0, 0)) for t in tables]
    return pl.pallas_call(
        forward_plane_kernel,
        grid=(planes // plane_step,),
        in_specs=[pl.BlockSpec((2, plane_step, rows, cols), lambda i: (0, i, 0, 0))] + table_specs,
        out_specs=pl.BlockSpec((2, plane_step, size, size), lambda i: (0, i, 0, 0)),
        out_shape=jax.ShapeDtypeStruct((2, planes, size, size), F32),
    )(block, *tables)


def cross_kernel(*refs, blocks, sets, box, window, part):
    rec_refs = refs[:blocks]
    lig_ref = refs[blocks]
    g_hi, g_lo = hi_lo(refs[blocks + 1][...])
    gl_hi, gl_lo = hi_lo(refs[blocks + 2][...])
    h_hi, h_lo = hi_lo(refs[blocks + 3][...])
    out_ref = refs[-1]
    rows = out_ref.shape[3]
    lanes = out_ref.shape[4]

    def gathered(ref, lo, count):
        turned = [jnp.swapaxes(ref[c, lo : lo + count], 0, 1) for c in range(2)]
        return jnp.concatenate(
            [jnp.concatenate([turned[0][r], turned[1][r]], axis=0) for r in range(rows)], axis=1
        )

    rec_in = jnp.concatenate(
        [gathered(rec_refs[b], 0, rec_refs[b].shape[1]) for b in range(blocks)], axis=0
    )
    rec = split_dot(rec_in, g_hi, g_lo, False)
    rec = jnp.concatenate([rec] * sets, axis=1)
    lig_in = jnp.concatenate([gathered(lig_ref, s * box, box) for s in range(sets)], axis=1)
    lig = split_dot(lig_in, gl_hi, gl_lo, False)
    rec_real = rec[:window]
    rec_imag = rec[window:]
    lig_real = lig[:window]
    lig_imag = lig[window:]
    prod = jnp.concatenate(
        [rec_real * lig_real + rec_imag * lig_imag, rec_imag * lig_real - rec_real * lig_imag],
        axis=0,
    )
    back = split_dot(prod, h_hi, h_lo, False)
    width = rows * lanes
    for s in range(sets):
        for c in range(2):
            pieces = jnp.stack(
                [
                    back[c * part : (c + 1) * part, s * width + r * lanes : s * width + (r + 1) * lanes]
                    for r in range(rows)
                ],
                axis=0,
            )
            out_ref[s, c] = jnp.swapaxes(pieces, 0, 1)


def cross_spectra(rec_blocks, lig_yz, g_tables, gl, hx, sets, box, window, row_step):
    part = rec_blocks[0].shape[1]
    size = rec_blocks[0].shape[2]
    lanes = rec_blocks[0].shape[3]
    blocks = len(rec_blocks)
    tables = [jnp.concatenate(g_tables, axis=1), gl, hx]
    kernel = functools.partial(
        cross_kernel, blocks=blocks, sets=sets, box=box, window=window, part=part
    )
    return pl.pallas_call(
        kernel,
        grid=(size // row_step,),
        in_specs=[pl.BlockSpec((2, b.shape[1], row_step, lanes), lambda i: (0, 0, i, 0)) for b in rec_blocks]
        + [pl.BlockSpec((2, sets * box, row_step, lanes), lambda i: (0, 0, i, 0))]
        + [pl.BlockSpec(t.shape, lambda i: (0, 0)) for t in tables],
        out_specs=pl.BlockSpec((sets, 2, part, row_step, lanes), lambda i: (0, 0, 0, i, 0)),
        out_shape=jax.ShapeDtypeStruct((sets, 2, part, size, lanes), F32),
    )(*rec_blocks, lig_yz, *tables)


def inverse_planes(spectra, tables, plane_step):
    sets, planes, size = spectra.shape[0], spectra.shape[2], spectra.shape[4]
    ly_spec = pl.BlockSpec((2 * size, 2 * size), lambda s, i: (0, 0))
    rz_spec = pl.BlockSpec((2 * size, size), lambda s, i: (0, 0))
    return pl.pallas_call(
        inverse_plane_kernel,
        grid=(sets, planes // plane_step),
        in_specs=[
            pl.BlockSpec((1, 2, plane_step, size, size), lambda s, i: (s, 0, i, 0, 0)),
            ly_spec,
            rz_spec,
        ],
        out_specs=pl.BlockSpec((1, plane_step, size, size), lambda s, i: (s, i, 0, 0)),
        out_shape=jax.ShapeDtypeStruct((sets, planes, size, size), F32),
    )(spectra, *tables)


def gather_by_sum(piece, axis_name, dim):
    count = lax.axis_size(axis_name)
    index = lax.axis_index(axis_name)
    width = piece.shape[dim]
    shape = list(piece.shape)
    shape[dim] = width * count
    start = [0] * len(shape)
    start[dim] = index * width
    placed = lax.dynamic_update_slice(jnp.zeros(shape, piece.dtype), piece, start)
    return lax.psum(placed, axis_name)


def gather_pieces(piece, axis_name, dim):
    count = lax.axis_size(axis_name)
    if count & (count - 1):
        return gather_by_sum(piece, axis_name, dim)
    index = lax.axis_index(axis_name)
    held = piece
    step = 1
    while step < count:
        pairs = [(i, i ^ step) for i in range(count)]
        other = lax.ppermute(held, axis_name, perm=pairs)
        low_half = (index // step) % 2 == 0
        held = jnp.where(
            low_half,
            jnp.concatenate([held, other], axis=dim),
            jnp.concatenate([other, held], axis=dim),
        )
        step *= 2
    return held


def score_grids(receptor, ligand_box, channel_weight):
    size = receptor.shape[2]
    slab_count = lax.axis_size("slab")
    part = receptor.shape[1]
    box = ligand_box.shape[4]
    sets = ligand_box.shape[0]
    extra = -(-(box - 1) // part)
    window = part * (1 + extra)
    plane_step = 8
    row_step = 16

    lead = ligand_box.shape[:4]
    dense = ligand_box.reshape(lead + (box * box,))
    full_box = gather_pieces(dense, "slab", 3)
    chunks = 1
    chunk = part // chunks
    blocks = [receptor]
    for hop in range(1, extra + 1):
        pairs = [(i, (i - hop) % slab_count) for i in range(slab_count)]
        for piece in range(chunks):
            sent = receptor[:, piece * chunk : (piece + 1) * chunk]
            blocks.append(lax.ppermute(sent, "slab", perm=pairs))

    cos_n, sin_n = phase_tables(size, size, size)
    rz = block2(cos_n, -sin_n, sin_n, cos_n)
    ly = block2(cos_n, sin_n, -sin_n, cos_n)
    rec_blocks = [forward_planes(planes, (rz, ly), plane_step, size) for planes in blocks]

    lig = jnp.stack(
        [full_box[:, 0, 0] * channel_weight[0], full_box[:, 0, 1] * channel_weight[1]], axis=0
    ).reshape(2, sets * box, box, box)
    cos_b, sin_b = phase_tables(box, size, size)
    rz_box = block2(cos_b, -sin_b, sin_b, cos_b)
    ly_box = block2(cos_b.T, sin_b.T, -sin_b.T, cos_b.T)
    lig_yz = forward_planes(lig, (rz_box, ly_box), plane_step, size)

    cos_w, sin_w = phase_tables(window, window, window)
    g_tables = []
    first = 0
    for planes in blocks:
        cols = slice(first, first + planes.shape[1])
        first += planes.shape[1]
        g_tables.append(block2(cos_w[:, cols], sin_w[:, cols], -sin_w[:, cols], cos_w[:, cols]))
    cos_xb, sin_xb = phase_tables(window, box, window)
    gl = block2(cos_xb, sin_xb, -sin_xb, cos_xb)
    cos_t, sin_t = phase_tables(part, window, window)
    scale = 1.0 / float(window * size * size)
    hx = block2(cos_t, -sin_t, sin_t, cos_t) * scale
    back_x = cross_spectra(rec_blocks, lig_yz, g_tables, gl, hx, sets, box, window, row_step)

    lyi = block2(cos_n, -sin_n, sin_n, cos_n)
    rzi = jnp.concatenate([cos_n, -sin_n], axis=0)
    inverse_tables = (lyi, rzi)
    grids = inverse_planes(back_x, inverse_tables, plane_step)
    return grids.reshape(sets, 1, part, size, size)


def pose_statistics(
    rotation_table,
    ligand_atoms,
    cluster_center,
    pose_rotation,
    pose_translation,
    pose_owner,
    pose_member,
    size,
):
    all_centers = gather_pieces(cluster_center, "rot", 0)
    local_count = cluster_center.shape[0]
    cluster = pose_owner[:, 0] * local_count + pose_member
    rotation = jnp.take(rotation_table, pose_rotation, axis=1, mode="clip").T.reshape(-1, 3, 3)
    coords = jnp.stack(
        [
            pose_translation // (size * size),
            pose_translation // size % size,
            pose_translation % size,
        ],
        axis=1,
    )
    shifts = ((coords + size // 2) % size - size // 2).astype(F32) / size
    center = jnp.take(all_centers, cluster, axis=0, mode="clip")
    moved = jnp.einsum("pjk,ka->pja", rotation, ligand_atoms, precision=PRECISE) + shifts[:, :, None]
    spread = moved - center
    mean_square = jnp.mean(jnp.sum(spread * spread, axis=1), axis=1)
    moved_centred = moved - jnp.mean(moved, axis=2, keepdims=True)
    center_centred = center - jnp.mean(center, axis=2, keepdims=True)
    covariance = jnp.einsum("pja,pka->pjk", moved_centred, center_centred, precision=PRECISE)
    stats = jnp.concatenate([covariance.reshape(-1, 9), mean_square[:, None]], axis=1)
    return stats.T


def local(
    receptor,
    ligand_box,
    channel_weight,
    rotation_table,
    ligand_atoms,
    cluster_center,
    pose_rotation,
    pose_translation,
    pose_owner,
    pose_member,
):
    size = receptor.shape[2]
    scores = score_grids(receptor, ligand_box, channel_weight)
    pose_stats = pose_statistics(
        rotation_table,
        ligand_atoms,
        cluster_center,
        pose_rotation,
        pose_translation,
        pose_owner,
        pose_member,
        size,
    )
    return (scores, pose_stats)


def solution(mesh):
    return jax.shard_map(
        local,
        mesh=mesh,
        in_specs=(
            P(None, "slab", None, None),
            P(None, "rot", None, "slab", None, None),
            P(),
            P(),
            P(),
            P("rot", None, None),
            P(("slab", "rot")),
            P(("slab", "rot")),
            P(("slab", "rot"), None),
            P(("slab", "rot")),
        ),
        out_specs=(P(None, "rot", "slab", None, None), P(None, ("slab", "rot"))),
        check_vma=False,
    )
```

```python
import functools

import jax
import jax.numpy as jnp
from jax import lax
from jax.experimental import pallas as pl
from jax.experimental.pallas import tpu as pltpu
from jax.sharding import PartitionSpec as P

PRECISE = lax.Precision.HIGHEST
SPLIT3 = lax.Precision.HIGH
TWO_PI = 6.283185307179586
F32 = jnp.float32
BF16 = jnp.bfloat16


def phase_tables(rows, cols, length):
    row_index = lax.broadcasted_iota(jnp.int32, (rows, cols), 0)
    col_index = lax.broadcasted_iota(jnp.int32, (rows, cols), 1)
    phase = (row_index * col_index % length).astype(F32) * (TWO_PI / length)
    return (jnp.cos(phase), jnp.sin(phase))


def block2(top_left, top_right, bottom_left, bottom_right):
    top = jnp.concatenate([top_left, top_right], axis=1)
    bottom = jnp.concatenate([bottom_left, bottom_right], axis=1)
    return jnp.concatenate([top, bottom], axis=0)


def hi_lo(table):
    high = table.astype(BF16)
    low = (table - high.astype(F32)).astype(BF16)
    return high, low


def split_dot(a, b_high, b_low, a_left):
    a_high = a.astype(BF16)
    a_low = (a - a_high.astype(F32)).astype(BF16)
    dot = functools.partial(jnp.dot, preferred_element_type=F32)
    if a_left:
        return dot(a_high, b_high) + (dot(a_low, b_high) + dot(a_high, b_low))
    return dot(b_high, a_high) + (dot(b_high, a_low) + dot(b_low, a_high))


def forward_plane_kernel(in_ref, rz_ref, ly_ref, out_ref):
    planes, rows, cols = in_ref.shape[1], in_ref.shape[2], in_ref.shape[3]
    size = out_ref.shape[3]
    rz_hi, rz_lo = hi_lo(rz_ref[...])
    ly_hi, ly_lo = hi_lo(ly_ref[...])
    joined = jnp.concatenate(
        [in_ref[0].reshape(planes * rows, cols), in_ref[1].reshape(planes * rows, cols)], axis=1
    )
    along_z = split_dot(joined, rz_hi, rz_lo, True)
    stacked = jnp.concatenate(
        [
            jnp.concatenate(
                [along_z[p * rows : (p + 1) * rows, :size], along_z[p * rows : (p + 1) * rows, size:]],
                axis=0,
            )
            for p in range(planes)
        ],
        axis=1,
    )
    along_y = split_dot(stacked, ly_hi, ly_lo, False)
    for p in range(planes):
        out_ref[0, p] = along_y[:size, p * size : (p + 1) * size]
        out_ref[1, p] = along_y[size:, p * size : (p + 1) * size]


def inverse_plane_kernel(in_ref, ly_ref, rz_ref, out_ref):
    planes = in_ref.shape[2]
    size = in_ref.shape[4]
    ly_hi, ly_lo = hi_lo(ly_ref[...])
    rz_hi, rz_lo = hi_lo(rz_ref[...])
    stacked = jnp.concatenate(
        [jnp.concatenate([in_ref[0, 0, p], in_ref[0, 1, p]], axis=0) for p in range(planes)], axis=1
    )
    along_y = split_dot(stacked, ly_hi, ly_lo, False)
    joined = jnp.concatenate(
        [
            jnp.concatenate(
                [along_y[:size, p * size : (p + 1) * size], along_y[size:, p * size : (p + 1) * size]],
                axis=1,
            )
            for p in range(planes)
        ],
        axis=0,
    )
    out_ref[0] = split_dot(joined, rz_hi, rz_lo, True).reshape(planes, size, size)


def forward_planes(block, tables, plane_step, size):
    planes, rows, cols = block.shape[1], block.shape[2], block.shape[3]
    table_specs = [pl.BlockSpec(t.shape, lambda i: (0, 0)) for t in tables]
    return pl.pallas_call(
        forward_plane_kernel,
        grid=(planes // plane_step,),
        in_specs=[pl.BlockSpec((2, plane_step, rows, cols), lambda i: (0, i, 0, 0))] + table_specs,
        out_specs=pl.BlockSpec((2, plane_step, size, size), lambda i: (0, i, 0, 0)),
        out_shape=jax.ShapeDtypeStruct((2, planes, size, size), F32),
    )(block, *tables)


def cross_kernel(*refs, blocks, sets, box, window, part):
    rec_refs = refs[:blocks]
    lig_ref = refs[blocks]
    g_hi, g_lo = hi_lo(refs[blocks + 1][...])
    gl_hi, gl_lo = hi_lo(refs[blocks + 2][...])
    h_hi, h_lo = hi_lo(refs[blocks + 3][...])
    out_ref = refs[-1]
    rows = out_ref.shape[3]
    lanes = out_ref.shape[4]

    def gathered(ref, lo, count):
        turned = [jnp.swapaxes(ref[c, lo : lo + count], 0, 1) for c in range(2)]
        return jnp.concatenate(
            [jnp.concatenate([turned[0][r], turned[1][r]], axis=0) for r in range(rows)], axis=1
        )

    rec_in = jnp.concatenate(
        [gathered(rec_refs[b], 0, rec_refs[b].shape[1]) for b in range(blocks)], axis=0
    )
    rec = split_dot(rec_in, g_hi, g_lo, False)
    rec = jnp.concatenate([rec] * sets, axis=1)
    lig_in = jnp.concatenate([gathered(lig_ref, s * box, box) for s in range(sets)], axis=1)
    lig = split_dot(lig_in, gl_hi, gl_lo, False)
    rec_real = rec[:window]
    rec_imag = rec[window:]
    lig_real = lig[:window]
    lig_imag = lig[window:]
    prod = jnp.concatenate(
        [rec_real * lig_real + rec_imag * lig_imag, rec_imag * lig_real - rec_real * lig_imag],
        axis=0,
    )
    back = split_dot(prod, h_hi, h_lo, False)
    width = rows * lanes
    for s in range(sets):
        for c in range(2):
            pieces = jnp.stack(
                [
                    back[c * part : (c + 1) * part, s * width + r * lanes : s * width + (r + 1) * lanes]
                    for r in range(rows)
                ],
                axis=0,
            )
            out_ref[s, c] = jnp.swapaxes(pieces, 0, 1)


def cross_spectra(rec_blocks, lig_yz, g_tables, gl, hx, sets, box, window, row_step):
    part = rec_blocks[0].shape[1]
    size = rec_blocks[0].shape[2]
    lanes = rec_blocks[0].shape[3]
    blocks = len(rec_blocks)
    tables = [jnp.concatenate(g_tables, axis=1), gl, hx]
    kernel = functools.partial(
        cross_kernel, blocks=blocks, sets=sets, box=box, window=window, part=part
    )
    return pl.pallas_call(
        kernel,
        grid=(size // row_step,),
        in_specs=[pl.BlockSpec((2, b.shape[1], row_step, lanes), lambda i: (0, 0, i, 0)) for b in rec_blocks]
        + [pl.BlockSpec((2, sets * box, row_step, lanes), lambda i: (0, 0, i, 0))]
        + [pl.BlockSpec(t.shape, lambda i: (0, 0)) for t in tables],
        out_specs=pl.BlockSpec((sets, 2, part, row_step, lanes), lambda i: (0, 0, 0, i, 0)),
        out_shape=jax.ShapeDtypeStruct((sets, 2, part, size, lanes), F32),
    )(*rec_blocks, lig_yz, *tables)


def inverse_planes(spectra, tables, plane_step):
    sets, planes, size = spectra.shape[0], spectra.shape[2], spectra.shape[4]
    ly_spec = pl.BlockSpec((2 * size, 2 * size), lambda s, i: (0, 0))
    rz_spec = pl.BlockSpec((2 * size, size), lambda s, i: (0, 0))
    return pl.pallas_call(
        inverse_plane_kernel,
        grid=(sets, planes // plane_step),
        in_specs=[
            pl.BlockSpec((1, 2, plane_step, size, size), lambda s, i: (s, 0, i, 0, 0)),
            ly_spec,
            rz_spec,
        ],
        out_specs=pl.BlockSpec((1, plane_step, size, size), lambda s, i: (s, i, 0, 0)),
        out_shape=jax.ShapeDtypeStruct((sets, planes, size, size), F32),
    )(spectra, *tables)


def gather_by_sum(piece, axis_name, dim):
    count = lax.axis_size(axis_name)
    index = lax.axis_index(axis_name)
    width = piece.shape[dim]
    shape = list(piece.shape)
    shape[dim] = width * count
    start = [0] * len(shape)
    start[dim] = index * width
    placed = lax.dynamic_update_slice(jnp.zeros(shape, piece.dtype), piece, start)
    return lax.psum(placed, axis_name)


def gather_pieces(piece, axis_name, dim):
    count = lax.axis_size(axis_name)
    if count & (count - 1):
        return gather_by_sum(piece, axis_name, dim)
    index = lax.axis_index(axis_name)
    held = piece
    step = 1
    while step < count:
        pairs = [(i, i ^ step) for i in range(count)]
        other = lax.ppermute(held, axis_name, perm=pairs)
        low_half = (index // step) % 2 == 0
        held = jnp.where(
            low_half,
            jnp.concatenate([held, other], axis=dim),
            jnp.concatenate([other, held], axis=dim),
        )
        step *= 2
    return held


def gather_direct(piece, axis_name, dim):
    count = lax.axis_size(axis_name)
    index = lax.axis_index(axis_name)
    held = [piece]
    for hop in range(1, count):
        pairs = [(i, (i + hop) % count) for i in range(count)]
        held.append(lax.ppermute(piece, axis_name, perm=pairs))
    stacked = jnp.stack(held, axis=0)
    order = (index - jnp.arange(count)) % count
    ordered = jnp.take(stacked, order, axis=0, mode="clip")
    ordered = jnp.moveaxis(ordered, 0, dim)
    shape = list(piece.shape)
    shape[dim] = shape[dim] * count
    return ordered.reshape(shape)


def score_grids(receptor, ligand_box, channel_weight):
    size = receptor.shape[2]
    slab_count = lax.axis_size("slab")
    part = receptor.shape[1]
    box = ligand_box.shape[4]
    sets = ligand_box.shape[0]
    extra = -(-(box - 1) // part)
    window = part * (1 + extra)
    plane_step = 8
    row_step = 16

    lead = ligand_box.shape[:4]
    dense = ligand_box.reshape(lead + (box * box,))
    full_box = gather_direct(dense, "slab", 3)
    full_box, outgoing = lax.optimization_barrier((full_box, receptor))
    chunks = 1
    chunk = part // chunks
    blocks = [receptor]
    for hop in range(1, extra + 1):
        pairs = [(i, (i - hop) % slab_count) for i in range(slab_count)]
        for piece in range(chunks):
            sent = outgoing[:, piece * chunk : (piece + 1) * chunk]
            blocks.append(lax.ppermute(sent, "slab", perm=pairs))

    cos_n, sin_n = phase_tables(size, size, size)
    rz = block2(cos_n, -sin_n, sin_n, cos_n)
    ly = block2(cos_n, sin_n, -sin_n, cos_n)
    rec_blocks = [forward_planes(planes, (rz, ly), plane_step, size) for planes in blocks]

    lig = jnp.stack(
        [full_box[:, 0, 0] * channel_weight[0], full_box[:, 0, 1] * channel_weight[1]], axis=0
    ).reshape(2, sets * box, box, box)
    cos_b, sin_b = phase_tables(box, size, size)
    rz_box = block2(cos_b, -sin_b, sin_b, cos_b)
    ly_box = block2(cos_b.T, sin_b.T, -sin_b.T, cos_b.T)
    lig_yz = forward_planes(lig, (rz_box, ly_box), plane_step, size)

    cos_w, sin_w = phase_tables(window, window, window)
    g_tables = []
    first = 0
    for planes in blocks:
        cols = slice(first, first + planes.shape[1])
        first += planes.shape[1]
        g_tables.append(block2(cos_w[:, cols], sin_w[:, cols], -sin_w[:, cols], cos_w[:, cols]))
    cos_xb, sin_xb = phase_tables(window, box, window)
    gl = block2(cos_xb, sin_xb, -sin_xb, cos_xb)
    cos_t, sin_t = phase_tables(part, window, window)
    scale = 1.0 / float(window * size * size)
    hx = block2(cos_t, -sin_t, sin_t, cos_t) * scale
    back_x = cross_spectra(rec_blocks, lig_yz, g_tables, gl, hx, sets, box, window, row_step)

    lyi = block2(cos_n, -sin_n, sin_n, cos_n)
    rzi = jnp.concatenate([cos_n, -sin_n], axis=0)
    inverse_tables = (lyi, rzi)
    grids = inverse_planes(back_x, inverse_tables, plane_step)
    return grids.reshape(sets, 1, part, size, size)


def pose_statistics(
    rotation_table,
    ligand_atoms,
    cluster_center,
    pose_rotation,
    pose_translation,
    pose_owner,
    pose_member,
    size,
):
    all_centers = gather_pieces(cluster_center, "rot", 0)
    local_count = cluster_center.shape[0]
    cluster = pose_owner[:, 0] * local_count + pose_member
    rotation = jnp.take(rotation_table, pose_rotation, axis=1, mode="clip").T.reshape(-1, 3, 3)
    coords = jnp.stack(
        [
            pose_translation // (size * size),
            pose_translation // size % size,
            pose_translation % size,
        ],
        axis=1,
    )
    shifts = ((coords + size // 2) % size - size // 2).astype(F32) / size
    center = jnp.take(all_centers, cluster, axis=0, mode="clip")
    moved = jnp.einsum("pjk,ka->pja", rotation, ligand_atoms, precision=PRECISE) + shifts[:, :, None]
    spread = moved - center
    mean_square = jnp.mean(jnp.sum(spread * spread, axis=1), axis=1)
    moved_centred = moved - jnp.mean(moved, axis=2, keepdims=True)
    center_centred = center - jnp.mean(center, axis=2, keepdims=True)
    covariance = jnp.einsum("pja,pka->pjk", moved_centred, center_centred, precision=PRECISE)
    stats = jnp.concatenate([covariance.reshape(-1, 9), mean_square[:, None]], axis=1)
    return stats.T


def local(
    receptor,
    ligand_box,
    channel_weight,
    rotation_table,
    ligand_atoms,
    cluster_center,
    pose_rotation,
    pose_translation,
    pose_owner,
    pose_member,
):
    size = receptor.shape[2]
    scores = score_grids(receptor, ligand_box, channel_weight)
    pose_stats = pose_statistics(
        rotation_table,
        ligand_atoms,
        cluster_center,
        pose_rotation,
        pose_translation,
        pose_owner,
        pose_member,
        size,
    )
    return (scores, pose_stats)


def solution(mesh):
    return jax.shard_map(
        local,
        mesh=mesh,
        in_specs=(
            P(None, "slab", None, None),
            P(None, "rot", None, "slab", None, None),
            P(),
            P(),
            P(),
            P("rot", None, None),
            P(("slab", "rot")),
            P(("slab", "rot")),
            P(("slab", "rot"), None),
            P(("slab", "rot")),
        ),
        out_specs=(P(None, "rot", "slab", None, None), P(None, ("slab", "rot"))),
        check_vma=False,
    )
```

```python
import functools

import jax
import jax.numpy as jnp
from jax import lax
from jax.experimental import pallas as pl
from jax.experimental.pallas import tpu as pltpu
from jax.sharding import PartitionSpec as P

PRECISE = lax.Precision.HIGHEST
SPLIT3 = lax.Precision.HIGH
TWO_PI = 6.283185307179586
F32 = jnp.float32
BF16 = jnp.bfloat16


def phase_tables(rows, cols, length):
    row_index = lax.broadcasted_iota(jnp.int32, (rows, cols), 0)
    col_index = lax.broadcasted_iota(jnp.int32, (rows, cols), 1)
    phase = (row_index * col_index % length).astype(F32) * (TWO_PI / length)
    return (jnp.cos(phase), jnp.sin(phase))


def block2(top_left, top_right, bottom_left, bottom_right):
    top = jnp.concatenate([top_left, top_right], axis=1)
    bottom = jnp.concatenate([bottom_left, bottom_right], axis=1)
    return jnp.concatenate([top, bottom], axis=0)


def hi_lo(table):
    high = table.astype(BF16)
    low = (table - high.astype(F32)).astype(BF16)
    return high, low


def split_dot(a, b_high, b_low, a_left):
    a_high = a.astype(BF16)
    a_low = (a - a_high.astype(F32)).astype(BF16)
    dot = functools.partial(jnp.dot, preferred_element_type=F32)
    if a_left:
        return dot(a_high, b_high) + (dot(a_low, b_high) + dot(a_high, b_low))
    return dot(b_high, a_high) + (dot(b_high, a_low) + dot(b_low, a_high))


def forward_plane_kernel(in_ref, rz_ref, ly_ref, out_ref):
    planes, rows, cols = in_ref.shape[1], in_ref.shape[2], in_ref.shape[3]
    size = out_ref.shape[3]
    rz_hi, rz_lo = hi_lo(rz_ref[...])
    ly_hi, ly_lo = hi_lo(ly_ref[...])
    joined = jnp.concatenate(
        [in_ref[0].reshape(planes * rows, cols), in_ref[1].reshape(planes * rows, cols)], axis=1
    )
    along_z = split_dot(joined, rz_hi, rz_lo, True)
    stacked = jnp.concatenate(
        [
            jnp.concatenate(
                [along_z[p * rows : (p + 1) * rows, :size], along_z[p * rows : (p + 1) * rows, size:]],
                axis=0,
            )
            for p in range(planes)
        ],
        axis=1,
    )
    along_y = split_dot(stacked, ly_hi, ly_lo, False)
    for p in range(planes):
        out_ref[0, p] = along_y[:size, p * size : (p + 1) * size]
        out_ref[1, p] = along_y[size:, p * size : (p + 1) * size]


def inverse_plane_kernel(in_ref, ly_ref, rz_ref, out_ref):
    planes = in_ref.shape[2]
    size = in_ref.shape[4]
    ly_hi, ly_lo = hi_lo(ly_ref[...])
    rz_hi, rz_lo = hi_lo(rz_ref[...])
    stacked = jnp.concatenate(
        [jnp.concatenate([in_ref[0, 0, p], in_ref[0, 1, p]], axis=0) for p in range(planes)], axis=1
    )
    along_y = split_dot(stacked, ly_hi, ly_lo, False)
    joined = jnp.concatenate(
        [
            jnp.concatenate(
                [along_y[:size, p * size : (p + 1) * size], along_y[size:, p * size : (p + 1) * size]],
                axis=1,
            )
            for p in range(planes)
        ],
        axis=0,
    )
    out_ref[0] = split_dot(joined, rz_hi, rz_lo, True).reshape(planes, size, size)


def forward_planes(block, tables, plane_step, size):
    planes, rows, cols = block.shape[1], block.shape[2], block.shape[3]
    table_specs = [pl.BlockSpec(t.shape, lambda i: (0, 0)) for t in tables]
    return pl.pallas_call(
        forward_plane_kernel,
        grid=(planes // plane_step,),
        in_specs=[pl.BlockSpec((2, plane_step, rows, cols), lambda i: (0, i, 0, 0))] + table_specs,
        out_specs=pl.BlockSpec((2, plane_step, size, size), lambda i: (0, i, 0, 0)),
        out_shape=jax.ShapeDtypeStruct((2, planes, size, size), F32),
    )(block, *tables)


def cross_kernel(*refs, blocks, sets, box, window, part):
    rec_refs = refs[:blocks]
    lig_ref = refs[blocks]
    g_hi, g_lo = hi_lo(refs[blocks + 1][...])
    gl_hi, gl_lo = hi_lo(refs[blocks + 2][...])
    h_hi, h_lo = hi_lo(refs[blocks + 3][...])
    out_ref = refs[-1]
    rows = out_ref.shape[3]
    lanes = out_ref.shape[4]

    def gathered(ref, lo, count):
        turned = [jnp.swapaxes(ref[c, lo : lo + count], 0, 1) for c in range(2)]
        return jnp.concatenate(
            [jnp.concatenate([turned[0][r], turned[1][r]], axis=0) for r in range(rows)], axis=1
        )

    rec_in = jnp.concatenate(
        [gathered(rec_refs[b], 0, rec_refs[b].shape[1]) for b in range(blocks)], axis=0
    )
    rec = split_dot(rec_in, g_hi, g_lo, False)
    rec = jnp.concatenate([rec] * sets, axis=1)
    lig_in = jnp.concatenate([gathered(lig_ref, s * box, box) for s in range(sets)], axis=1)
    lig = split_dot(lig_in, gl_hi, gl_lo, False)
    rec_real = rec[:window]
    rec_imag = rec[window:]
    lig_real = lig[:window]
    lig_imag = lig[window:]
    prod = jnp.concatenate(
        [rec_real * lig_real + rec_imag * lig_imag, rec_imag * lig_real - rec_real * lig_imag],
        axis=0,
    )
    back = split_dot(prod, h_hi, h_lo, False)
    width = rows * lanes
    for s in range(sets):
        for c in range(2):
            pieces = jnp.stack(
                [
                    back[c * part : (c + 1) * part, s * width + r * lanes : s * width + (r + 1) * lanes]
                    for r in range(rows)
                ],
                axis=0,
            )
            out_ref[s, c] = jnp.swapaxes(pieces, 0, 1)


def cross_spectra(rec_blocks, lig_yz, g_tables, gl, hx, sets, box, window, row_step):
    part = rec_blocks[0].shape[1]
    size = rec_blocks[0].shape[2]
    lanes = rec_blocks[0].shape[3]
    blocks = len(rec_blocks)
    tables = [jnp.concatenate(g_tables, axis=1), gl, hx]
    kernel = functools.partial(
        cross_kernel, blocks=blocks, sets=sets, box=box, window=window, part=part
    )
    return pl.pallas_call(
        kernel,
        grid=(size // row_step,),
        in_specs=[pl.BlockSpec((2, b.shape[1], row_step, lanes), lambda i: (0, 0, i, 0)) for b in rec_blocks]
        + [pl.BlockSpec((2, sets * box, row_step, lanes), lambda i: (0, 0, i, 0))]
        + [pl.BlockSpec(t.shape, lambda i: (0, 0)) for t in tables],
        out_specs=pl.BlockSpec((sets, 2, part, row_step, lanes), lambda i: (0, 0, 0, i, 0)),
        out_shape=jax.ShapeDtypeStruct((sets, 2, part, size, lanes), F32),
    )(*rec_blocks, lig_yz, *tables)


def inverse_planes(spectra, tables, plane_step):
    sets, planes, size = spectra.shape[0], spectra.shape[2], spectra.shape[4]
    ly_spec = pl.BlockSpec((2 * size, 2 * size), lambda s, i: (0, 0))
    rz_spec = pl.BlockSpec((2 * size, size), lambda s, i: (0, 0))
    return pl.pallas_call(
        inverse_plane_kernel,
        grid=(sets, planes // plane_step),
        in_specs=[
            pl.BlockSpec((1, 2, plane_step, size, size), lambda s, i: (s, 0, i, 0, 0)),
            ly_spec,
            rz_spec,
        ],
        out_specs=pl.BlockSpec((1, plane_step, size, size), lambda s, i: (s, i, 0, 0)),
        out_shape=jax.ShapeDtypeStruct((sets, planes, size, size), F32),
    )(spectra, *tables)


def gather_by_sum(piece, axis_name, dim):
    count = lax.axis_size(axis_name)
    index = lax.axis_index(axis_name)
    width = piece.shape[dim]
    shape = list(piece.shape)
    shape[dim] = width * count
    start = [0] * len(shape)
    start[dim] = index * width
    placed = lax.dynamic_update_slice(jnp.zeros(shape, piece.dtype), piece, start)
    return lax.psum(placed, axis_name)


def gather_pieces(piece, axis_name, dim):
    count = lax.axis_size(axis_name)
    if count & (count - 1):
        return gather_by_sum(piece, axis_name, dim)
    index = lax.axis_index(axis_name)
    held = piece
    step = 1
    while step < count:
        pairs = [(i, i ^ step) for i in range(count)]
        other = lax.ppermute(held, axis_name, perm=pairs)
        low_half = (index // step) % 2 == 0
        held = jnp.where(
            low_half,
            jnp.concatenate([held, other], axis=dim),
            jnp.concatenate([other, held], axis=dim),
        )
        step *= 2
    return held


def gather_direct(piece, axis_name, dim):
    count = lax.axis_size(axis_name)
    index = lax.axis_index(axis_name)
    held = [piece]
    for hop in range(1, count):
        pairs = [(i, (i + hop) % count) for i in range(count)]
        held.append(lax.ppermute(piece, axis_name, perm=pairs))
    stacked = jnp.stack(held, axis=0)
    order = (index - jnp.arange(count)) % count
    ordered = jnp.take(stacked, order, axis=0, mode="clip")
    ordered = jnp.moveaxis(ordered, 0, dim)
    shape = list(piece.shape)
    shape[dim] = shape[dim] * count
    return ordered.reshape(shape)


def score_grids(receptor, ligand_box, channel_weight):
    size = receptor.shape[2]
    slab_count = lax.axis_size("slab")
    part = receptor.shape[1]
    box = ligand_box.shape[4]
    sets = ligand_box.shape[0]
    extra = -(-(box - 1) // part)
    window = part * (1 + extra)
    plane_step = 8
    row_step = 16

    lead = ligand_box.shape[:4]
    dense = ligand_box.reshape(lead + (box * box,))
    full_box = gather_direct(dense, "slab", 3)
    cos_n, sin_n = phase_tables(size, size, size)
    rz = block2(cos_n, -sin_n, sin_n, cos_n)
    ly = block2(cos_n, sin_n, -sin_n, cos_n)
    own = forward_planes(receptor, (rz, ly), plane_step, size)
    full_box, outgoing = lax.optimization_barrier((full_box, own))
    rec_blocks = [own]
    for hop in range(1, extra + 1):
        pairs = [(i, (i - hop) % slab_count) for i in range(slab_count)]
        rec_blocks.append(lax.ppermute(outgoing, "slab", perm=pairs))

    lig = jnp.stack(
        [full_box[:, 0, 0] * channel_weight[0], full_box[:, 0, 1] * channel_weight[1]], axis=0
    ).reshape(2, sets * box, box, box)
    cos_b, sin_b = phase_tables(box, size, size)
    rz_box = block2(cos_b, -sin_b, sin_b, cos_b)
    ly_box = block2(cos_b.T, sin_b.T, -sin_b.T, cos_b.T)
    lig_yz = forward_planes(lig, (rz_box, ly_box), plane_step, size)

    cos_w, sin_w = phase_tables(window, window, window)
    g_tables = []
    first = 0
    for planes in rec_blocks:
        cols = slice(first, first + planes.shape[1])
        first += planes.shape[1]
        g_tables.append(block2(cos_w[:, cols], sin_w[:, cols], -sin_w[:, cols], cos_w[:, cols]))
    cos_xb, sin_xb = phase_tables(window, box, window)
    gl = block2(cos_xb, sin_xb, -sin_xb, cos_xb)
    cos_t, sin_t = phase_tables(part, window, window)
    scale = 1.0 / float(window * size * size)
    hx = block2(cos_t, -sin_t, sin_t, cos_t) * scale
    back_x = cross_spectra(rec_blocks, lig_yz, g_tables, gl, hx, sets, box, window, row_step)

    lyi = block2(cos_n, -sin_n, sin_n, cos_n)
    rzi = jnp.concatenate([cos_n, -sin_n], axis=0)
    inverse_tables = (lyi, rzi)
    grids = inverse_planes(back_x, inverse_tables, plane_step)
    return grids.reshape(sets, 1, part, size, size)


def pose_statistics(
    rotation_table,
    ligand_atoms,
    cluster_center,
    pose_rotation,
    pose_translation,
    pose_owner,
    pose_member,
    size,
):
    all_centers = gather_pieces(cluster_center, "rot", 0)
    local_count = cluster_center.shape[0]
    cluster = pose_owner[:, 0] * local_count + pose_member
    rotation = jnp.take(rotation_table, pose_rotation, axis=1, mode="clip").T.reshape(-1, 3, 3)
    coords = jnp.stack(
        [
            pose_translation // (size * size),
            pose_translation // size % size,
            pose_translation % size,
        ],
        axis=1,
    )
    shifts = ((coords + size // 2) % size - size // 2).astype(F32) / size
    center = jnp.take(all_centers, cluster, axis=0, mode="clip")
    moved = jnp.einsum("pjk,ka->pja", rotation, ligand_atoms, precision=PRECISE) + shifts[:, :, None]
    spread = moved - center
    mean_square = jnp.mean(jnp.sum(spread * spread, axis=1), axis=1)
    moved_centred = moved - jnp.mean(moved, axis=2, keepdims=True)
    center_centred = center - jnp.mean(center, axis=2, keepdims=True)
    covariance = jnp.einsum("pja,pka->pjk", moved_centred, center_centred, precision=PRECISE)
    stats = jnp.concatenate([covariance.reshape(-1, 9), mean_square[:, None]], axis=1)
    return stats.T


def local(
    receptor,
    ligand_box,
    channel_weight,
    rotation_table,
    ligand_atoms,
    cluster_center,
    pose_rotation,
    pose_translation,
    pose_owner,
    pose_member,
):
    size = receptor.shape[2]
    scores = score_grids(receptor, ligand_box, channel_weight)
    pose_stats = pose_statistics(
        rotation_table,
        ligand_atoms,
        cluster_center,
        pose_rotation,
        pose_translation,
        pose_owner,
        pose_member,
        size,
    )
    return (scores, pose_stats)


def solution(mesh):
    return jax.shard_map(
        local,
        mesh=mesh,
        in_specs=(
            P(None, "slab", None, None),
            P(None, "rot", None, "slab", None, None),
            P(),
            P(),
            P(),
            P("rot", None, None),
            P(("slab", "rot")),
            P(("slab", "rot")),
            P(("slab", "rot"), None),
            P(("slab", "rot")),
        ),
        out_specs=(P(None, "rot", "slab", None, None), P(None, ("slab", "rot"))),
        check_vma=False,
    )
```

```python
import functools

import jax
import jax.numpy as jnp
from jax import lax
from jax.experimental import pallas as pl
from jax.experimental.pallas import tpu as pltpu
from jax.sharding import PartitionSpec as P

PRECISE = lax.Precision.HIGHEST
SPLIT3 = lax.Precision.HIGH
TWO_PI = 6.283185307179586
F32 = jnp.float32
BF16 = jnp.bfloat16


def phase_tables(rows, cols, length):
    row_index = lax.broadcasted_iota(jnp.int32, (rows, cols), 0)
    col_index = lax.broadcasted_iota(jnp.int32, (rows, cols), 1)
    phase = (row_index * col_index % length).astype(F32) * (TWO_PI / length)
    return (jnp.cos(phase), jnp.sin(phase))


def block2(top_left, top_right, bottom_left, bottom_right):
    top = jnp.concatenate([top_left, top_right], axis=1)
    bottom = jnp.concatenate([bottom_left, bottom_right], axis=1)
    return jnp.concatenate([top, bottom], axis=0)


def hi_lo(table):
    high = table.astype(BF16)
    low = (table - high.astype(F32)).astype(BF16)
    return high, low


def split_dot(a, b_high, b_low, a_left):
    a_high = a.astype(BF16)
    a_low = (a - a_high.astype(F32)).astype(BF16)
    dot = functools.partial(jnp.dot, preferred_element_type=F32)
    if a_left:
        return dot(a_high, b_high) + (dot(a_low, b_high) + dot(a_high, b_low))
    return dot(b_high, a_high) + (dot(b_high, a_low) + dot(b_low, a_high))


def forward_plane_kernel(in_ref, rz_ref, ly_ref, out_ref):
    planes, rows, cols = in_ref.shape[1], in_ref.shape[2], in_ref.shape[3]
    size = out_ref.shape[3]
    rz_hi, rz_lo = hi_lo(rz_ref[...])
    ly_hi, ly_lo = hi_lo(ly_ref[...])
    joined = jnp.concatenate(
        [in_ref[0].reshape(planes * rows, cols), in_ref[1].reshape(planes * rows, cols)], axis=1
    )
    along_z = split_dot(joined, rz_hi, rz_lo, True)
    stacked = jnp.concatenate(
        [
            jnp.concatenate(
                [along_z[p * rows : (p + 1) * rows, :size], along_z[p * rows : (p + 1) * rows, size:]],
                axis=0,
            )
            for p in range(planes)
        ],
        axis=1,
    )
    along_y = split_dot(stacked, ly_hi, ly_lo, False)
    for p in range(planes):
        out_ref[0, p] = along_y[:size, p * size : (p + 1) * size]
        out_ref[1, p] = along_y[size:, p * size : (p + 1) * size]


def inverse_plane_kernel(in_ref, ly_ref, rz_ref, out_ref):
    planes = in_ref.shape[2]
    size = in_ref.shape[4]
    ly_hi, ly_lo = hi_lo(ly_ref[...])
    rz_hi, rz_lo = hi_lo(rz_ref[...])
    stacked = jnp.concatenate(
        [jnp.concatenate([in_ref[0, 0, p], in_ref[0, 1, p]], axis=0) for p in range(planes)], axis=1
    )
    along_y = split_dot(stacked, ly_hi, ly_lo, False)
    joined = jnp.concatenate(
        [
            jnp.concatenate(
                [along_y[:size, p * size : (p + 1) * size], along_y[size:, p * size : (p + 1) * size]],
                axis=1,
            )
            for p in range(planes)
        ],
        axis=0,
    )
    out_ref[0] = split_dot(joined, rz_hi, rz_lo, True).reshape(planes, size, size)


def forward_planes(block, tables, plane_step, size):
    planes, rows, cols = block.shape[1], block.shape[2], block.shape[3]
    table_specs = [pl.BlockSpec(t.shape, lambda i: (0, 0)) for t in tables]
    return pl.pallas_call(
        forward_plane_kernel,
        grid=(planes // plane_step,),
        in_specs=[pl.BlockSpec((2, plane_step, rows, cols), lambda i: (0, i, 0, 0))] + table_specs,
        out_specs=pl.BlockSpec((2, plane_step, size, size), lambda i: (0, i, 0, 0)),
        out_shape=jax.ShapeDtypeStruct((2, planes, size, size), F32),
    )(block, *tables)


def cross_kernel(*refs, blocks, sets, box, window, part):
    rec_refs = refs[:blocks]
    lig_ref = refs[blocks]
    g_hi, g_lo = hi_lo(refs[blocks + 1][...])
    gl_hi, gl_lo = hi_lo(refs[blocks + 2][...])
    h_hi, h_lo = hi_lo(refs[blocks + 3][...])
    out_ref = refs[-1]
    rows = out_ref.shape[3]
    lanes = out_ref.shape[4]

    def gathered(ref, lo, count):
        turned = [jnp.swapaxes(ref[c, lo : lo + count], 0, 1) for c in range(2)]
        return jnp.concatenate(
            [jnp.concatenate([turned[0][r], turned[1][r]], axis=0) for r in range(rows)], axis=1
        )

    rec_in = jnp.concatenate(
        [gathered(rec_refs[b], 0, rec_refs[b].shape[1]) for b in range(blocks)], axis=0
    )
    rec = split_dot(rec_in, g_hi, g_lo, False)
    rec = jnp.concatenate([rec] * sets, axis=1)
    lig_in = jnp.concatenate([gathered(lig_ref, s * box, box) for s in range(sets)], axis=1)
    lig = split_dot(lig_in, gl_hi, gl_lo, False)
    rec_real = rec[:window]
    rec_imag = rec[window:]
    lig_real = lig[:window]
    lig_imag = lig[window:]
    prod = jnp.concatenate(
        [rec_real * lig_real + rec_imag * lig_imag, rec_imag * lig_real - rec_real * lig_imag],
        axis=0,
    )
    back = split_dot(prod, h_hi, h_lo, False)
    width = rows * lanes
    for s in range(sets):
        for c in range(2):
            pieces = jnp.stack(
                [
                    back[c * part : (c + 1) * part, s * width + r * lanes : s * width + (r + 1) * lanes]
                    for r in range(rows)
                ],
                axis=0,
            )
            out_ref[s, c] = jnp.swapaxes(pieces, 0, 1)


def cross_spectra(rec_blocks, lig_yz, g_tables, gl, hx, sets, box, window, row_step):
    part = hx.shape[0] // 2
    size = rec_blocks[0].shape[2]
    lanes = rec_blocks[0].shape[3]
    blocks = len(rec_blocks)
    tables = [jnp.concatenate(g_tables, axis=1), gl, hx]
    kernel = functools.partial(
        cross_kernel, blocks=blocks, sets=sets, box=box, window=window, part=part
    )
    return pl.pallas_call(
        kernel,
        grid=(size // row_step,),
        in_specs=[pl.BlockSpec((2, b.shape[1], row_step, lanes), lambda i: (0, 0, i, 0)) for b in rec_blocks]
        + [pl.BlockSpec((2, sets * box, row_step, lanes), lambda i: (0, 0, i, 0))]
        + [pl.BlockSpec(t.shape, lambda i: (0, 0)) for t in tables],
        out_specs=pl.BlockSpec((sets, 2, part, row_step, lanes), lambda i: (0, 0, 0, i, 0)),
        out_shape=jax.ShapeDtypeStruct((sets, 2, part, size, lanes), F32),
    )(*rec_blocks, lig_yz, *tables)


def inverse_planes(spectra, tables, plane_step):
    sets, planes, size = spectra.shape[0], spectra.shape[2], spectra.shape[4]
    ly_spec = pl.BlockSpec((2 * size, 2 * size), lambda s, i: (0, 0))
    rz_spec = pl.BlockSpec((2 * size, size), lambda s, i: (0, 0))
    return pl.pallas_call(
        inverse_plane_kernel,
        grid=(sets, planes // plane_step),
        in_specs=[
            pl.BlockSpec((1, 2, plane_step, size, size), lambda s, i: (s, 0, i, 0, 0)),
            ly_spec,
            rz_spec,
        ],
        out_specs=pl.BlockSpec((1, plane_step, size, size), lambda s, i: (s, i, 0, 0)),
        out_shape=jax.ShapeDtypeStruct((sets, planes, size, size), F32),
    )(spectra, *tables)


def gather_by_sum(piece, axis_name, dim):
    count = lax.axis_size(axis_name)
    index = lax.axis_index(axis_name)
    width = piece.shape[dim]
    shape = list(piece.shape)
    shape[dim] = width * count
    start = [0] * len(shape)
    start[dim] = index * width
    placed = lax.dynamic_update_slice(jnp.zeros(shape, piece.dtype), piece, start)
    return lax.psum(placed, axis_name)


def gather_pieces(piece, axis_name, dim):
    count = lax.axis_size(axis_name)
    if count & (count - 1):
        return gather_by_sum(piece, axis_name, dim)
    index = lax.axis_index(axis_name)
    held = piece
    step = 1
    while step < count:
        pairs = [(i, i ^ step) for i in range(count)]
        other = lax.ppermute(held, axis_name, perm=pairs)
        low_half = (index // step) % 2 == 0
        held = jnp.where(
            low_half,
            jnp.concatenate([held, other], axis=dim),
            jnp.concatenate([other, held], axis=dim),
        )
        step *= 2
    return held


def gather_direct(piece, axis_name, dim):
    count = lax.axis_size(axis_name)
    index = lax.axis_index(axis_name)
    held = [piece]
    for hop in range(1, count):
        pairs = [(i, (i + hop) % count) for i in range(count)]
        held.append(lax.ppermute(piece, axis_name, perm=pairs))
    stacked = jnp.stack(held, axis=0)
    order = (index - jnp.arange(count)) % count
    ordered = jnp.take(stacked, order, axis=0, mode="clip")
    ordered = jnp.moveaxis(ordered, 0, dim)
    shape = list(piece.shape)
    shape[dim] = shape[dim] * count
    return ordered.reshape(shape)


def score_grids(receptor, ligand_box, channel_weight):
    size = receptor.shape[2]
    slab_count = lax.axis_size("slab")
    part = receptor.shape[1]
    box = ligand_box.shape[4]
    sets = ligand_box.shape[0]
    extra = -(-(box - 1) // part)
    window = part * (1 + extra)
    plane_step = 8
    row_step = 16

    lead = ligand_box.shape[:4]
    dense = ligand_box.reshape(lead + (box * box,))
    full_box = gather_direct(dense, "slab", 3)
    cos_n, sin_n = phase_tables(size, size, size)
    rz = block2(cos_n, -sin_n, sin_n, cos_n)
    ly = block2(cos_n, sin_n, -sin_n, cos_n)
    own = forward_planes(receptor, (rz, ly), plane_step, size)
    rec_blocks = [own]
    for hop in range(1, extra + 1):
        pairs = [(i, (i - hop) % slab_count) for i in range(slab_count)]
        rec_blocks.append(lax.ppermute(own, "slab", perm=pairs))

    lig = jnp.stack(
        [full_box[:, 0, 0] * channel_weight[0], full_box[:, 0, 1] * channel_weight[1]], axis=0
    ).reshape(2, sets * box, box, box)
    cos_b, sin_b = phase_tables(box, size, size)
    rz_box = block2(cos_b, -sin_b, sin_b, cos_b)
    ly_box = block2(cos_b.T, sin_b.T, -sin_b.T, cos_b.T)
    lig_yz = forward_planes(lig, (rz_box, ly_box), plane_step, size)

    cos_w, sin_w = phase_tables(window, window, window)
    g_tables = []
    first = 0
    for planes in rec_blocks:
        cols = slice(first, first + planes.shape[1])
        first += planes.shape[1]
        g_tables.append(block2(cos_w[:, cols], sin_w[:, cols], -sin_w[:, cols], cos_w[:, cols]))
    cos_xb, sin_xb = phase_tables(window, box, window)
    gl = block2(cos_xb, sin_xb, -sin_xb, cos_xb)
    cos_t, sin_t = phase_tables(part, window, window)
    scale = 1.0 / float(window * size * size)
    hx = block2(cos_t, -sin_t, sin_t, cos_t) * scale
    back_x = cross_spectra(rec_blocks, lig_yz, g_tables, gl, hx, sets, box, window, row_step)

    lyi = block2(cos_n, -sin_n, sin_n, cos_n)
    rzi = jnp.concatenate([cos_n, -sin_n], axis=0)
    inverse_tables = (lyi, rzi)
    grids = inverse_planes(back_x, inverse_tables, plane_step)
    return grids.reshape(sets, 1, part, size, size)


def pose_statistics(
    rotation_table,
    ligand_atoms,
    cluster_center,
    pose_rotation,
    pose_translation,
    pose_owner,
    pose_member,
    size,
):
    all_centers = gather_pieces(cluster_center, "rot", 0)
    local_count = cluster_center.shape[0]
    cluster = pose_owner[:, 0] * local_count + pose_member
    rotation = jnp.take(rotation_table, pose_rotation, axis=1, mode="clip").T.reshape(-1, 3, 3)
    coords = jnp.stack(
        [
            pose_translation // (size * size),
            pose_translation // size % size,
            pose_translation % size,
        ],
        axis=1,
    )
    shifts = ((coords + size // 2) % size - size // 2).astype(F32) / size
    center = jnp.take(all_centers, cluster, axis=0, mode="clip")
    moved = jnp.einsum("pjk,ka->pja", rotation, ligand_atoms, precision=PRECISE) + shifts[:, :, None]
    spread = moved - center
    mean_square = jnp.mean(jnp.sum(spread * spread, axis=1), axis=1)
    moved_centred = moved - jnp.mean(moved, axis=2, keepdims=True)
    center_centred = center - jnp.mean(center, axis=2, keepdims=True)
    covariance = jnp.einsum("pja,pka->pjk", moved_centred, center_centred, precision=PRECISE)
    stats = jnp.concatenate([covariance.reshape(-1, 9), mean_square[:, None]], axis=1)
    return stats.T


def local(
    receptor,
    ligand_box,
    channel_weight,
    rotation_table,
    ligand_atoms,
    cluster_center,
    pose_rotation,
    pose_translation,
    pose_owner,
    pose_member,
):
    size = receptor.shape[2]
    scores = score_grids(receptor, ligand_box, channel_weight)
    pose_stats = pose_statistics(
        rotation_table,
        ligand_atoms,
        cluster_center,
        pose_rotation,
        pose_translation,
        pose_owner,
        pose_member,
        size,
    )
    return (scores, pose_stats)


def solution(mesh):
    return jax.shard_map(
        local,
        mesh=mesh,
        in_specs=(
            P(None, "slab", None, None),
            P(None, "rot", None, "slab", None, None),
            P(),
            P(),
            P(),
            P("rot", None, None),
            P(("slab", "rot")),
            P(("slab", "rot")),
            P(("slab", "rot"), None),
            P(("slab", "rot")),
        ),
        out_specs=(P(None, "rot", "slab", None, None), P(None, ("slab", "rot"))),
        check_vma=False,
    )
```

```python
import functools

import jax
import jax.numpy as jnp
from jax import lax
from jax.experimental import pallas as pl
from jax.experimental.pallas import tpu as pltpu
from jax.sharding import PartitionSpec as P

PRECISE = lax.Precision.HIGHEST
SPLIT3 = lax.Precision.HIGH
TWO_PI = 6.283185307179586
F32 = jnp.float32
BF16 = jnp.bfloat16


def phase_tables(rows, cols, length):
    row_index = lax.broadcasted_iota(jnp.int32, (rows, cols), 0)
    col_index = lax.broadcasted_iota(jnp.int32, (rows, cols), 1)
    phase = (row_index * col_index % length).astype(F32) * (TWO_PI / length)
    return (jnp.cos(phase), jnp.sin(phase))


def block2(top_left, top_right, bottom_left, bottom_right):
    top = jnp.concatenate([top_left, top_right], axis=1)
    bottom = jnp.concatenate([bottom_left, bottom_right], axis=1)
    return jnp.concatenate([top, bottom], axis=0)


def hi_lo(table):
    high = table.astype(BF16)
    low = (table - high.astype(F32)).astype(BF16)
    return high, low


def split_dot(a, b_high, b_low, a_left):
    a_high = a.astype(BF16)
    a_low = (a - a_high.astype(F32)).astype(BF16)
    dot = functools.partial(jnp.dot, preferred_element_type=F32)
    if a_left:
        return dot(a_high, b_high) + (dot(a_low, b_high) + dot(a_high, b_low))
    return dot(b_high, a_high) + (dot(b_high, a_low) + dot(b_low, a_high))


def forward_plane_kernel(in_ref, rz_ref, ly_ref, *out_refs):
    planes, rows, cols = in_ref.shape[1], in_ref.shape[2], in_ref.shape[3]
    size = out_refs[0].shape[3]
    rz_hi, rz_lo = hi_lo(rz_ref[...])
    ly_hi, ly_lo = hi_lo(ly_ref[...])
    joined = jnp.concatenate(
        [in_ref[0].reshape(planes * rows, cols), in_ref[1].reshape(planes * rows, cols)], axis=1
    )
    along_z = split_dot(joined, rz_hi, rz_lo, True)
    stacked = jnp.concatenate(
        [
            jnp.concatenate(
                [along_z[p * rows : (p + 1) * rows, :size], along_z[p * rows : (p + 1) * rows, size:]],
                axis=0,
            )
            for p in range(planes)
        ],
        axis=1,
    )
    along_y = split_dot(stacked, ly_hi, ly_lo, False)
    step = size // len(out_refs)
    for q, out_ref in enumerate(out_refs):
        for p in range(planes):
            cols = slice(p * size, (p + 1) * size)
            out_ref[0, p] = along_y[q * step : (q + 1) * step, cols]
            out_ref[1, p] = along_y[size + q * step : size + (q + 1) * step, cols]


def inverse_plane_kernel(*refs):
    in_refs = refs[:-3]
    ly_ref, rz_ref, out_ref = refs[-3:]
    planes = in_refs[0].shape[2]
    size = in_refs[0].shape[4]
    ly_hi, ly_lo = hi_lo(ly_ref[...])
    rz_hi, rz_lo = hi_lo(rz_ref[...])

    def plane(c, p):
        return jnp.concatenate([r[0, c, p] for r in in_refs], axis=0)

    stacked = jnp.concatenate(
        [jnp.concatenate([plane(0, p), plane(1, p)], axis=0) for p in range(planes)], axis=1
    )
    along_y = split_dot(stacked, ly_hi, ly_lo, False)
    joined = jnp.concatenate(
        [
            jnp.concatenate(
                [along_y[:size, p * size : (p + 1) * size], along_y[size:, p * size : (p + 1) * size]],
                axis=1,
            )
            for p in range(planes)
        ],
        axis=0,
    )
    out_ref[0] = split_dot(joined, rz_hi, rz_lo, True).reshape(planes, size, size)


def forward_planes(block, tables, plane_step, size, splits=1):
    planes, rows, cols = block.shape[1], block.shape[2], block.shape[3]
    table_specs = [pl.BlockSpec(t.shape, lambda i: (0, 0)) for t in tables]
    step = size // splits
    outs = pl.pallas_call(
        forward_plane_kernel,
        grid=(planes // plane_step,),
        in_specs=[pl.BlockSpec((2, plane_step, rows, cols), lambda i: (0, i, 0, 0))] + table_specs,
        out_specs=[pl.BlockSpec((2, plane_step, step, size), lambda i: (0, i, 0, 0))] * splits,
        out_shape=[jax.ShapeDtypeStruct((2, planes, step, size), F32)] * splits,
    )(block, *tables)
    return outs if splits > 1 else outs[0]


def cross_kernel(*refs, blocks, sets, box, window, part):
    rec_refs = refs[:blocks]
    lig_ref = refs[blocks]
    g_hi, g_lo = hi_lo(refs[blocks + 1][...])
    gl_hi, gl_lo = hi_lo(refs[blocks + 2][...])
    h_hi, h_lo = hi_lo(refs[blocks + 3][...])
    out_ref = refs[-1]
    rows = out_ref.shape[3]
    lanes = out_ref.shape[4]

    def gathered(ref, lo, count):
        turned = [jnp.swapaxes(ref[c, lo : lo + count], 0, 1) for c in range(2)]
        return jnp.concatenate(
            [jnp.concatenate([turned[0][r], turned[1][r]], axis=0) for r in range(rows)], axis=1
        )

    rec_in = jnp.concatenate(
        [gathered(rec_refs[b], 0, rec_refs[b].shape[1]) for b in range(blocks)], axis=0
    )
    rec = split_dot(rec_in, g_hi, g_lo, False)
    rec = jnp.concatenate([rec] * sets, axis=1)
    lig_in = jnp.concatenate([gathered(lig_ref, s * box, box) for s in range(sets)], axis=1)
    lig = split_dot(lig_in, gl_hi, gl_lo, False)
    rec_real = rec[:window]
    rec_imag = rec[window:]
    lig_real = lig[:window]
    lig_imag = lig[window:]
    prod = jnp.concatenate(
        [rec_real * lig_real + rec_imag * lig_imag, rec_imag * lig_real - rec_real * lig_imag],
        axis=0,
    )
    back = split_dot(prod, h_hi, h_lo, False)
    width = rows * lanes
    for s in range(sets):
        for c in range(2):
            pieces = jnp.stack(
                [
                    back[c * part : (c + 1) * part, s * width + r * lanes : s * width + (r + 1) * lanes]
                    for r in range(rows)
                ],
                axis=0,
            )
            out_ref[s, c] = jnp.swapaxes(pieces, 0, 1)


def cross_spectra(rec_blocks, lig_yz, g_tables, gl, hx, sets, box, window, row_step, lig_from):
    part = hx.shape[0] // 2
    size = rec_blocks[0].shape[2]
    offset = lig_from // row_step
    lanes = rec_blocks[0].shape[3]
    blocks = len(rec_blocks)
    tables = [jnp.concatenate(g_tables, axis=1), gl, hx]
    kernel = functools.partial(
        cross_kernel, blocks=blocks, sets=sets, box=box, window=window, part=part
    )
    return pl.pallas_call(
        kernel,
        grid=(size // row_step,),
        in_specs=[pl.BlockSpec((2, b.shape[1], row_step, lanes), lambda i: (0, 0, i, 0)) for b in rec_blocks]
        + [pl.BlockSpec((2, sets * box, row_step, lanes), lambda i: (0, 0, i + offset, 0))]
        + [pl.BlockSpec(t.shape, lambda i: (0, 0)) for t in tables],
        out_specs=pl.BlockSpec((sets, 2, part, row_step, lanes), lambda i: (0, 0, 0, i, 0)),
        out_shape=jax.ShapeDtypeStruct((sets, 2, part, size, lanes), F32),
    )(*rec_blocks, lig_yz, *tables)


def inverse_planes(spectra, tables, plane_step):
    sets, planes, size = spectra[0].shape[0], spectra[0].shape[2], spectra[0].shape[4]
    ly_spec = pl.BlockSpec((2 * size, 2 * size), lambda s, i: (0, 0))
    rz_spec = pl.BlockSpec((2 * size, size), lambda s, i: (0, 0))
    return pl.pallas_call(
        inverse_plane_kernel,
        grid=(sets, planes // plane_step),
        in_specs=[
            pl.BlockSpec((1, 2, plane_step, x.shape[3], size), lambda s, i: (s, 0, i, 0, 0))
            for x in spectra
        ]
        + [ly_spec, rz_spec],
        out_specs=pl.BlockSpec((1, plane_step, size, size), lambda s, i: (s, i, 0, 0)),
        out_shape=jax.ShapeDtypeStruct((sets, planes, size, size), F32),
    )(*spectra, *tables)


def gather_by_sum(piece, axis_name, dim):
    count = lax.axis_size(axis_name)
    index = lax.axis_index(axis_name)
    width = piece.shape[dim]
    shape = list(piece.shape)
    shape[dim] = width * count
    start = [0] * len(shape)
    start[dim] = index * width
    placed = lax.dynamic_update_slice(jnp.zeros(shape, piece.dtype), piece, start)
    return lax.psum(placed, axis_name)


def gather_pieces(piece, axis_name, dim):
    count = lax.axis_size(axis_name)
    if count & (count - 1):
        return gather_by_sum(piece, axis_name, dim)
    index = lax.axis_index(axis_name)
    held = piece
    step = 1
    while step < count:
        pairs = [(i, i ^ step) for i in range(count)]
        other = lax.ppermute(held, axis_name, perm=pairs)
        low_half = (index // step) % 2 == 0
        held = jnp.where(
            low_half,
            jnp.concatenate([held, other], axis=dim),
            jnp.concatenate([other, held], axis=dim),
        )
        step *= 2
    return held


def gather_direct(piece, axis_name, dim):
    count = lax.axis_size(axis_name)
    index = lax.axis_index(axis_name)
    held = [piece]
    for hop in range(1, count):
        pairs = [(i, (i + hop) % count) for i in range(count)]
        held.append(lax.ppermute(piece, axis_name, perm=pairs))
    stacked = jnp.stack(held, axis=0)
    order = (index - jnp.arange(count)) % count
    ordered = jnp.take(stacked, order, axis=0, mode="clip")
    ordered = jnp.moveaxis(ordered, 0, dim)
    shape = list(piece.shape)
    shape[dim] = shape[dim] * count
    return ordered.reshape(shape)


def score_grids(receptor, ligand_box, channel_weight):
    size = receptor.shape[2]
    slab_count = lax.axis_size("slab")
    part = receptor.shape[1]
    box = ligand_box.shape[4]
    sets = ligand_box.shape[0]
    extra = -(-(box - 1) // part)
    window = part * (1 + extra)
    plane_step = 8
    row_step = 16

    lead = ligand_box.shape[:4]
    dense = ligand_box.reshape(lead + (box * box,))
    full_box = gather_direct(dense, "slab", 3)
    cos_n, sin_n = phase_tables(size, size, size)
    rz = block2(cos_n, -sin_n, sin_n, cos_n)
    ly = block2(cos_n, sin_n, -sin_n, cos_n)
    splits = max(1, min(4, size // (2 * row_step)))
    full_box, receptor = lax.optimization_barrier((full_box, receptor))
    own = forward_planes(receptor, (rz, ly), plane_step, size, splits)
    own = own if splits > 1 else [own]
    arrived = []
    for hop in range(1, extra + 1):
        pairs = [(i, (i - hop) % slab_count) for i in range(slab_count)]
        arrived.append([lax.ppermute(rows, "slab", perm=pairs) for rows in own])

    lig = jnp.stack(
        [full_box[:, 0, 0] * channel_weight[0], full_box[:, 0, 1] * channel_weight[1]], axis=0
    ).reshape(2, sets * box, box, box)
    cos_b, sin_b = phase_tables(box, size, size)
    rz_box = block2(cos_b, -sin_b, sin_b, cos_b)
    ly_box = block2(cos_b.T, sin_b.T, -sin_b.T, cos_b.T)
    lig_yz = forward_planes(lig, (rz_box, ly_box), plane_step, size)

    cos_w, sin_w = phase_tables(window, window, window)
    g_tables = []
    for index in range(1 + extra):
        cols = slice(index * part, (index + 1) * part)
        g_tables.append(block2(cos_w[:, cols], sin_w[:, cols], -sin_w[:, cols], cos_w[:, cols]))
    cos_xb, sin_xb = phase_tables(window, box, window)
    gl = block2(cos_xb, sin_xb, -sin_xb, cos_xb)
    cos_t, sin_t = phase_tables(part, window, window)
    scale = 1.0 / float(window * size * size)
    hx = block2(cos_t, -sin_t, sin_t, cos_t) * scale
    step = size // splits
    back_x = []
    for q in range(splits):
        rec_blocks = [own[q]] + [hop_rows[q] for hop_rows in arrived]
        back_x.append(
            cross_spectra(rec_blocks, lig_yz, g_tables, gl, hx, sets, box, window, row_step, q * step)
        )

    lyi = block2(cos_n, -sin_n, sin_n, cos_n)
    rzi = jnp.concatenate([cos_n, -sin_n], axis=0)
    inverse_tables = (lyi, rzi)
    grids = inverse_planes(back_x, inverse_tables, plane_step)
    return grids.reshape(sets, 1, part, size, size), own


def pose_statistics(
    rotation_table,
    ligand_atoms,
    cluster_center,
    pose_rotation,
    pose_translation,
    pose_owner,
    pose_member,
    size,
):
    all_centers = gather_pieces(cluster_center, "rot", 0)
    local_count = cluster_center.shape[0]
    cluster = pose_owner[:, 0] * local_count + pose_member
    rotation = jnp.take(rotation_table, pose_rotation, axis=1, mode="clip").T.reshape(-1, 3, 3)
    coords = jnp.stack(
        [
            pose_translation // (size * size),
            pose_translation // size % size,
            pose_translation % size,
        ],
        axis=1,
    )
    shifts = ((coords + size // 2) % size - size // 2).astype(F32) / size
    center = jnp.take(all_centers, cluster, axis=0, mode="clip")
    moved = jnp.einsum("pjk,ka->pja", rotation, ligand_atoms, precision=PRECISE) + shifts[:, :, None]
    spread = moved - center
    mean_square = jnp.mean(jnp.sum(spread * spread, axis=1), axis=1)
    moved_centred = moved - jnp.mean(moved, axis=2, keepdims=True)
    center_centred = center - jnp.mean(center, axis=2, keepdims=True)
    covariance = jnp.einsum("pja,pka->pjk", moved_centred, center_centred, precision=PRECISE)
    stats = jnp.concatenate([covariance.reshape(-1, 9), mean_square[:, None]], axis=1)
    return stats.T


def local(
    receptor,
    ligand_box,
    channel_weight,
    rotation_table,
    ligand_atoms,
    cluster_center,
    pose_rotation,
    pose_translation,
    pose_owner,
    pose_member,
):
    size = receptor.shape[2]
    scores, own = score_grids(receptor, ligand_box, channel_weight)
    cluster_center, own = lax.optimization_barrier((cluster_center, own))
    pose_stats = pose_statistics(
        rotation_table,
        ligand_atoms,
        cluster_center,
        pose_rotation,
        pose_translation,
        pose_owner,
        pose_member,
        size,
    )
    return (scores, pose_stats)


def solution(mesh):
    return jax.shard_map(
        local,
        mesh=mesh,
        in_specs=(
            P(None, "slab", None, None),
            P(None, "rot", None, "slab", None, None),
            P(),
            P(),
            P(),
            P("rot", None, None),
            P(("slab", "rot")),
            P(("slab", "rot")),
            P(("slab", "rot"), None),
            P(("slab", "rot")),
        ),
        out_specs=(P(None, "rot", "slab", None, None), P(None, ("slab", "rot"))),
        check_vma=False,
    )
```

```python
import functools

import jax
import jax.numpy as jnp
from jax import lax
from jax.experimental import pallas as pl
from jax.experimental.pallas import tpu as pltpu
from jax.sharding import PartitionSpec as P

PRECISE = lax.Precision.HIGHEST
SPLIT3 = lax.Precision.HIGH
TWO_PI = 6.283185307179586
F32 = jnp.float32
BF16 = jnp.bfloat16


def phase_tables(rows, cols, length):
    row_index = lax.broadcasted_iota(jnp.int32, (rows, cols), 0)
    col_index = lax.broadcasted_iota(jnp.int32, (rows, cols), 1)
    phase = (row_index * col_index % length).astype(F32) * (TWO_PI / length)
    return (jnp.cos(phase), jnp.sin(phase))


def block2(top_left, top_right, bottom_left, bottom_right):
    top = jnp.concatenate([top_left, top_right], axis=1)
    bottom = jnp.concatenate([bottom_left, bottom_right], axis=1)
    return jnp.concatenate([top, bottom], axis=0)


def hi_lo(table):
    high = table.astype(BF16)
    low = (table - high.astype(F32)).astype(BF16)
    return high, low


def split_dot(a, b_high, b_low, a_left):
    a_high = a.astype(BF16)
    a_low = (a - a_high.astype(F32)).astype(BF16)
    dot = functools.partial(jnp.dot, preferred_element_type=F32)
    if a_left:
        return dot(a_high, b_high) + (dot(a_low, b_high) + dot(a_high, b_low))
    return dot(b_high, a_high) + (dot(b_high, a_low) + dot(b_low, a_high))


def forward_plane_kernel(in_ref, rz_ref, ly_ref, *out_refs):
    planes, rows, cols = in_ref.shape[1], in_ref.shape[2], in_ref.shape[3]
    size = out_refs[0].shape[3]
    rz_hi, rz_lo = hi_lo(rz_ref[...])
    ly_hi, ly_lo = hi_lo(ly_ref[...])
    joined = jnp.concatenate(
        [in_ref[0].reshape(planes * rows, cols), in_ref[1].reshape(planes * rows, cols)], axis=1
    )
    along_z = split_dot(joined, rz_hi, rz_lo, True)
    stacked = jnp.concatenate(
        [
            jnp.concatenate(
                [along_z[p * rows : (p + 1) * rows, :size], along_z[p * rows : (p + 1) * rows, size:]],
                axis=0,
            )
            for p in range(planes)
        ],
        axis=1,
    )
    along_y = split_dot(stacked, ly_hi, ly_lo, False)
    step = size // len(out_refs)
    for q, out_ref in enumerate(out_refs):
        for p in range(planes):
            cols = slice(p * size, (p + 1) * size)
            out_ref[0, p] = along_y[q * step : (q + 1) * step, cols]
            out_ref[1, p] = along_y[size + q * step : size + (q + 1) * step, cols]


def inverse_plane_kernel(*refs):
    in_refs = refs[:-3]
    ly_ref, rz_ref, out_ref = refs[-3:]
    planes = in_refs[0].shape[2]
    size = in_refs[0].shape[4]
    ly_hi, ly_lo = hi_lo(ly_ref[...])
    rz_hi, rz_lo = hi_lo(rz_ref[...])

    def plane(c, p):
        return jnp.concatenate([r[0, c, p] for r in in_refs], axis=0)

    stacked = jnp.concatenate(
        [jnp.concatenate([plane(0, p), plane(1, p)], axis=0) for p in range(planes)], axis=1
    )
    along_y = split_dot(stacked, ly_hi, ly_lo, False)
    joined = jnp.concatenate(
        [
            jnp.concatenate(
                [along_y[:size, p * size : (p + 1) * size], along_y[size:, p * size : (p + 1) * size]],
                axis=1,
            )
            for p in range(planes)
        ],
        axis=0,
    )
    out_ref[0] = split_dot(joined, rz_hi, rz_lo, True).reshape(planes, size, size)


def forward_planes(block, tables, plane_step, size, splits=1):
    planes, rows, cols = block.shape[1], block.shape[2], block.shape[3]
    table_specs = [pl.BlockSpec(t.shape, lambda i: (0, 0)) for t in tables]
    step = size // splits
    outs = pl.pallas_call(
        forward_plane_kernel,
        grid=(planes // plane_step,),
        in_specs=[pl.BlockSpec((2, plane_step, rows, cols), lambda i: (0, i, 0, 0))] + table_specs,
        out_specs=[pl.BlockSpec((2, plane_step, step, size), lambda i: (0, i, 0, 0))] * splits,
        out_shape=[jax.ShapeDtypeStruct((2, planes, step, size), F32)] * splits,
    )(block, *tables)
    return outs if splits > 1 else outs[0]


def cross_kernel(*refs, blocks, sets, box, window, part):
    rec_refs = refs[:blocks]
    lig_ref = refs[blocks]
    g_hi, g_lo = hi_lo(refs[blocks + 1][...])
    gl_hi, gl_lo = hi_lo(refs[blocks + 2][...])
    h_hi, h_lo = hi_lo(refs[blocks + 3][...])
    out_ref = refs[-1]
    rows = out_ref.shape[3]
    lanes = out_ref.shape[4]

    def gathered(ref, lo, count):
        turned = [jnp.swapaxes(ref[c, lo : lo + count], 0, 1) for c in range(2)]
        return jnp.concatenate(
            [jnp.concatenate([turned[0][r], turned[1][r]], axis=0) for r in range(rows)], axis=1
        )

    rec_in = jnp.concatenate(
        [gathered(rec_refs[b], 0, rec_refs[b].shape[1]) for b in range(blocks)], axis=0
    )
    rec = split_dot(rec_in, g_hi, g_lo, False)
    rec = jnp.concatenate([rec] * sets, axis=1)
    lig_in = jnp.concatenate([gathered(lig_ref, s * box, box) for s in range(sets)], axis=1)
    lig = split_dot(lig_in, gl_hi, gl_lo, False)
    rec_real = rec[:window]
    rec_imag = rec[window:]
    lig_real = lig[:window]
    lig_imag = lig[window:]
    prod = jnp.concatenate(
        [rec_real * lig_real + rec_imag * lig_imag, rec_imag * lig_real - rec_real * lig_imag],
        axis=0,
    )
    back = split_dot(prod, h_hi, h_lo, False)
    width = rows * lanes
    for s in range(sets):
        for c in range(2):
            pieces = jnp.stack(
                [
                    back[c * part : (c + 1) * part, s * width + r * lanes : s * width + (r + 1) * lanes]
                    for r in range(rows)
                ],
                axis=0,
            )
            out_ref[s, c] = jnp.swapaxes(pieces, 0, 1)


def cross_spectra(rec_blocks, lig_yz, g_tables, gl, hx, sets, box, window, row_step, lig_from):
    part = hx.shape[0] // 2
    size = rec_blocks[0].shape[2]
    offset = lig_from // row_step
    lanes = rec_blocks[0].shape[3]
    blocks = len(rec_blocks)
    tables = [jnp.concatenate(g_tables, axis=1), gl, hx]
    kernel = functools.partial(
        cross_kernel, blocks=blocks, sets=sets, box=box, window=window, part=part
    )
    return pl.pallas_call(
        kernel,
        grid=(size // row_step,),
        in_specs=[pl.BlockSpec((2, b.shape[1], row_step, lanes), lambda i: (0, 0, i, 0)) for b in rec_blocks]
        + [pl.BlockSpec((2, sets * box, row_step, lanes), lambda i: (0, 0, i + offset, 0))]
        + [pl.BlockSpec(t.shape, lambda i: (0, 0)) for t in tables],
        out_specs=pl.BlockSpec((sets, 2, part, row_step, lanes), lambda i: (0, 0, 0, i, 0)),
        out_shape=jax.ShapeDtypeStruct((sets, 2, part, size, lanes), F32),
    )(*rec_blocks, lig_yz, *tables)


def inverse_planes(spectra, tables, plane_step):
    sets, planes, size = spectra[0].shape[0], spectra[0].shape[2], spectra[0].shape[4]
    ly_spec = pl.BlockSpec((2 * size, 2 * size), lambda s, i: (0, 0))
    rz_spec = pl.BlockSpec((2 * size, size), lambda s, i: (0, 0))
    return pl.pallas_call(
        inverse_plane_kernel,
        grid=(sets, planes // plane_step),
        in_specs=[
            pl.BlockSpec((1, 2, plane_step, x.shape[3], size), lambda s, i: (s, 0, i, 0, 0))
            for x in spectra
        ]
        + [ly_spec, rz_spec],
        out_specs=pl.BlockSpec((1, plane_step, size, size), lambda s, i: (s, i, 0, 0)),
        out_shape=jax.ShapeDtypeStruct((sets, planes, size, size), F32),
    )(*spectra, *tables)


def gather_by_sum(piece, axis_name, dim):
    count = lax.axis_size(axis_name)
    index = lax.axis_index(axis_name)
    width = piece.shape[dim]
    shape = list(piece.shape)
    shape[dim] = width * count
    start = [0] * len(shape)
    start[dim] = index * width
    placed = lax.dynamic_update_slice(jnp.zeros(shape, piece.dtype), piece, start)
    return lax.psum(placed, axis_name)


def gather_pieces(piece, axis_name, dim):
    count = lax.axis_size(axis_name)
    if count & (count - 1):
        return gather_by_sum(piece, axis_name, dim)
    index = lax.axis_index(axis_name)
    held = piece
    step = 1
    while step < count:
        pairs = [(i, i ^ step) for i in range(count)]
        other = lax.ppermute(held, axis_name, perm=pairs)
        low_half = (index // step) % 2 == 0
        held = jnp.where(
            low_half,
            jnp.concatenate([held, other], axis=dim),
            jnp.concatenate([other, held], axis=dim),
        )
        step *= 2
    return held


def gather_direct(piece, axis_name, dim):
    count = lax.axis_size(axis_name)
    index = lax.axis_index(axis_name)
    held = [piece]
    for hop in range(1, count):
        pairs = [(i, (i + hop) % count) for i in range(count)]
        held.append(lax.ppermute(piece, axis_name, perm=pairs))
    stacked = jnp.stack(held, axis=0)
    order = (index - jnp.arange(count)) % count
    ordered = jnp.take(stacked, order, axis=0, mode="clip")
    ordered = jnp.moveaxis(ordered, 0, dim)
    shape = list(piece.shape)
    shape[dim] = shape[dim] * count
    return ordered.reshape(shape)


def score_grids(receptor, ligand_box, channel_weight):
    size = receptor.shape[2]
    slab_count = lax.axis_size("slab")
    part = receptor.shape[1]
    box = ligand_box.shape[4]
    sets = ligand_box.shape[0]
    extra = -(-(box - 1) // part)
    window = part * (1 + extra)
    plane_step = 8
    row_step = 16

    lead = ligand_box.shape[:4]
    dense = ligand_box.reshape(lead + (box * box,))
    full_box = gather_direct(dense, "slab", 3)
    cos_n, sin_n = phase_tables(size, size, size)
    rz = block2(cos_n, -sin_n, sin_n, cos_n)
    ly = block2(cos_n, sin_n, -sin_n, cos_n)
    splits = max(1, min(2, size // (2 * row_step)))
    own = forward_planes(receptor, (rz, ly), plane_step, size, splits)
    own = own if splits > 1 else [own]
    arrived = []
    for hop in range(1, extra + 1):
        pairs = [(i, (i - hop) % slab_count) for i in range(slab_count)]
        arrived.append([lax.ppermute(rows, "slab", perm=pairs) for rows in own])

    lig = jnp.stack(
        [full_box[:, 0, 0] * channel_weight[0], full_box[:, 0, 1] * channel_weight[1]], axis=0
    ).reshape(2, sets * box, box, box)
    cos_b, sin_b = phase_tables(box, size, size)
    rz_box = block2(cos_b, -sin_b, sin_b, cos_b)
    ly_box = block2(cos_b.T, sin_b.T, -sin_b.T, cos_b.T)
    lig_yz = forward_planes(lig, (rz_box, ly_box), plane_step, size)

    cos_w, sin_w = phase_tables(window, window, window)
    g_tables = []
    for index in range(1 + extra):
        cols = slice(index * part, (index + 1) * part)
        g_tables.append(block2(cos_w[:, cols], sin_w[:, cols], -sin_w[:, cols], cos_w[:, cols]))
    cos_xb, sin_xb = phase_tables(window, box, window)
    gl = block2(cos_xb, sin_xb, -sin_xb, cos_xb)
    cos_t, sin_t = phase_tables(part, window, window)
    scale = 1.0 / float(window * size * size)
    hx = block2(cos_t, -sin_t, sin_t, cos_t) * scale
    step = size // splits
    back_x = []
    for q in range(splits):
        rec_blocks = [own[q]] + [hop_rows[q] for hop_rows in arrived]
        back_x.append(
            cross_spectra(rec_blocks, lig_yz, g_tables, gl, hx, sets, box, window, row_step, q * step)
        )

    lyi = block2(cos_n, -sin_n, sin_n, cos_n)
    rzi = jnp.concatenate([cos_n, -sin_n], axis=0)
    inverse_tables = (lyi, rzi)
    grids = inverse_planes(back_x, inverse_tables, plane_step)
    return grids.reshape(sets, 1, part, size, size), arrived[0][0]


def pose_statistics(
    rotation_table,
    ligand_atoms,
    cluster_center,
    pose_rotation,
    pose_translation,
    pose_owner,
    pose_member,
    size,
):
    all_centers = gather_pieces(cluster_center, "rot", 0)
    local_count = cluster_center.shape[0]
    cluster = pose_owner[:, 0] * local_count + pose_member
    rotation = jnp.take(rotation_table, pose_rotation, axis=1, mode="clip").T.reshape(-1, 3, 3)
    coords = jnp.stack(
        [
            pose_translation // (size * size),
            pose_translation // size % size,
            pose_translation % size,
        ],
        axis=1,
    )
    shifts = ((coords + size // 2) % size - size // 2).astype(F32) / size
    center = jnp.take(all_centers, cluster, axis=0, mode="clip")
    moved = jnp.einsum("pjk,ka->pja", rotation, ligand_atoms, precision=PRECISE) + shifts[:, :, None]
    spread = moved - center
    mean_square = jnp.mean(jnp.sum(spread * spread, axis=1), axis=1)
    moved_centred = moved - jnp.mean(moved, axis=2, keepdims=True)
    center_centred = center - jnp.mean(center, axis=2, keepdims=True)
    covariance = jnp.einsum("pja,pka->pjk", moved_centred, center_centred, precision=PRECISE)
    stats = jnp.concatenate([covariance.reshape(-1, 9), mean_square[:, None]], axis=1)
    return stats.T


def local(
    receptor,
    ligand_box,
    channel_weight,
    rotation_table,
    ligand_atoms,
    cluster_center,
    pose_rotation,
    pose_translation,
    pose_owner,
    pose_member,
):
    size = receptor.shape[2]
    scores, first_rows = score_grids(receptor, ligand_box, channel_weight)
    cluster_center, first_rows = lax.optimization_barrier((cluster_center, first_rows))
    pose_stats = pose_statistics(
        rotation_table,
        ligand_atoms,
        cluster_center,
        pose_rotation,
        pose_translation,
        pose_owner,
        pose_member,
        size,
    )
    return (scores, pose_stats)


def solution(mesh):
    return jax.shard_map(
        local,
        mesh=mesh,
        in_specs=(
            P(None, "slab", None, None),
            P(None, "rot", None, "slab", None, None),
            P(),
            P(),
            P(),
            P("rot", None, None),
            P(("slab", "rot")),
            P(("slab", "rot")),
            P(("slab", "rot"), None),
            P(("slab", "rot")),
        ),
        out_specs=(P(None, "rot", "slab", None, None), P(None, ("slab", "rot"))),
        check_vma=False,
    )
```

```python
import functools

import jax
import jax.numpy as jnp
from jax import lax
from jax.experimental import pallas as pl
from jax.experimental.pallas import tpu as pltpu
from jax.sharding import PartitionSpec as P

PRECISE = lax.Precision.HIGHEST
SPLIT3 = lax.Precision.HIGH
TWO_PI = 6.283185307179586
F32 = jnp.float32
BF16 = jnp.bfloat16


def phase_tables(rows, cols, length):
    row_index = lax.broadcasted_iota(jnp.int32, (rows, cols), 0)
    col_index = lax.broadcasted_iota(jnp.int32, (rows, cols), 1)
    phase = (row_index * col_index % length).astype(F32) * (TWO_PI / length)
    return (jnp.cos(phase), jnp.sin(phase))


def block2(top_left, top_right, bottom_left, bottom_right):
    top = jnp.concatenate([top_left, top_right], axis=1)
    bottom = jnp.concatenate([bottom_left, bottom_right], axis=1)
    return jnp.concatenate([top, bottom], axis=0)


def hi_lo(table):
    high = table.astype(BF16)
    low = (table - high.astype(F32)).astype(BF16)
    return high, low


def split_dot(a, b_high, b_low, a_left):
    a_high = a.astype(BF16)
    a_low = (a - a_high.astype(F32)).astype(BF16)
    dot = functools.partial(jnp.dot, preferred_element_type=F32)
    if a_left:
        return dot(a_high, b_high) + (dot(a_low, b_high) + dot(a_high, b_low))
    return dot(b_high, a_high) + (dot(b_high, a_low) + dot(b_low, a_high))


def forward_plane_kernel(in_ref, rz_ref, ly_ref, *out_refs):
    planes, rows, cols = in_ref.shape[1], in_ref.shape[2], in_ref.shape[3]
    size = out_refs[0].shape[3]
    rz_hi, rz_lo = hi_lo(rz_ref[...])
    ly_hi, ly_lo = hi_lo(ly_ref[...])
    joined = jnp.concatenate(
        [in_ref[0].reshape(planes * rows, cols), in_ref[1].reshape(planes * rows, cols)], axis=1
    )
    along_z = split_dot(joined, rz_hi, rz_lo, True)
    stacked = jnp.concatenate(
        [
            jnp.concatenate(
                [along_z[p * rows : (p + 1) * rows, :size], along_z[p * rows : (p + 1) * rows, size:]],
                axis=0,
            )
            for p in range(planes)
        ],
        axis=1,
    )
    along_y = split_dot(stacked, ly_hi, ly_lo, False)
    step = size // len(out_refs)
    for q, out_ref in enumerate(out_refs):
        for p in range(planes):
            cols = slice(p * size, (p + 1) * size)
            out_ref[0, p] = along_y[q * step : (q + 1) * step, cols]
            out_ref[1, p] = along_y[size + q * step : size + (q + 1) * step, cols]


def inverse_plane_kernel(*refs):
    in_refs = refs[:-3]
    ly_ref, rz_ref, out_ref = refs[-3:]
    planes = in_refs[0].shape[2]
    size = in_refs[0].shape[4]
    ly_hi, ly_lo = hi_lo(ly_ref[...])
    rz_hi, rz_lo = hi_lo(rz_ref[...])

    def plane(c, p):
        return jnp.concatenate([r[0, c, p] for r in in_refs], axis=0)

    stacked = jnp.concatenate(
        [jnp.concatenate([plane(0, p), plane(1, p)], axis=0) for p in range(planes)], axis=1
    )
    along_y = split_dot(stacked, ly_hi, ly_lo, False)
    joined = jnp.concatenate(
        [
            jnp.concatenate(
                [along_y[:size, p * size : (p + 1) * size], along_y[size:, p * size : (p + 1) * size]],
                axis=1,
            )
            for p in range(planes)
        ],
        axis=0,
    )
    out_ref[0] = split_dot(joined, rz_hi, rz_lo, True).reshape(planes, size, size)


def forward_planes(block, tables, plane_step, size, splits=1):
    planes, rows, cols = block.shape[1], block.shape[2], block.shape[3]
    table_specs = [pl.BlockSpec(t.shape, lambda i: (0, 0)) for t in tables]
    step = size // splits
    outs = pl.pallas_call(
        forward_plane_kernel,
        grid=(planes // plane_step,),
        in_specs=[pl.BlockSpec((2, plane_step, rows, cols), lambda i: (0, i, 0, 0))] + table_specs,
        out_specs=[pl.BlockSpec((2, plane_step, step, size), lambda i: (0, i, 0, 0))] * splits,
        out_shape=[jax.ShapeDtypeStruct((2, planes, step, size), F32)] * splits,
    )(block, *tables)
    return outs if splits > 1 else outs[0]


def cross_kernel(*refs, blocks, sets, box, window, part):
    rec_refs = refs[:blocks]
    lig_ref = refs[blocks]
    g_hi, g_lo = hi_lo(refs[blocks + 1][...])
    gl_hi, gl_lo = hi_lo(refs[blocks + 2][...])
    h_hi, h_lo = hi_lo(refs[blocks + 3][...])
    out_ref = refs[-1]
    rows = out_ref.shape[3]
    lanes = out_ref.shape[4]

    def gathered(ref, lo, count):
        turned = [jnp.swapaxes(ref[c, lo : lo + count], 0, 1) for c in range(2)]
        return jnp.concatenate(
            [jnp.concatenate([turned[0][r], turned[1][r]], axis=0) for r in range(rows)], axis=1
        )

    rec_in = jnp.concatenate(
        [gathered(rec_refs[b], 0, rec_refs[b].shape[1]) for b in range(blocks)], axis=0
    )
    rec = split_dot(rec_in, g_hi, g_lo, False)
    rec = jnp.concatenate([rec] * sets, axis=1)
    lig_in = jnp.concatenate([gathered(lig_ref, s * box, box) for s in range(sets)], axis=1)
    lig = split_dot(lig_in, gl_hi, gl_lo, False)
    rec_real = rec[:window]
    rec_imag = rec[window:]
    lig_real = lig[:window]
    lig_imag = lig[window:]
    prod = jnp.concatenate(
        [rec_real * lig_real + rec_imag * lig_imag, rec_imag * lig_real - rec_real * lig_imag],
        axis=0,
    )
    back = split_dot(prod, h_hi, h_lo, False)
    width = rows * lanes
    for s in range(sets):
        for c in range(2):
            pieces = jnp.stack(
                [
                    back[c * part : (c + 1) * part, s * width + r * lanes : s * width + (r + 1) * lanes]
                    for r in range(rows)
                ],
                axis=0,
            )
            out_ref[s, c] = jnp.swapaxes(pieces, 0, 1)


def cross_spectra(rec_blocks, lig_yz, g_tables, gl, hx, sets, box, window, row_step, lig_from):
    part = hx.shape[0] // 2
    size = rec_blocks[0].shape[2]
    offset = lig_from // row_step
    lanes = rec_blocks[0].shape[3]
    blocks = len(rec_blocks)
    tables = [jnp.concatenate(g_tables, axis=1), gl, hx]
    kernel = functools.partial(
        cross_kernel, blocks=blocks, sets=sets, box=box, window=window, part=part
    )
    return pl.pallas_call(
        kernel,
        grid=(size // row_step,),
        in_specs=[pl.BlockSpec((2, b.shape[1], row_step, lanes), lambda i: (0, 0, i, 0)) for b in rec_blocks]
        + [pl.BlockSpec((2, sets * box, row_step, lanes), lambda i: (0, 0, i + offset, 0))]
        + [pl.BlockSpec(t.shape, lambda i: (0, 0)) for t in tables],
        out_specs=pl.BlockSpec((sets, 2, part, row_step, lanes), lambda i: (0, 0, 0, i, 0)),
        out_shape=jax.ShapeDtypeStruct((sets, 2, part, size, lanes), F32),
    )(*rec_blocks, lig_yz, *tables)


def inverse_planes(spectra, tables, plane_step):
    sets, planes, size = spectra[0].shape[0], spectra[0].shape[2], spectra[0].shape[4]
    ly_spec = pl.BlockSpec((2 * size, 2 * size), lambda s, i: (0, 0))
    rz_spec = pl.BlockSpec((2 * size, size), lambda s, i: (0, 0))
    return pl.pallas_call(
        inverse_plane_kernel,
        grid=(sets, planes // plane_step),
        in_specs=[
            pl.BlockSpec((1, 2, plane_step, x.shape[3], size), lambda s, i: (s, 0, i, 0, 0))
            for x in spectra
        ]
        + [ly_spec, rz_spec],
        out_specs=pl.BlockSpec((1, plane_step, size, size), lambda s, i: (s, i, 0, 0)),
        out_shape=jax.ShapeDtypeStruct((sets, planes, size, size), F32),
    )(*spectra, *tables)


def gather_by_sum(piece, axis_name, dim):
    count = lax.axis_size(axis_name)
    index = lax.axis_index(axis_name)
    width = piece.shape[dim]
    shape = list(piece.shape)
    shape[dim] = width * count
    start = [0] * len(shape)
    start[dim] = index * width
    placed = lax.dynamic_update_slice(jnp.zeros(shape, piece.dtype), piece, start)
    return lax.psum(placed, axis_name)


def gather_pieces(piece, axis_name, dim):
    count = lax.axis_size(axis_name)
    if count & (count - 1):
        return gather_by_sum(piece, axis_name, dim)
    index = lax.axis_index(axis_name)
    held = piece
    step = 1
    while step < count:
        pairs = [(i, i ^ step) for i in range(count)]
        other = lax.ppermute(held, axis_name, perm=pairs)
        low_half = (index // step) % 2 == 0
        held = jnp.where(
            low_half,
            jnp.concatenate([held, other], axis=dim),
            jnp.concatenate([other, held], axis=dim),
        )
        step *= 2
    return held


def gather_direct(piece, axis_name, dim):
    count = lax.axis_size(axis_name)
    index = lax.axis_index(axis_name)
    held = [piece]
    for hop in range(1, count):
        pairs = [(i, (i + hop) % count) for i in range(count)]
        held.append(lax.ppermute(piece, axis_name, perm=pairs))
    stacked = jnp.stack(held, axis=0)
    order = (index - jnp.arange(count)) % count
    ordered = jnp.take(stacked, order, axis=0, mode="clip")
    ordered = jnp.moveaxis(ordered, 0, dim)
    shape = list(piece.shape)
    shape[dim] = shape[dim] * count
    return ordered.reshape(shape)


def score_grids(receptor, ligand_box, channel_weight):
    size = receptor.shape[2]
    slab_count = lax.axis_size("slab")
    part = receptor.shape[1]
    box = ligand_box.shape[4]
    sets = ligand_box.shape[0]
    extra = -(-(box - 1) // part)
    window = part * (1 + extra)
    plane_step = 8
    row_step = 16

    lead = ligand_box.shape[:4]
    dense = ligand_box.reshape(lead + (box * box,))
    full_box = gather_direct(dense, "slab", 3)
    cos_n, sin_n = phase_tables(size, size, size)
    rz = block2(cos_n, -sin_n, sin_n, cos_n)
    ly = block2(cos_n, sin_n, -sin_n, cos_n)
    splits = max(1, min(2, size // (2 * row_step)))
    own = forward_planes(receptor, (rz, ly), plane_step, size, splits)
    own = own if splits > 1 else [own]
    arrived = []
    for hop in range(1, extra + 1):
        pairs = [(i, (i - hop) % slab_count) for i in range(slab_count)]
        arrived.append([lax.ppermute(rows, "slab", perm=pairs) for rows in own])

    lig = jnp.stack(
        [full_box[:, 0, 0] * channel_weight[0], full_box[:, 0, 1] * channel_weight[1]], axis=0
    ).reshape(2, sets * box, box, box)
    cos_b, sin_b = phase_tables(box, size, size)
    rz_box = block2(cos_b, -sin_b, sin_b, cos_b)
    ly_box = block2(cos_b.T, sin_b.T, -sin_b.T, cos_b.T)
    lig_yz = forward_planes(lig, (rz_box, ly_box), plane_step, size)

    cos_w, sin_w = phase_tables(window, window, window)
    g_tables = []
    for index in range(1 + extra):
        cols = slice(index * part, (index + 1) * part)
        g_tables.append(block2(cos_w[:, cols], sin_w[:, cols], -sin_w[:, cols], cos_w[:, cols]))
    cos_xb, sin_xb = phase_tables(window, box, window)
    gl = block2(cos_xb, sin_xb, -sin_xb, cos_xb)
    cos_t, sin_t = phase_tables(part, window, window)
    scale = 1.0 / float(window * size * size)
    hx = block2(cos_t, -sin_t, sin_t, cos_t) * scale
    step = size // splits
    back_x = []
    for q in range(splits):
        rec_blocks = [own[q]] + [hop_rows[q] for hop_rows in arrived]
        back_x.append(
            cross_spectra(rec_blocks, lig_yz, g_tables, gl, hx, sets, box, window, row_step, q * step)
        )

    lyi = block2(cos_n, -sin_n, sin_n, cos_n)
    rzi = jnp.concatenate([cos_n, -sin_n], axis=0)
    inverse_tables = (lyi, rzi)
    grids = inverse_planes(back_x, inverse_tables, plane_step)
    return grids.reshape(sets, 1, part, size, size), lig_yz


def pose_statistics(
    rotation_table,
    ligand_atoms,
    cluster_center,
    pose_rotation,
    pose_translation,
    pose_owner,
    pose_member,
    size,
):
    all_centers = gather_pieces(cluster_center, "rot", 0)
    local_count = cluster_center.shape[0]
    cluster = pose_owner[:, 0] * local_count + pose_member
    rotation = jnp.take(rotation_table, pose_rotation, axis=1, mode="clip").T.reshape(-1, 3, 3)
    coords = jnp.stack(
        [
            pose_translation // (size * size),
            pose_translation // size % size,
            pose_translation % size,
        ],
        axis=1,
    )
    shifts = ((coords + size // 2) % size - size // 2).astype(F32) / size
    center = jnp.take(all_centers, cluster, axis=0, mode="clip")
    moved = jnp.einsum("pjk,ka->pja", rotation, ligand_atoms, precision=PRECISE) + shifts[:, :, None]
    spread = moved - center
    mean_square = jnp.mean(jnp.sum(spread * spread, axis=1), axis=1)
    moved_centred = moved - jnp.mean(moved, axis=2, keepdims=True)
    center_centred = center - jnp.mean(center, axis=2, keepdims=True)
    covariance = jnp.einsum("pja,pka->pjk", moved_centred, center_centred, precision=PRECISE)
    stats = jnp.concatenate([covariance.reshape(-1, 9), mean_square[:, None]], axis=1)
    return stats.T


def local(
    receptor,
    ligand_box,
    channel_weight,
    rotation_table,
    ligand_atoms,
    cluster_center,
    pose_rotation,
    pose_translation,
    pose_owner,
    pose_member,
):
    size = receptor.shape[2]
    scores, first_rows = score_grids(receptor, ligand_box, channel_weight)
    cluster_center, first_rows = lax.optimization_barrier((cluster_center, first_rows))
    pose_stats = pose_statistics(
        rotation_table,
        ligand_atoms,
        cluster_center,
        pose_rotation,
        pose_translation,
        pose_owner,
        pose_member,
        size,
    )
    return (scores, pose_stats)


def solution(mesh):
    return jax.shard_map(
        local,
        mesh=mesh,
        in_specs=(
            P(None, "slab", None, None),
            P(None, "rot", None, "slab", None, None),
            P(),
            P(),
            P(),
            P("rot", None, None),
            P(("slab", "rot")),
            P(("slab", "rot")),
            P(("slab", "rot"), None),
            P(("slab", "rot")),
        ),
        out_specs=(P(None, "rot", "slab", None, None), P(None, ("slab", "rot"))),
        check_vma=False,
    )
```

```python
import functools

import jax
import jax.numpy as jnp
import numpy as np
from jax import lax
from jax.experimental import pallas as pl
from jax.experimental.pallas import tpu as pltpu
from jax.sharding import PartitionSpec as P

PRECISE = lax.Precision.HIGHEST
SPLIT3 = lax.Precision.HIGH
TWO_PI = 6.283185307179586
F32 = jnp.float32
BF16 = jnp.bfloat16


def phase_tables(rows, cols, length):
    turns = np.outer(np.arange(rows), np.arange(cols)) % length
    phase = turns.astype(np.float64) * (TWO_PI / length)
    return (np.cos(phase), np.sin(phase))


def block2(top_left, top_right, bottom_left, bottom_right):
    top = np.concatenate([top_left, top_right], axis=1)
    bottom = np.concatenate([bottom_left, bottom_right], axis=1)
    return np.concatenate([top, bottom], axis=0).astype(np.float32)


def hi_lo(table):
    high = table.astype(BF16)
    low = (table - high.astype(F32)).astype(BF16)
    return high, low


def split_dot(a, b_high, b_low, a_left):
    a_high = a.astype(BF16)
    a_low = (a - a_high.astype(F32)).astype(BF16)
    dot = functools.partial(jnp.dot, preferred_element_type=F32)
    if a_left:
        return dot(a_high, b_high) + (dot(a_low, b_high) + dot(a_high, b_low))
    return dot(b_high, a_high) + (dot(b_high, a_low) + dot(b_low, a_high))


def forward_plane_kernel(in_ref, rz_ref, ly_ref, *out_refs):
    planes, rows, cols = in_ref.shape[1], in_ref.shape[2], in_ref.shape[3]
    size = out_refs[0].shape[3]
    rz_hi, rz_lo = hi_lo(rz_ref[...])
    ly_hi, ly_lo = hi_lo(ly_ref[...])
    joined = jnp.concatenate(
        [in_ref[0].reshape(planes * rows, cols), in_ref[1].reshape(planes * rows, cols)], axis=1
    )
    along_z = split_dot(joined, rz_hi, rz_lo, True)
    stacked = jnp.concatenate(
        [
            jnp.concatenate(
                [along_z[p * rows : (p + 1) * rows, :size], along_z[p * rows : (p + 1) * rows, size:]],
                axis=0,
            )
            for p in range(planes)
        ],
        axis=1,
    )
    along_y = split_dot(stacked, ly_hi, ly_lo, False)
    step = size // len(out_refs)
    for q, out_ref in enumerate(out_refs):
        for p in range(planes):
            cols = slice(p * size, (p + 1) * size)
            out_ref[0, p] = along_y[q * step : (q + 1) * step, cols]
            out_ref[1, p] = along_y[size + q * step : size + (q + 1) * step, cols]


def inverse_plane_kernel(*refs):
    in_refs = refs[:-3]
    ly_ref, rz_ref, out_ref = refs[-3:]
    planes = in_refs[0].shape[2]
    size = in_refs[0].shape[4]
    ly_hi, ly_lo = hi_lo(ly_ref[...])
    rz_hi, rz_lo = hi_lo(rz_ref[...])

    def plane(c, p):
        return jnp.concatenate([r[0, c, p] for r in in_refs], axis=0)

    stacked = jnp.concatenate(
        [jnp.concatenate([plane(0, p), plane(1, p)], axis=0) for p in range(planes)], axis=1
    )
    along_y = split_dot(stacked, ly_hi, ly_lo, False)
    joined = jnp.concatenate(
        [
            jnp.concatenate(
                [along_y[:size, p * size : (p + 1) * size], along_y[size:, p * size : (p + 1) * size]],
                axis=1,
            )
            for p in range(planes)
        ],
        axis=0,
    )
    out_ref[0] = split_dot(joined, rz_hi, rz_lo, True).reshape(planes, size, size)


def forward_planes(block, tables, plane_step, size, splits=1):
    planes, rows, cols = block.shape[1], block.shape[2], block.shape[3]
    table_specs = [pl.BlockSpec(t.shape, lambda i: (0, 0)) for t in tables]
    step = size // splits
    outs = pl.pallas_call(
        forward_plane_kernel,
        grid=(planes // plane_step,),
        in_specs=[pl.BlockSpec((2, plane_step, rows, cols), lambda i: (0, i, 0, 0))] + table_specs,
        out_specs=[pl.BlockSpec((2, plane_step, step, size), lambda i: (0, i, 0, 0))] * splits,
        out_shape=[jax.ShapeDtypeStruct((2, planes, step, size), F32)] * splits,
    )(block, *tables)
    return outs if splits > 1 else outs[0]


def cross_kernel(*refs, blocks, sets, box, window, part):
    rec_refs = refs[:blocks]
    lig_ref = refs[blocks]
    g_hi, g_lo = hi_lo(refs[blocks + 1][...])
    gl_hi, gl_lo = hi_lo(refs[blocks + 2][...])
    h_hi, h_lo = hi_lo(refs[blocks + 3][...])
    out_ref = refs[-1]
    rows = out_ref.shape[3]
    lanes = out_ref.shape[4]

    def gathered(ref, lo, count):
        turned = [jnp.swapaxes(ref[c, lo : lo + count], 0, 1) for c in range(2)]
        return jnp.concatenate(
            [jnp.concatenate([turned[0][r], turned[1][r]], axis=0) for r in range(rows)], axis=1
        )

    rec_in = jnp.concatenate(
        [gathered(rec_refs[b], 0, rec_refs[b].shape[1]) for b in range(blocks)], axis=0
    )
    rec = split_dot(rec_in, g_hi, g_lo, False)
    rec = jnp.concatenate([rec] * sets, axis=1)
    lig_in = jnp.concatenate([gathered(lig_ref, s * box, box) for s in range(sets)], axis=1)
    lig = split_dot(lig_in, gl_hi, gl_lo, False)
    rec_real = rec[:window]
    rec_imag = rec[window:]
    lig_real = lig[:window]
    lig_imag = lig[window:]
    prod = jnp.concatenate(
        [rec_real * lig_real + rec_imag * lig_imag, rec_imag * lig_real - rec_real * lig_imag],
        axis=0,
    )
    back = split_dot(prod, h_hi, h_lo, False)
    width = rows * lanes
    for s in range(sets):
        for c in range(2):
            pieces = jnp.stack(
                [
                    back[c * part : (c + 1) * part, s * width + r * lanes : s * width + (r + 1) * lanes]
                    for r in range(rows)
                ],
                axis=0,
            )
            out_ref[s, c] = jnp.swapaxes(pieces, 0, 1)


def cross_spectra(rec_blocks, lig_yz, g_tables, gl, hx, sets, box, window, row_step, lig_from):
    part = hx.shape[0] // 2
    size = rec_blocks[0].shape[2]
    offset = lig_from // row_step
    lanes = rec_blocks[0].shape[3]
    blocks = len(rec_blocks)
    tables = [np.concatenate(g_tables, axis=1), gl, hx]
    kernel = functools.partial(
        cross_kernel, blocks=blocks, sets=sets, box=box, window=window, part=part
    )
    return pl.pallas_call(
        kernel,
        grid=(size // row_step,),
        in_specs=[pl.BlockSpec((2, b.shape[1], row_step, lanes), lambda i: (0, 0, i, 0)) for b in rec_blocks]
        + [pl.BlockSpec((2, sets * box, row_step, lanes), lambda i: (0, 0, i + offset, 0))]
        + [pl.BlockSpec(t.shape, lambda i: (0, 0)) for t in tables],
        out_specs=pl.BlockSpec((sets, 2, part, row_step, lanes), lambda i: (0, 0, 0, i, 0)),
        out_shape=jax.ShapeDtypeStruct((sets, 2, part, size, lanes), F32),
    )(*rec_blocks, lig_yz, *tables)


def inverse_planes(spectra, tables, plane_step):
    sets, planes, size = spectra[0].shape[0], spectra[0].shape[2], spectra[0].shape[4]
    ly_spec = pl.BlockSpec((2 * size, 2 * size), lambda s, i: (0, 0))
    rz_spec = pl.BlockSpec((2 * size, size), lambda s, i: (0, 0))
    return pl.pallas_call(
        inverse_plane_kernel,
        grid=(sets, planes // plane_step),
        in_specs=[
            pl.BlockSpec((1, 2, plane_step, x.shape[3], size), lambda s, i: (s, 0, i, 0, 0))
            for x in spectra
        ]
        + [ly_spec, rz_spec],
        out_specs=pl.BlockSpec((1, plane_step, size, size), lambda s, i: (s, i, 0, 0)),
        out_shape=jax.ShapeDtypeStruct((sets, planes, size, size), F32),
    )(*spectra, *tables)


def gather_by_sum(piece, axis_name, dim):
    count = lax.axis_size(axis_name)
    index = lax.axis_index(axis_name)
    width = piece.shape[dim]
    shape = list(piece.shape)
    shape[dim] = width * count
    start = [0] * len(shape)
    start[dim] = index * width
    placed = lax.dynamic_update_slice(jnp.zeros(shape, piece.dtype), piece, start)
    return lax.psum(placed, axis_name)


def gather_pieces(piece, axis_name, dim):
    count = lax.axis_size(axis_name)
    if count & (count - 1):
        return gather_by_sum(piece, axis_name, dim)
    index = lax.axis_index(axis_name)
    held = piece
    step = 1
    while step < count:
        pairs = [(i, i ^ step) for i in range(count)]
        other = lax.ppermute(held, axis_name, perm=pairs)
        low_half = (index // step) % 2 == 0
        held = jnp.where(
            low_half,
            jnp.concatenate([held, other], axis=dim),
            jnp.concatenate([other, held], axis=dim),
        )
        step *= 2
    return held


def gather_direct(piece, axis_name, dim):
    count = lax.axis_size(axis_name)
    index = lax.axis_index(axis_name)
    held = [piece]
    for hop in range(1, count):
        pairs = [(i, (i + hop) % count) for i in range(count)]
        held.append(lax.ppermute(piece, axis_name, perm=pairs))
    stacked = jnp.stack(held, axis=0)
    order = (index - jnp.arange(count)) % count
    ordered = jnp.take(stacked, order, axis=0, mode="clip")
    ordered = jnp.moveaxis(ordered, 0, dim)
    shape = list(piece.shape)
    shape[dim] = shape[dim] * count
    return ordered.reshape(shape)


def score_grids(receptor, ligand_box, channel_weight):
    size = receptor.shape[2]
    slab_count = lax.axis_size("slab")
    part = receptor.shape[1]
    box = ligand_box.shape[4]
    sets = ligand_box.shape[0]
    extra = -(-(box - 1) // part)
    window = part * (1 + extra)
    plane_step = 8
    row_step = 16

    lead = ligand_box.shape[:4]
    dense = ligand_box.reshape(lead + (box * box,))
    full_box = gather_direct(dense, "slab", 3)
    cos_n, sin_n = phase_tables(size, size, size)
    rz = block2(cos_n, -sin_n, sin_n, cos_n)
    ly = block2(cos_n, sin_n, -sin_n, cos_n)
    splits = max(1, min(2, size // (2 * row_step)))
    own = forward_planes(receptor, (rz, ly), plane_step, size, splits)
    own = own if splits > 1 else [own]
    arrived = []
    for hop in range(1, extra + 1):
        pairs = [(i, (i - hop) % slab_count) for i in range(slab_count)]
        arrived.append([lax.ppermute(rows, "slab", perm=pairs) for rows in own])

    lig = jnp.stack(
        [full_box[:, 0, 0] * channel_weight[0], full_box[:, 0, 1] * channel_weight[1]], axis=0
    ).reshape(2, sets * box, box, box)
    cos_b, sin_b = phase_tables(box, size, size)
    rz_box = block2(cos_b, -sin_b, sin_b, cos_b)
    ly_box = block2(cos_b.T, sin_b.T, -sin_b.T, cos_b.T)
    lig_yz = forward_planes(lig, (rz_box, ly_box), plane_step, size)

    cos_w, sin_w = phase_tables(window, window, window)
    g_tables = []
    for index in range(1 + extra):
        cols = slice(index * part, (index + 1) * part)
        g_tables.append(block2(cos_w[:, cols], sin_w[:, cols], -sin_w[:, cols], cos_w[:, cols]))
    cos_xb, sin_xb = phase_tables(window, box, window)
    gl = block2(cos_xb, sin_xb, -sin_xb, cos_xb)
    cos_t, sin_t = phase_tables(part, window, window)
    scale = 1.0 / float(window * size * size)
    hx = (block2(cos_t, -sin_t, sin_t, cos_t) * scale).astype(np.float32)
    step = size // splits
    back_x = []
    for q in range(splits):
        rec_blocks = [own[q]] + [hop_rows[q] for hop_rows in arrived]
        back_x.append(
            cross_spectra(rec_blocks, lig_yz, g_tables, gl, hx, sets, box, window, row_step, q * step)
        )

    lyi = block2(cos_n, -sin_n, sin_n, cos_n)
    rzi = np.concatenate([cos_n, -sin_n], axis=0).astype(np.float32)
    inverse_tables = (lyi, rzi)
    grids = inverse_planes(back_x, inverse_tables, plane_step)
    return grids.reshape(sets, 1, part, size, size), lig_yz


def pose_statistics(
    rotation_table,
    ligand_atoms,
    cluster_center,
    pose_rotation,
    pose_translation,
    pose_owner,
    pose_member,
    size,
):
    all_centers = gather_pieces(cluster_center, "rot", 0)
    local_count = cluster_center.shape[0]
    cluster = pose_owner[:, 0] * local_count + pose_member
    rotation = jnp.take(rotation_table, pose_rotation, axis=1, mode="clip").T.reshape(-1, 3, 3)
    coords = jnp.stack(
        [
            pose_translation // (size * size),
            pose_translation // size % size,
            pose_translation % size,
        ],
        axis=1,
    )
    shifts = ((coords + size // 2) % size - size // 2).astype(F32) / size
    center = jnp.take(all_centers, cluster, axis=0, mode="clip")
    moved = jnp.einsum("pjk,ka->pja", rotation, ligand_atoms, precision=PRECISE) + shifts[:, :, None]
    spread = moved - center
    mean_square = jnp.mean(jnp.sum(spread * spread, axis=1), axis=1)
    moved_centred = moved - jnp.mean(moved, axis=2, keepdims=True)
    center_centred = center - jnp.mean(center, axis=2, keepdims=True)
    covariance = jnp.einsum("pja,pka->pjk", moved_centred, center_centred, precision=PRECISE)
    stats = jnp.concatenate([covariance.reshape(-1, 9), mean_square[:, None]], axis=1)
    return stats.T


def local(
    receptor,
    ligand_box,
    channel_weight,
    rotation_table,
    ligand_atoms,
    cluster_center,
    pose_rotation,
    pose_translation,
    pose_owner,
    pose_member,
):
    size = receptor.shape[2]
    scores, first_rows = score_grids(receptor, ligand_box, channel_weight)
    cluster_center, first_rows = lax.optimization_barrier((cluster_center, first_rows))
    pose_stats = pose_statistics(
        rotation_table,
        ligand_atoms,
        cluster_center,
        pose_rotation,
        pose_translation,
        pose_owner,
        pose_member,
        size,
    )
    return (scores, pose_stats)


def solution(mesh):
    return jax.shard_map(
        local,
        mesh=mesh,
        in_specs=(
            P(None, "slab", None, None),
            P(None, "rot", None, "slab", None, None),
            P(),
            P(),
            P(),
            P("rot", None, None),
            P(("slab", "rot")),
            P(("slab", "rot")),
            P(("slab", "rot"), None),
            P(("slab", "rot")),
        ),
        out_specs=(P(None, "rot", "slab", None, None), P(None, ("slab", "rot"))),
        check_vma=False,
    )
```

```python
import functools

import jax
import jax.numpy as jnp
import numpy as np
from jax import lax
from jax.experimental import pallas as pl
from jax.experimental.pallas import tpu as pltpu
from jax.sharding import PartitionSpec as P

PRECISE = lax.Precision.HIGHEST
SPLIT3 = lax.Precision.HIGH
TWO_PI = 6.283185307179586
F32 = jnp.float32
BF16 = jnp.bfloat16


def phase_tables(rows, cols, length):
    turns = np.outer(np.arange(rows), np.arange(cols)) % length
    phase = turns.astype(np.float64) * (TWO_PI / length)
    return (np.cos(phase), np.sin(phase))


def block2(top_left, top_right, bottom_left, bottom_right):
    top = np.concatenate([top_left, top_right], axis=1)
    bottom = np.concatenate([bottom_left, bottom_right], axis=1)
    return np.concatenate([top, bottom], axis=0).astype(np.float32)


def hi_lo(table):
    high = table.astype(BF16)
    low = (table - high.astype(F32)).astype(BF16)
    return high, low


def split_dot(a, b_high, b_low, a_left):
    a_high = a.astype(BF16)
    a_low = (a - a_high.astype(F32)).astype(BF16)
    dot = functools.partial(jnp.dot, preferred_element_type=F32)
    if a_left:
        return dot(a_high, b_high) + (dot(a_low, b_high) + dot(a_high, b_low))
    return dot(b_high, a_high) + (dot(b_high, a_low) + dot(b_low, a_high))


def forward_plane_kernel(in_ref, rz_ref, ly_ref, *out_refs):
    planes, rows, cols = in_ref.shape[1], in_ref.shape[2], in_ref.shape[3]
    size = out_refs[0].shape[3]
    rz_hi, rz_lo = hi_lo(rz_ref[...])
    ly_hi, ly_lo = hi_lo(ly_ref[...])
    joined = jnp.concatenate(
        [in_ref[0].reshape(planes * rows, cols), in_ref[1].reshape(planes * rows, cols)], axis=1
    )
    along_z = split_dot(joined, rz_hi, rz_lo, True)
    stacked = jnp.concatenate(
        [
            jnp.concatenate(
                [along_z[p * rows : (p + 1) * rows, :size], along_z[p * rows : (p + 1) * rows, size:]],
                axis=0,
            )
            for p in range(planes)
        ],
        axis=1,
    )
    along_y = split_dot(stacked, ly_hi, ly_lo, False)
    step = size // len(out_refs)
    for q, out_ref in enumerate(out_refs):
        for p in range(planes):
            cols = slice(p * size, (p + 1) * size)
            out_ref[0, p] = along_y[q * step : (q + 1) * step, cols]
            out_ref[1, p] = along_y[size + q * step : size + (q + 1) * step, cols]


def inverse_plane_kernel(*refs):
    in_refs = refs[:-3]
    ly_ref, rz_ref, out_ref = refs[-3:]
    planes = in_refs[0].shape[2]
    size = in_refs[0].shape[4]
    ly_hi, ly_lo = hi_lo(ly_ref[...])
    rz_hi, rz_lo = hi_lo(rz_ref[...])

    def plane(c, p):
        return jnp.concatenate([r[0, c, p] for r in in_refs], axis=0)

    stacked = jnp.concatenate(
        [jnp.concatenate([plane(0, p), plane(1, p)], axis=0) for p in range(planes)], axis=1
    )
    along_y = split_dot(stacked, ly_hi, ly_lo, False)
    joined = jnp.concatenate(
        [
            jnp.concatenate(
                [along_y[:size, p * size : (p + 1) * size], along_y[size:, p * size : (p + 1) * size]],
                axis=1,
            )
            for p in range(planes)
        ],
        axis=0,
    )
    out_ref[0] = split_dot(joined, rz_hi, rz_lo, True).reshape(planes, size, size)


def forward_planes(block, tables, plane_step, size, splits=1):
    planes, rows, cols = block.shape[1], block.shape[2], block.shape[3]
    table_specs = [pl.BlockSpec(t.shape, lambda i: (0, 0)) for t in tables]
    step = size // splits
    outs = pl.pallas_call(
        forward_plane_kernel,
        grid=(planes // plane_step,),
        in_specs=[pl.BlockSpec((2, plane_step, rows, cols), lambda i: (0, i, 0, 0))] + table_specs,
        out_specs=[pl.BlockSpec((2, plane_step, step, size), lambda i: (0, i, 0, 0))] * splits,
        out_shape=[jax.ShapeDtypeStruct((2, planes, step, size), F32)] * splits,
    )(block, *tables)
    return outs if splits > 1 else outs[0]


def cross_kernel(*refs, blocks, sets, box, window, part):
    rec_refs = refs[:blocks]
    lig_ref = refs[blocks]
    g_hi, g_lo = hi_lo(refs[blocks + 1][...])
    gl_hi, gl_lo = hi_lo(refs[blocks + 2][...])
    h_hi, h_lo = hi_lo(refs[blocks + 3][...])
    out_ref = refs[-1]
    rows = out_ref.shape[3]
    lanes = out_ref.shape[4]

    def gathered(ref, lo, count):
        turned = [jnp.swapaxes(ref[c, lo : lo + count], 0, 1) for c in range(2)]
        return jnp.concatenate(
            [jnp.concatenate([turned[0][r], turned[1][r]], axis=0) for r in range(rows)], axis=1
        )

    rec_in = jnp.concatenate(
        [gathered(rec_refs[b], 0, rec_refs[b].shape[1]) for b in range(blocks)], axis=0
    )
    rec = split_dot(rec_in, g_hi, g_lo, False)
    rec = jnp.concatenate([rec] * sets, axis=1)
    lig_in = jnp.concatenate([gathered(lig_ref, s * box, box) for s in range(sets)], axis=1)
    lig = split_dot(lig_in, gl_hi, gl_lo, False)
    rec_real = rec[:window]
    rec_imag = rec[window:]
    lig_real = lig[:window]
    lig_imag = lig[window:]
    prod = jnp.concatenate(
        [rec_real * lig_real + rec_imag * lig_imag, rec_imag * lig_real - rec_real * lig_imag],
        axis=0,
    )
    back = split_dot(prod, h_hi, h_lo, False)
    width = rows * lanes
    for s in range(sets):
        for c in range(2):
            pieces = jnp.stack(
                [
                    back[c * part : (c + 1) * part, s * width + r * lanes : s * width + (r + 1) * lanes]
                    for r in range(rows)
                ],
                axis=0,
            )
            out_ref[s, c] = jnp.swapaxes(pieces, 0, 1)


def cross_spectra(rec_blocks, lig_yz, g_tables, gl, hx, sets, box, window, row_step, lig_from):
    part = hx.shape[0] // 2
    size = rec_blocks[0].shape[2]
    offset = lig_from // row_step
    lanes = rec_blocks[0].shape[3]
    blocks = len(rec_blocks)
    tables = [np.concatenate(g_tables, axis=1), gl, hx]
    kernel = functools.partial(
        cross_kernel, blocks=blocks, sets=sets, box=box, window=window, part=part
    )
    return pl.pallas_call(
        kernel,
        grid=(size // row_step,),
        in_specs=[pl.BlockSpec((2, b.shape[1], row_step, lanes), lambda i: (0, 0, i, 0)) for b in rec_blocks]
        + [pl.BlockSpec((2, sets * box, row_step, lanes), lambda i: (0, 0, i + offset, 0))]
        + [pl.BlockSpec(t.shape, lambda i: (0, 0)) for t in tables],
        out_specs=pl.BlockSpec((sets, 2, part, row_step, lanes), lambda i: (0, 0, 0, i, 0)),
        out_shape=jax.ShapeDtypeStruct((sets, 2, part, size, lanes), F32),
    )(*rec_blocks, lig_yz, *tables)


def inverse_planes(spectra, tables, plane_step):
    sets, planes, size = spectra[0].shape[0], spectra[0].shape[2], spectra[0].shape[4]
    ly_spec = pl.BlockSpec((2 * size, 2 * size), lambda s, i: (0, 0))
    rz_spec = pl.BlockSpec((2 * size, size), lambda s, i: (0, 0))
    return pl.pallas_call(
        inverse_plane_kernel,
        grid=(sets, planes // plane_step),
        in_specs=[
            pl.BlockSpec((1, 2, plane_step, x.shape[3], size), lambda s, i: (s, 0, i, 0, 0))
            for x in spectra
        ]
        + [ly_spec, rz_spec],
        out_specs=pl.BlockSpec((1, plane_step, size, size), lambda s, i: (s, i, 0, 0)),
        out_shape=jax.ShapeDtypeStruct((sets, planes, size, size), F32),
    )(*spectra, *tables)


def gather_by_sum(piece, axis_name, dim):
    count = lax.axis_size(axis_name)
    index = lax.axis_index(axis_name)
    width = piece.shape[dim]
    shape = list(piece.shape)
    shape[dim] = width * count
    start = [0] * len(shape)
    start[dim] = index * width
    placed = lax.dynamic_update_slice(jnp.zeros(shape, piece.dtype), piece, start)
    return lax.psum(placed, axis_name)


def gather_pieces(piece, axis_name, dim):
    count = lax.axis_size(axis_name)
    if count & (count - 1):
        return gather_by_sum(piece, axis_name, dim)
    index = lax.axis_index(axis_name)
    held = piece
    step = 1
    while step < count:
        pairs = [(i, i ^ step) for i in range(count)]
        other = lax.ppermute(held, axis_name, perm=pairs)
        low_half = (index // step) % 2 == 0
        held = jnp.where(
            low_half,
            jnp.concatenate([held, other], axis=dim),
            jnp.concatenate([other, held], axis=dim),
        )
        step *= 2
    return held


def gather_direct(piece, axis_name, dim):
    count = lax.axis_size(axis_name)
    index = lax.axis_index(axis_name)
    held = [piece]
    for hop in range(1, count):
        pairs = [(i, (i + hop) % count) for i in range(count)]
        held.append(lax.ppermute(piece, axis_name, perm=pairs))
    stacked = jnp.stack(held, axis=0)
    order = (index - jnp.arange(count)) % count
    ordered = jnp.take(stacked, order, axis=0, mode="clip")
    ordered = jnp.moveaxis(ordered, 0, dim)
    shape = list(piece.shape)
    shape[dim] = shape[dim] * count
    return ordered.reshape(shape)


def score_grids(receptor, ligand_box, channel_weight):
    size = receptor.shape[2]
    slab_count = lax.axis_size("slab")
    part = receptor.shape[1]
    box = ligand_box.shape[4]
    sets = ligand_box.shape[0]
    extra = -(-(box - 1) // part)
    window = part * (1 + extra)
    plane_step = 8
    row_step = 16

    lead = ligand_box.shape[:4]
    dense = ligand_box.reshape(lead + (box * box,))
    full_box = gather_direct(dense, "slab", 3)
    cos_n, sin_n = phase_tables(size, size, size)
    rz = block2(cos_n, -sin_n, sin_n, cos_n)
    ly = block2(cos_n, sin_n, -sin_n, cos_n)
    splits = max(1, min(2, size // (2 * row_step)))
    own = forward_planes(receptor, (rz, ly), plane_step, size, splits)
    own = own if splits > 1 else [own]
    arrived = []
    for hop in range(1, extra + 1):
        pairs = [(i, (i - hop) % slab_count) for i in range(slab_count)]
        arrived.append([lax.ppermute(rows, "slab", perm=pairs) for rows in own])

    lig = jnp.stack(
        [full_box[:, 0, 0] * channel_weight[0], full_box[:, 0, 1] * channel_weight[1]], axis=0
    ).reshape(2, sets * box, box, box)
    cos_b, sin_b = phase_tables(box, size, size)
    rz_box = block2(cos_b, -sin_b, sin_b, cos_b)
    ly_box = block2(cos_b.T, sin_b.T, -sin_b.T, cos_b.T)
    lig_yz = forward_planes(lig, (rz_box, ly_box), plane_step, size)

    cos_w, sin_w = phase_tables(window, window, window)
    g_tables = []
    for index in range(1 + extra):
        cols = slice(index * part, (index + 1) * part)
        g_tables.append(block2(cos_w[:, cols], sin_w[:, cols], -sin_w[:, cols], cos_w[:, cols]))
    cos_xb, sin_xb = phase_tables(window, box, window)
    gl = block2(cos_xb, sin_xb, -sin_xb, cos_xb)
    cos_t, sin_t = phase_tables(part, window, window)
    scale = 1.0 / float(window * size * size)
    hx = (block2(cos_t, -sin_t, sin_t, cos_t) * scale).astype(np.float32)
    step = size // splits
    back_x = []
    for q in range(splits):
        rec_blocks = [own[q]] + [hop_rows[q] for hop_rows in arrived]
        back_x.append(
            cross_spectra(rec_blocks, lig_yz, g_tables, gl, hx, sets, box, window, row_step, q * step)
        )

    lyi = block2(cos_n, -sin_n, sin_n, cos_n)
    rzi = np.concatenate([cos_n, -sin_n], axis=0).astype(np.float32)
    inverse_tables = (lyi, rzi)
    grids = inverse_planes(back_x, inverse_tables, min(2 * plane_step, part))
    return grids.reshape(sets, 1, part, size, size), lig_yz


def pose_statistics(
    rotation_table,
    ligand_atoms,
    cluster_center,
    pose_rotation,
    pose_translation,
    pose_owner,
    pose_member,
    size,
):
    all_centers = gather_pieces(cluster_center, "rot", 0)
    local_count = cluster_center.shape[0]
    cluster = pose_owner[:, 0] * local_count + pose_member
    rotation = jnp.take(rotation_table, pose_rotation, axis=1, mode="clip").T.reshape(-1, 3, 3)
    coords = jnp.stack(
        [
            pose_translation // (size * size),
            pose_translation // size % size,
            pose_translation % size,
        ],
        axis=1,
    )
    shifts = ((coords + size // 2) % size - size // 2).astype(F32) / size
    center = jnp.take(all_centers, cluster, axis=0, mode="clip")
    moved = jnp.einsum("pjk,ka->pja", rotation, ligand_atoms, precision=PRECISE) + shifts[:, :, None]
    spread = moved - center
    mean_square = jnp.mean(jnp.sum(spread * spread, axis=1), axis=1)
    moved_centred = moved - jnp.mean(moved, axis=2, keepdims=True)
    center_centred = center - jnp.mean(center, axis=2, keepdims=True)
    covariance = jnp.einsum("pja,pka->pjk", moved_centred, center_centred, precision=PRECISE)
    stats = jnp.concatenate([covariance.reshape(-1, 9), mean_square[:, None]], axis=1)
    return stats.T


def local(
    receptor,
    ligand_box,
    channel_weight,
    rotation_table,
    ligand_atoms,
    cluster_center,
    pose_rotation,
    pose_translation,
    pose_owner,
    pose_member,
):
    size = receptor.shape[2]
    scores, first_rows = score_grids(receptor, ligand_box, channel_weight)
    cluster_center, first_rows = lax.optimization_barrier((cluster_center, first_rows))
    pose_stats = pose_statistics(
        rotation_table,
        ligand_atoms,
        cluster_center,
        pose_rotation,
        pose_translation,
        pose_owner,
        pose_member,
        size,
    )
    return (scores, pose_stats)


def solution(mesh):
    return jax.shard_map(
        local,
        mesh=mesh,
        in_specs=(
            P(None, "slab", None, None),
            P(None, "rot", None, "slab", None, None),
            P(),
            P(),
            P(),
            P("rot", None, None),
            P(("slab", "rot")),
            P(("slab", "rot")),
            P(("slab", "rot"), None),
            P(("slab", "rot")),
        ),
        out_specs=(P(None, "rot", "slab", None, None), P(None, ("slab", "rot"))),
        check_vma=False,
    )
```

```python
import functools

import jax
import jax.numpy as jnp
import numpy as np
from jax import lax
from jax.experimental import pallas as pl
from jax.experimental.pallas import tpu as pltpu
from jax.sharding import PartitionSpec as P

PRECISE = lax.Precision.HIGHEST
SPLIT3 = lax.Precision.HIGH
TWO_PI = 6.283185307179586
F32 = jnp.float32
BF16 = jnp.bfloat16


def phase_tables(rows, cols, length):
    turns = np.outer(np.arange(rows), np.arange(cols)) % length
    phase = turns.astype(np.float64) * (TWO_PI / length)
    return (np.cos(phase), np.sin(phase))


def block2(top_left, top_right, bottom_left, bottom_right):
    top = np.concatenate([top_left, top_right], axis=1)
    bottom = np.concatenate([bottom_left, bottom_right], axis=1)
    return np.concatenate([top, bottom], axis=0).astype(np.float32)


def hi_lo(table):
    high = table.astype(BF16)
    low = (table - high.astype(F32)).astype(BF16)
    return high, low


def split_dot(a, b_high, b_low, a_left):
    a_high = a.astype(BF16)
    a_low = (a - a_high.astype(F32)).astype(BF16)
    dot = functools.partial(jnp.dot, preferred_element_type=F32)
    if a_left:
        return dot(a_high, b_high) + (dot(a_low, b_high) + dot(a_high, b_low))
    return dot(b_high, a_high) + (dot(b_high, a_low) + dot(b_low, a_high))


def forward_plane_kernel(in_ref, rz_ref, ly_ref, *out_refs):
    planes, rows, cols = in_ref.shape[1], in_ref.shape[2], in_ref.shape[3]
    size = out_refs[0].shape[3]
    rz_hi, rz_lo = hi_lo(rz_ref[...])
    ly_hi, ly_lo = hi_lo(ly_ref[...])
    joined = jnp.concatenate(
        [in_ref[0].reshape(planes * rows, cols), in_ref[1].reshape(planes * rows, cols)], axis=1
    )
    along_z = split_dot(joined, rz_hi, rz_lo, True)
    stacked = jnp.concatenate(
        [
            jnp.concatenate(
                [along_z[p * rows : (p + 1) * rows, :size], along_z[p * rows : (p + 1) * rows, size:]],
                axis=0,
            )
            for p in range(planes)
        ],
        axis=1,
    )
    along_y = split_dot(stacked, ly_hi, ly_lo, False)
    step = size // len(out_refs)
    for q, out_ref in enumerate(out_refs):
        for p in range(planes):
            cols = slice(p * size, (p + 1) * size)
            out_ref[0, p] = along_y[q * step : (q + 1) * step, cols]
            out_ref[1, p] = along_y[size + q * step : size + (q + 1) * step, cols]


def inverse_plane_kernel(*refs):
    in_refs = refs[:-3]
    ly_ref, rz_ref, out_ref = refs[-3:]
    planes = in_refs[0].shape[2]
    size = in_refs[0].shape[4]
    ly_hi, ly_lo = hi_lo(ly_ref[...])
    rz_hi, rz_lo = hi_lo(rz_ref[...])

    def plane(c, p):
        return jnp.concatenate([r[0, c, p] for r in in_refs], axis=0)

    stacked = jnp.concatenate(
        [jnp.concatenate([plane(0, p), plane(1, p)], axis=0) for p in range(planes)], axis=1
    )
    along_y = split_dot(stacked, ly_hi, ly_lo, False)
    joined = jnp.concatenate(
        [
            jnp.concatenate(
                [along_y[:size, p * size : (p + 1) * size], along_y[size:, p * size : (p + 1) * size]],
                axis=1,
            )
            for p in range(planes)
        ],
        axis=0,
    )
    out_ref[0] = split_dot(joined, rz_hi, rz_lo, True).reshape(planes, size, size)


def forward_planes(block, tables, plane_step, size, splits=1):
    planes, rows, cols = block.shape[1], block.shape[2], block.shape[3]
    table_specs = [pl.BlockSpec(t.shape, lambda i: (0, 0)) for t in tables]
    step = size // splits
    outs = pl.pallas_call(
        forward_plane_kernel,
        grid=(planes // plane_step,),
        in_specs=[pl.BlockSpec((2, plane_step, rows, cols), lambda i: (0, i, 0, 0))] + table_specs,
        out_specs=[pl.BlockSpec((2, plane_step, step, size), lambda i: (0, i, 0, 0))] * splits,
        out_shape=[jax.ShapeDtypeStruct((2, planes, step, size), F32)] * splits,
    )(block, *tables)
    return outs if splits > 1 else outs[0]


def cross_kernel(*refs, blocks, sets, box, window, part):
    rec_refs = refs[:blocks]
    lig_ref = refs[blocks]
    g_hi, g_lo = hi_lo(refs[blocks + 1][...])
    gl_hi, gl_lo = hi_lo(refs[blocks + 2][...])
    h_hi, h_lo = hi_lo(refs[blocks + 3][...])
    out_ref = refs[-1]
    rows = out_ref.shape[3]
    lanes = out_ref.shape[4]

    def gathered(ref, lo, count):
        turned = [jnp.swapaxes(ref[c, lo : lo + count], 0, 1) for c in range(2)]
        return jnp.concatenate(
            [jnp.concatenate([turned[0][r], turned[1][r]], axis=0) for r in range(rows)], axis=1
        )

    rec_in = jnp.concatenate(
        [gathered(rec_refs[b], 0, rec_refs[b].shape[1]) for b in range(blocks)], axis=0
    )
    rec = split_dot(rec_in, g_hi, g_lo, False)
    rec = jnp.concatenate([rec] * sets, axis=1)
    lig_in = jnp.concatenate([gathered(lig_ref, s * box, box) for s in range(sets)], axis=1)
    lig = split_dot(lig_in, gl_hi, gl_lo, False)
    rec_real = rec[:window]
    rec_imag = rec[window:]
    lig_real = lig[:window]
    lig_imag = lig[window:]
    prod = jnp.concatenate(
        [rec_real * lig_real + rec_imag * lig_imag, rec_imag * lig_real - rec_real * lig_imag],
        axis=0,
    )
    back = split_dot(prod, h_hi, h_lo, False)
    width = rows * lanes
    for s in range(sets):
        for c in range(2):
            pieces = jnp.stack(
                [
                    back[c * part : (c + 1) * part, s * width + r * lanes : s * width + (r + 1) * lanes]
                    for r in range(rows)
                ],
                axis=0,
            )
            out_ref[s, c] = jnp.swapaxes(pieces, 0, 1)


def cross_spectra(rec_blocks, lig_yz, g_tables, gl, hx, sets, box, window, row_step, lig_from):
    part = hx.shape[0] // 2
    size = rec_blocks[0].shape[2]
    offset = lig_from // row_step
    lanes = rec_blocks[0].shape[3]
    blocks = len(rec_blocks)
    tables = [np.concatenate(g_tables, axis=1), gl, hx]
    kernel = functools.partial(
        cross_kernel, blocks=blocks, sets=sets, box=box, window=window, part=part
    )
    return pl.pallas_call(
        kernel,
        grid=(size // row_step,),
        in_specs=[pl.BlockSpec((2, b.shape[1], row_step, lanes), lambda i: (0, 0, i, 0)) for b in rec_blocks]
        + [pl.BlockSpec((2, sets * box, row_step, lanes), lambda i: (0, 0, i + offset, 0))]
        + [pl.BlockSpec(t.shape, lambda i: (0, 0)) for t in tables],
        out_specs=pl.BlockSpec((sets, 2, part, row_step, lanes), lambda i: (0, 0, 0, i, 0)),
        out_shape=jax.ShapeDtypeStruct((sets, 2, part, size, lanes), F32),
    )(*rec_blocks, lig_yz, *tables)


def inverse_planes(spectra, tables, plane_step):
    sets, planes, size = spectra[0].shape[0], spectra[0].shape[2], spectra[0].shape[4]
    ly_spec = pl.BlockSpec((2 * size, 2 * size), lambda s, i: (0, 0))
    rz_spec = pl.BlockSpec((2 * size, size), lambda s, i: (0, 0))
    return pl.pallas_call(
        inverse_plane_kernel,
        grid=(sets, planes // plane_step),
        in_specs=[
            pl.BlockSpec((1, 2, plane_step, x.shape[3], size), lambda s, i: (s, 0, i, 0, 0))
            for x in spectra
        ]
        + [ly_spec, rz_spec],
        out_specs=pl.BlockSpec((1, plane_step, size, size), lambda s, i: (s, i, 0, 0)),
        out_shape=jax.ShapeDtypeStruct((sets, planes, size, size), F32),
    )(*spectra, *tables)


def gather_by_sum(piece, axis_name, dim):
    count = lax.axis_size(axis_name)
    index = lax.axis_index(axis_name)
    width = piece.shape[dim]
    shape = list(piece.shape)
    shape[dim] = width * count
    start = [0] * len(shape)
    start[dim] = index * width
    placed = lax.dynamic_update_slice(jnp.zeros(shape, piece.dtype), piece, start)
    return lax.psum(placed, axis_name)


def gather_pieces(piece, axis_name, dim):
    count = lax.axis_size(axis_name)
    if count & (count - 1):
        return gather_by_sum(piece, axis_name, dim)
    index = lax.axis_index(axis_name)
    held = piece
    step = 1
    while step < count:
        pairs = [(i, i ^ step) for i in range(count)]
        other = lax.ppermute(held, axis_name, perm=pairs)
        low_half = (index // step) % 2 == 0
        held = jnp.where(
            low_half,
            jnp.concatenate([held, other], axis=dim),
            jnp.concatenate([other, held], axis=dim),
        )
        step *= 2
    return held


def gather_direct(piece, axis_name, dim):
    count = lax.axis_size(axis_name)
    index = lax.axis_index(axis_name)
    held = [piece]
    for hop in range(1, count):
        pairs = [(i, (i + hop) % count) for i in range(count)]
        held.append(lax.ppermute(piece, axis_name, perm=pairs))
    stacked = jnp.stack(held, axis=0)
    order = (index - jnp.arange(count)) % count
    ordered = jnp.take(stacked, order, axis=0, mode="clip")
    ordered = jnp.moveaxis(ordered, 0, dim)
    shape = list(piece.shape)
    shape[dim] = shape[dim] * count
    return ordered.reshape(shape)


def score_grids(receptor, ligand_box, channel_weight):
    size = receptor.shape[2]
    slab_count = lax.axis_size("slab")
    part = receptor.shape[1]
    box = ligand_box.shape[4]
    sets = ligand_box.shape[0]
    extra = -(-(box - 1) // part)
    window = part * (1 + extra)
    plane_step = 8
    row_step = 16

    lead = ligand_box.shape[:4]
    dense = ligand_box.reshape(lead + (box * box,))
    full_box = gather_direct(dense, "slab", 3)
    cos_n, sin_n = phase_tables(size, size, size)
    rz = block2(cos_n, -sin_n, sin_n, cos_n)
    ly = block2(cos_n, sin_n, -sin_n, cos_n)
    splits = max(1, min(2, size // (2 * row_step)))
    own = forward_planes(receptor, (rz, ly), plane_step, size, splits)
    own = own if splits > 1 else [own]
    arrived = []
    for hop in range(1, extra + 1):
        pairs = [(i, (i - hop) % slab_count) for i in range(slab_count)]
        arrived.append([lax.ppermute(rows, "slab", perm=pairs) for rows in own])

    lig = jnp.stack(
        [full_box[:, 0, 0] * channel_weight[0], full_box[:, 0, 1] * channel_weight[1]], axis=0
    ).reshape(2, sets * box, box, box)
    cos_b, sin_b = phase_tables(box, size, size)
    rz_box = block2(cos_b, -sin_b, sin_b, cos_b)
    ly_box = block2(cos_b.T, sin_b.T, -sin_b.T, cos_b.T)
    lig_yz = forward_planes(lig, (rz_box, ly_box), 2 * plane_step, size)

    cos_w, sin_w = phase_tables(window, window, window)
    g_tables = []
    for index in range(1 + extra):
        cols = slice(index * part, (index + 1) * part)
        g_tables.append(block2(cos_w[:, cols], sin_w[:, cols], -sin_w[:, cols], cos_w[:, cols]))
    cos_xb, sin_xb = phase_tables(window, box, window)
    gl = block2(cos_xb, sin_xb, -sin_xb, cos_xb)
    cos_t, sin_t = phase_tables(part, window, window)
    scale = 1.0 / float(window * size * size)
    hx = (block2(cos_t, -sin_t, sin_t, cos_t) * scale).astype(np.float32)
    step = size // splits
    back_x = []
    for q in range(splits):
        rec_blocks = [own[q]] + [hop_rows[q] for hop_rows in arrived]
        back_x.append(
            cross_spectra(rec_blocks, lig_yz, g_tables, gl, hx, sets, box, window, row_step, q * step)
        )

    lyi = block2(cos_n, -sin_n, sin_n, cos_n)
    rzi = np.concatenate([cos_n, -sin_n], axis=0).astype(np.float32)
    inverse_tables = (lyi, rzi)
    grids = inverse_planes(back_x, inverse_tables, min(2 * plane_step, part))
    return grids.reshape(sets, 1, part, size, size), lig_yz


def pose_statistics(
    rotation_table,
    ligand_atoms,
    cluster_center,
    pose_rotation,
    pose_translation,
    pose_owner,
    pose_member,
    size,
):
    all_centers = gather_pieces(cluster_center, "rot", 0)
    local_count = cluster_center.shape[0]
    cluster = pose_owner[:, 0] * local_count + pose_member
    rotation = jnp.take(rotation_table, pose_rotation, axis=1, mode="clip").T.reshape(-1, 3, 3)
    coords = jnp.stack(
        [
            pose_translation // (size * size),
            pose_translation // size % size,
            pose_translation % size,
        ],
        axis=1,
    )
    shifts = ((coords + size // 2) % size - size // 2).astype(F32) / size
    center = jnp.take(all_centers, cluster, axis=0, mode="clip")
    moved = jnp.einsum("pjk,ka->pja", rotation, ligand_atoms, precision=PRECISE) + shifts[:, :, None]
    spread = moved - center
    mean_square = jnp.mean(jnp.sum(spread * spread, axis=1), axis=1)
    moved_centred = moved - jnp.mean(moved, axis=2, keepdims=True)
    center_centred = center - jnp.mean(center, axis=2, keepdims=True)
    covariance = jnp.einsum("pja,pka->pjk", moved_centred, center_centred, precision=PRECISE)
    stats = jnp.concatenate([covariance.reshape(-1, 9), mean_square[:, None]], axis=1)
    return stats.T


def local(
    receptor,
    ligand_box,
    channel_weight,
    rotation_table,
    ligand_atoms,
    cluster_center,
    pose_rotation,
    pose_translation,
    pose_owner,
    pose_member,
):
    size = receptor.shape[2]
    scores, first_rows = score_grids(receptor, ligand_box, channel_weight)
    cluster_center, first_rows = lax.optimization_barrier((cluster_center, first_rows))
    pose_stats = pose_statistics(
        rotation_table,
        ligand_atoms,
        cluster_center,
        pose_rotation,
        pose_translation,
        pose_owner,
        pose_member,
        size,
    )
    return (scores, pose_stats)


def solution(mesh):
    return jax.shard_map(
        local,
        mesh=mesh,
        in_specs=(
            P(None, "slab", None, None),
            P(None, "rot", None, "slab", None, None),
            P(),
            P(),
            P(),
            P("rot", None, None),
            P(("slab", "rot")),
            P(("slab", "rot")),
            P(("slab", "rot"), None),
            P(("slab", "rot")),
        ),
        out_specs=(P(None, "rot", "slab", None, None), P(None, ("slab", "rot"))),
        check_vma=False,
    )
```

```python
import functools

import jax
import jax.numpy as jnp
import numpy as np
from jax import lax
from jax.experimental import pallas as pl
from jax.experimental.pallas import tpu as pltpu
from jax.sharding import PartitionSpec as P

PRECISE = lax.Precision.HIGHEST
SPLIT3 = lax.Precision.HIGH
TWO_PI = 6.283185307179586
F32 = jnp.float32
BF16 = jnp.bfloat16


def phase_tables(rows, cols, length):
    turns = np.outer(np.arange(rows), np.arange(cols)) % length
    phase = turns.astype(np.float64) * (TWO_PI / length)
    return (np.cos(phase), np.sin(phase))


def block2(top_left, top_right, bottom_left, bottom_right):
    top = np.concatenate([top_left, top_right], axis=1)
    bottom = np.concatenate([bottom_left, bottom_right], axis=1)
    return np.concatenate([top, bottom], axis=0).astype(np.float32)


def hi_lo(table):
    high = table.astype(BF16)
    low = (table - high.astype(F32)).astype(BF16)
    return high, low


def split_dot(a, b_high, b_low, a_left):
    a_high = a.astype(BF16)
    a_low = (a - a_high.astype(F32)).astype(BF16)
    dot = functools.partial(jnp.dot, preferred_element_type=F32)
    if a_left:
        return dot(a_high, b_high) + (dot(a_low, b_high) + dot(a_high, b_low))
    return dot(b_high, a_high) + (dot(b_high, a_low) + dot(b_low, a_high))


def forward_plane_kernel(in_ref, rz_ref, ly_ref, *out_refs):
    planes, rows, cols = in_ref.shape[1], in_ref.shape[2], in_ref.shape[3]
    size = out_refs[0].shape[3]
    rz_hi, rz_lo = hi_lo(rz_ref[...])
    ly_hi, ly_lo = hi_lo(ly_ref[...])
    joined = jnp.concatenate(
        [in_ref[0].reshape(planes * rows, cols), in_ref[1].reshape(planes * rows, cols)], axis=1
    )
    along_z = split_dot(joined, rz_hi, rz_lo, True)
    stacked = jnp.concatenate(
        [
            jnp.concatenate(
                [along_z[p * rows : (p + 1) * rows, :size], along_z[p * rows : (p + 1) * rows, size:]],
                axis=0,
            )
            for p in range(planes)
        ],
        axis=1,
    )
    along_y = split_dot(stacked, ly_hi, ly_lo, False)
    step = size // len(out_refs)
    for q, out_ref in enumerate(out_refs):
        for p in range(planes):
            cols = slice(p * size, (p + 1) * size)
            out_ref[0, p] = along_y[q * step : (q + 1) * step, cols]
            out_ref[1, p] = along_y[size + q * step : size + (q + 1) * step, cols]


def inverse_plane_kernel(*refs):
    in_refs = refs[:-3]
    ly_ref, rz_ref, out_ref = refs[-3:]
    planes = in_refs[0].shape[2]
    size = in_refs[0].shape[4]
    ly_hi, ly_lo = hi_lo(ly_ref[...])
    rz_hi, rz_lo = hi_lo(rz_ref[...])

    def plane(c, p):
        return jnp.concatenate([r[0, c, p] for r in in_refs], axis=0)

    stacked = jnp.concatenate(
        [jnp.concatenate([plane(0, p), plane(1, p)], axis=0) for p in range(planes)], axis=1
    )
    along_y = split_dot(stacked, ly_hi, ly_lo, False)
    joined = jnp.concatenate(
        [
            jnp.concatenate(
                [along_y[:size, p * size : (p + 1) * size], along_y[size:, p * size : (p + 1) * size]],
                axis=1,
            )
            for p in range(planes)
        ],
        axis=0,
    )
    out_ref[0] = split_dot(joined, rz_hi, rz_lo, True).reshape(planes, size, size)


def forward_planes(block, tables, plane_step, size, splits=1):
    planes, rows, cols = block.shape[1], block.shape[2], block.shape[3]
    table_specs = [pl.BlockSpec(t.shape, lambda i: (0, 0)) for t in tables]
    step = size // splits
    outs = pl.pallas_call(
        forward_plane_kernel,
        grid=(planes // plane_step,),
        in_specs=[pl.BlockSpec((2, plane_step, rows, cols), lambda i: (0, i, 0, 0))] + table_specs,
        out_specs=[pl.BlockSpec((2, plane_step, step, size), lambda i: (0, i, 0, 0))] * splits,
        out_shape=[jax.ShapeDtypeStruct((2, planes, step, size), F32)] * splits,
    )(block, *tables)
    return outs if splits > 1 else outs[0]


def cross_kernel(*refs, blocks, sets, box, window, part):
    rec_refs = refs[:blocks]
    lig_ref = refs[blocks]
    g_hi, g_lo = hi_lo(refs[blocks + 1][...])
    gl_hi, gl_lo = hi_lo(refs[blocks + 2][...])
    h_hi, h_lo = hi_lo(refs[blocks + 3][...])
    out_ref = refs[-1]
    rows = out_ref.shape[3]
    lanes = out_ref.shape[4]

    def gathered(ref, lo, count):
        turned = [jnp.swapaxes(ref[c, lo : lo + count], 0, 1) for c in range(2)]
        return jnp.concatenate(
            [jnp.concatenate([turned[0][r], turned[1][r]], axis=0) for r in range(rows)], axis=1
        )

    rec_in = jnp.concatenate(
        [gathered(rec_refs[b], 0, rec_refs[b].shape[1]) for b in range(blocks)], axis=0
    )
    rec = split_dot(rec_in, g_hi, g_lo, False)
    rec = jnp.concatenate([rec] * sets, axis=1)
    lig_in = jnp.concatenate([gathered(lig_ref, s * box, box) for s in range(sets)], axis=1)
    lig = split_dot(lig_in, gl_hi, gl_lo, False)
    rec_real = rec[:window]
    rec_imag = rec[window:]
    lig_real = lig[:window]
    lig_imag = lig[window:]
    prod = jnp.concatenate(
        [rec_real * lig_real + rec_imag * lig_imag, rec_imag * lig_real - rec_real * lig_imag],
        axis=0,
    )
    back = split_dot(prod, h_hi, h_lo, False)
    width = rows * lanes
    for s in range(sets):
        for c in range(2):
            pieces = jnp.stack(
                [
                    back[c * part : (c + 1) * part, s * width + r * lanes : s * width + (r + 1) * lanes]
                    for r in range(rows)
                ],
                axis=0,
            )
            out_ref[s, c] = jnp.swapaxes(pieces, 0, 1)


def cross_spectra(rec_blocks, lig_yz, g_tables, gl, hx, sets, box, window, row_step, lig_from):
    part = hx.shape[0] // 2
    size = rec_blocks[0].shape[2]
    offset = lig_from // row_step
    lanes = rec_blocks[0].shape[3]
    blocks = len(rec_blocks)
    tables = [np.concatenate(g_tables, axis=1), gl, hx]
    kernel = functools.partial(
        cross_kernel, blocks=blocks, sets=sets, box=box, window=window, part=part
    )
    return pl.pallas_call(
        kernel,
        grid=(size // row_step,),
        in_specs=[pl.BlockSpec((2, b.shape[1], row_step, lanes), lambda i: (0, 0, i, 0)) for b in rec_blocks]
        + [pl.BlockSpec((2, sets * box, row_step, lanes), lambda i: (0, 0, i + offset, 0))]
        + [pl.BlockSpec(t.shape, lambda i: (0, 0)) for t in tables],
        out_specs=pl.BlockSpec((sets, 2, part, row_step, lanes), lambda i: (0, 0, 0, i, 0)),
        out_shape=jax.ShapeDtypeStruct((sets, 2, part, size, lanes), F32),
    )(*rec_blocks, lig_yz, *tables)


def inverse_planes(spectra, tables, plane_step):
    sets, planes, size = spectra[0].shape[0], spectra[0].shape[2], spectra[0].shape[4]
    ly_spec = pl.BlockSpec((2 * size, 2 * size), lambda s, i: (0, 0))
    rz_spec = pl.BlockSpec((2 * size, size), lambda s, i: (0, 0))
    return pl.pallas_call(
        inverse_plane_kernel,
        grid=(sets, planes // plane_step),
        in_specs=[
            pl.BlockSpec((1, 2, plane_step, x.shape[3], size), lambda s, i: (s, 0, i, 0, 0))
            for x in spectra
        ]
        + [ly_spec, rz_spec],
        out_specs=pl.BlockSpec((1, plane_step, size, size), lambda s, i: (s, i, 0, 0)),
        out_shape=jax.ShapeDtypeStruct((sets, planes, size, size), F32),
    )(*spectra, *tables)


def gather_by_sum(piece, axis_name, dim):
    count = lax.axis_size(axis_name)
    index = lax.axis_index(axis_name)
    width = piece.shape[dim]
    shape = list(piece.shape)
    shape[dim] = width * count
    start = [0] * len(shape)
    start[dim] = index * width
    placed = lax.dynamic_update_slice(jnp.zeros(shape, piece.dtype), piece, start)
    return lax.psum(placed, axis_name)


def gather_pieces(piece, axis_name, dim):
    count = lax.axis_size(axis_name)
    if count & (count - 1):
        return gather_by_sum(piece, axis_name, dim)
    index = lax.axis_index(axis_name)
    held = piece
    step = 1
    while step < count:
        pairs = [(i, i ^ step) for i in range(count)]
        other = lax.ppermute(held, axis_name, perm=pairs)
        low_half = (index // step) % 2 == 0
        held = jnp.where(
            low_half,
            jnp.concatenate([held, other], axis=dim),
            jnp.concatenate([other, held], axis=dim),
        )
        step *= 2
    return held


def gather_direct(piece, axis_name, dim):
    count = lax.axis_size(axis_name)
    index = lax.axis_index(axis_name)
    held = [piece]
    for hop in range(1, count):
        pairs = [(i, (i + hop) % count) for i in range(count)]
        held.append(lax.ppermute(piece, axis_name, perm=pairs))
    stacked = jnp.stack(held, axis=0)
    order = (index - jnp.arange(count)) % count
    ordered = jnp.take(stacked, order, axis=0, mode="clip")
    ordered = jnp.moveaxis(ordered, 0, dim)
    shape = list(piece.shape)
    shape[dim] = shape[dim] * count
    return ordered.reshape(shape)


def score_grids(receptor, ligand_box, channel_weight):
    size = receptor.shape[2]
    slab_count = lax.axis_size("slab")
    part = receptor.shape[1]
    box = ligand_box.shape[4]
    sets = ligand_box.shape[0]
    extra = -(-(box - 1) // part)
    window = part * (1 + extra)
    plane_step = 8
    row_step = 16

    lead = ligand_box.shape[:4]
    dense = ligand_box.reshape(lead + (box * box,))
    full_box = gather_direct(dense, "slab", 3)
    cos_n, sin_n = phase_tables(size, size, size)
    rz = block2(cos_n, -sin_n, sin_n, cos_n)
    ly = block2(cos_n, sin_n, -sin_n, cos_n)
    splits = max(1, min(2, size // (2 * row_step)))
    own = forward_planes(receptor, (rz, ly), plane_step, size, splits)
    own = own if splits > 1 else [own]
    arrived = []
    for hop in range(1, extra + 1):
        pairs = [(i, (i - hop) % slab_count) for i in range(slab_count)]
        arrived.append([lax.ppermute(rows, "slab", perm=pairs) for rows in own])

    lig = jnp.stack(
        [full_box[:, 0, 0] * channel_weight[0], full_box[:, 0, 1] * channel_weight[1]], axis=0
    ).reshape(2, sets * box, box, box)
    cos_b, sin_b = phase_tables(box, size, size)
    rz_box = block2(cos_b, -sin_b, sin_b, cos_b)
    ly_box = block2(cos_b.T, sin_b.T, -sin_b.T, cos_b.T)
    lig_yz = forward_planes(lig, (rz_box, ly_box), 2 * plane_step, size)

    cos_w, sin_w = phase_tables(window, window, window)
    g_tables = []
    for index in range(1 + extra):
        cols = slice(index * part, (index + 1) * part)
        g_tables.append(block2(cos_w[:, cols], sin_w[:, cols], -sin_w[:, cols], cos_w[:, cols]))
    cos_xb, sin_xb = phase_tables(window, box, window)
    gl = block2(cos_xb, sin_xb, -sin_xb, cos_xb)
    cos_t, sin_t = phase_tables(part, window, window)
    scale = 1.0 / float(window * size * size)
    hx = (block2(cos_t, -sin_t, sin_t, cos_t) * scale).astype(np.float32)
    step = size // splits
    back_x = []
    for q in range(splits):
        rec_blocks = [own[q]] + [hop_rows[q] for hop_rows in arrived]
        back_x.append(
            cross_spectra(rec_blocks, lig_yz, g_tables, gl, hx, sets, box, window, row_step, q * step)
        )

    lyi = block2(cos_n, -sin_n, sin_n, cos_n)
    rzi = np.concatenate([cos_n, -sin_n], axis=0).astype(np.float32)
    inverse_tables = (lyi, rzi)
    grids = inverse_planes(back_x, inverse_tables, min(2 * plane_step, part))
    return grids.reshape(sets, 1, part, size, size), lig_yz


def pose_statistics(
    rotation_table,
    ligand_atoms,
    cluster_center,
    pose_rotation,
    pose_translation,
    pose_owner,
    pose_member,
    size,
):
    count = lax.axis_size("rot")
    copies = jnp.broadcast_to(cluster_center[None], (count,) + cluster_center.shape)
    copies = copies.reshape((count * cluster_center.shape[0],) + cluster_center.shape[1:])
    all_centers = lax.all_to_all(copies, "rot", split_axis=0, concat_axis=0, tiled=True)
    local_count = cluster_center.shape[0]
    cluster = pose_owner[:, 0] * local_count + pose_member
    rotation = jnp.take(rotation_table, pose_rotation, axis=1, mode="clip").T.reshape(-1, 3, 3)
    coords = jnp.stack(
        [
            pose_translation // (size * size),
            pose_translation // size % size,
            pose_translation % size,
        ],
        axis=1,
    )
    shifts = ((coords + size // 2) % size - size // 2).astype(F32) / size
    center = jnp.take(all_centers, cluster, axis=0, mode="clip")
    moved = jnp.einsum("pjk,ka->pja", rotation, ligand_atoms, precision=PRECISE) + shifts[:, :, None]
    spread = moved - center
    mean_square = jnp.mean(jnp.sum(spread * spread, axis=1), axis=1)
    moved_centred = moved - jnp.mean(moved, axis=2, keepdims=True)
    center_centred = center - jnp.mean(center, axis=2, keepdims=True)
    covariance = jnp.einsum("pja,pka->pjk", moved_centred, center_centred, precision=PRECISE)
    stats = jnp.concatenate([covariance.reshape(-1, 9), mean_square[:, None]], axis=1)
    return stats.T


def local(
    receptor,
    ligand_box,
    channel_weight,
    rotation_table,
    ligand_atoms,
    cluster_center,
    pose_rotation,
    pose_translation,
    pose_owner,
    pose_member,
):
    size = receptor.shape[2]
    scores, first_rows = score_grids(receptor, ligand_box, channel_weight)
    cluster_center, first_rows = lax.optimization_barrier((cluster_center, first_rows))
    pose_stats = pose_statistics(
        rotation_table,
        ligand_atoms,
        cluster_center,
        pose_rotation,
        pose_translation,
        pose_owner,
        pose_member,
        size,
    )
    return (scores, pose_stats)


def solution(mesh):
    return jax.shard_map(
        local,
        mesh=mesh,
        in_specs=(
            P(None, "slab", None, None),
            P(None, "rot", None, "slab", None, None),
            P(),
            P(),
            P(),
            P("rot", None, None),
            P(("slab", "rot")),
            P(("slab", "rot")),
            P(("slab", "rot"), None),
            P(("slab", "rot")),
        ),
        out_specs=(P(None, "rot", "slab", None, None), P(None, ("slab", "rot"))),
        check_vma=False,
    )
```

```python
import functools

import jax
import jax.numpy as jnp
import ml_dtypes
import numpy as np
from jax import lax
from jax.experimental import pallas as pl
from jax.experimental.pallas import tpu as pltpu
from jax.sharding import PartitionSpec as P

PRECISE = lax.Precision.HIGHEST
SPLIT3 = lax.Precision.HIGH
TWO_PI = 6.283185307179586
F32 = jnp.float32
BF16 = jnp.bfloat16


def phase_tables(rows, cols, length):
    turns = np.outer(np.arange(rows), np.arange(cols)) % length
    phase = turns.astype(np.float64) * (TWO_PI / length)
    return (np.cos(phase), np.sin(phase))


def block2(top_left, top_right, bottom_left, bottom_right):
    top = np.concatenate([top_left, top_right], axis=1)
    bottom = np.concatenate([bottom_left, bottom_right], axis=1)
    return np.concatenate([top, bottom], axis=0).astype(np.float32)


def hi_lo(table):
    high = table.astype(BF16)
    low = (table - high.astype(F32)).astype(BF16)
    return high, low


def table_parts(table):
    high = table.astype(ml_dtypes.bfloat16)
    low = (table - high.astype(np.float32)).astype(ml_dtypes.bfloat16)
    return [high, low]


def split_dot(a, b_high, b_low, a_left):
    a_high = a.astype(BF16)
    a_low = (a - a_high.astype(F32)).astype(BF16)
    dot = functools.partial(jnp.dot, preferred_element_type=F32)
    if a_left:
        return dot(a_high, b_high) + (dot(a_low, b_high) + dot(a_high, b_low))
    return dot(b_high, a_high) + (dot(b_high, a_low) + dot(b_low, a_high))


def forward_plane_kernel(in_ref, rz_hi_ref, rz_lo_ref, ly_hi_ref, ly_lo_ref, *out_refs):
    planes, rows, cols = in_ref.shape[1], in_ref.shape[2], in_ref.shape[3]
    size = out_refs[0].shape[3]
    rz_hi, rz_lo = rz_hi_ref[...], rz_lo_ref[...]
    ly_hi, ly_lo = ly_hi_ref[...], ly_lo_ref[...]
    joined = jnp.concatenate(
        [in_ref[0].reshape(planes * rows, cols), in_ref[1].reshape(planes * rows, cols)], axis=1
    )
    along_z = split_dot(joined, rz_hi, rz_lo, True)
    stacked = jnp.concatenate(
        [
            jnp.concatenate(
                [along_z[p * rows : (p + 1) * rows, :size], along_z[p * rows : (p + 1) * rows, size:]],
                axis=0,
            )
            for p in range(planes)
        ],
        axis=1,
    )
    along_y = split_dot(stacked, ly_hi, ly_lo, False)
    step = size // len(out_refs)
    for q, out_ref in enumerate(out_refs):
        for p in range(planes):
            cols = slice(p * size, (p + 1) * size)
            out_ref[0, p] = along_y[q * step : (q + 1) * step, cols]
            out_ref[1, p] = along_y[size + q * step : size + (q + 1) * step, cols]


def inverse_plane_kernel(*refs):
    in_refs = refs[:-5]
    ly_hi_ref, ly_lo_ref, rz_hi_ref, rz_lo_ref, out_ref = refs[-5:]
    planes = in_refs[0].shape[2]
    size = in_refs[0].shape[4]
    ly_hi, ly_lo = ly_hi_ref[...], ly_lo_ref[...]
    rz_hi, rz_lo = rz_hi_ref[...], rz_lo_ref[...]

    def plane(c, p):
        return jnp.concatenate([r[0, c, p] for r in in_refs], axis=0)

    stacked = jnp.concatenate(
        [jnp.concatenate([plane(0, p), plane(1, p)], axis=0) for p in range(planes)], axis=1
    )
    along_y = split_dot(stacked, ly_hi, ly_lo, False)
    joined = jnp.concatenate(
        [
            jnp.concatenate(
                [along_y[:size, p * size : (p + 1) * size], along_y[size:, p * size : (p + 1) * size]],
                axis=1,
            )
            for p in range(planes)
        ],
        axis=0,
    )
    out_ref[0] = split_dot(joined, rz_hi, rz_lo, True).reshape(planes, size, size)


def forward_planes(block, tables, plane_step, size, splits=1):
    planes, rows, cols = block.shape[1], block.shape[2], block.shape[3]
    tables = [part for t in tables for part in table_parts(t)]
    table_specs = [pl.BlockSpec(t.shape, lambda i: (0, 0)) for t in tables]
    step = size // splits
    outs = pl.pallas_call(
        forward_plane_kernel,
        grid=(planes // plane_step,),
        in_specs=[pl.BlockSpec((2, plane_step, rows, cols), lambda i: (0, i, 0, 0))] + table_specs,
        out_specs=[pl.BlockSpec((2, plane_step, step, size), lambda i: (0, i, 0, 0))] * splits,
        out_shape=[jax.ShapeDtypeStruct((2, planes, step, size), F32)] * splits,
    )(block, *tables)
    return outs if splits > 1 else outs[0]


def cross_kernel(*refs, blocks, sets, box, window, part):
    rec_refs = refs[:blocks]
    lig_ref = refs[blocks]
    g_hi, g_lo, gl_hi, gl_lo, h_hi, h_lo = [r[...] for r in refs[blocks + 1 : blocks + 7]]
    out_ref = refs[-1]
    rows = out_ref.shape[3]
    lanes = out_ref.shape[4]

    def gathered(ref, lo, count):
        turned = [jnp.swapaxes(ref[c, lo : lo + count], 0, 1) for c in range(2)]
        return jnp.concatenate(
            [jnp.concatenate([turned[0][r], turned[1][r]], axis=0) for r in range(rows)], axis=1
        )

    rec_in = jnp.concatenate(
        [gathered(rec_refs[b], 0, rec_refs[b].shape[1]) for b in range(blocks)], axis=0
    )
    rec = split_dot(rec_in, g_hi, g_lo, False)
    rec = jnp.concatenate([rec] * sets, axis=1)
    lig_in = jnp.concatenate([gathered(lig_ref, s * box, box) for s in range(sets)], axis=1)
    lig = split_dot(lig_in, gl_hi, gl_lo, False)
    rec_real = rec[:window]
    rec_imag = rec[window:]
    lig_real = lig[:window]
    lig_imag = lig[window:]
    prod = jnp.concatenate(
        [rec_real * lig_real + rec_imag * lig_imag, rec_imag * lig_real - rec_real * lig_imag],
        axis=0,
    )
    back = split_dot(prod, h_hi, h_lo, False)
    width = rows * lanes
    for s in range(sets):
        for c in range(2):
            pieces = jnp.stack(
                [
                    back[c * part : (c + 1) * part, s * width + r * lanes : s * width + (r + 1) * lanes]
                    for r in range(rows)
                ],
                axis=0,
            )
            out_ref[s, c] = jnp.swapaxes(pieces, 0, 1)


def cross_spectra(rec_blocks, lig_yz, g_tables, gl, hx, sets, box, window, row_step, lig_from):
    part = hx.shape[0] // 2
    size = rec_blocks[0].shape[2]
    offset = lig_from // row_step
    lanes = rec_blocks[0].shape[3]
    blocks = len(rec_blocks)
    tables = [np.concatenate(g_tables, axis=1), gl, hx]
    tables = [part for t in tables for part in table_parts(t)]
    kernel = functools.partial(
        cross_kernel, blocks=blocks, sets=sets, box=box, window=window, part=part
    )
    return pl.pallas_call(
        kernel,
        grid=(size // row_step,),
        in_specs=[pl.BlockSpec((2, b.shape[1], row_step, lanes), lambda i: (0, 0, i, 0)) for b in rec_blocks]
        + [pl.BlockSpec((2, sets * box, row_step, lanes), lambda i: (0, 0, i + offset, 0))]
        + [pl.BlockSpec(t.shape, lambda i: (0, 0)) for t in tables],
        out_specs=pl.BlockSpec((sets, 2, part, row_step, lanes), lambda i: (0, 0, 0, i, 0)),
        out_shape=jax.ShapeDtypeStruct((sets, 2, part, size, lanes), F32),
    )(*rec_blocks, lig_yz, *tables)


def inverse_planes(spectra, tables, plane_step):
    sets, planes, size = spectra[0].shape[0], spectra[0].shape[2], spectra[0].shape[4]
    ly_spec = pl.BlockSpec((2 * size, 2 * size), lambda s, i: (0, 0))
    rz_spec = pl.BlockSpec((2 * size, size), lambda s, i: (0, 0))
    return pl.pallas_call(
        inverse_plane_kernel,
        grid=(sets, planes // plane_step),
        in_specs=[
            pl.BlockSpec((1, 2, plane_step, x.shape[3], size), lambda s, i: (s, 0, i, 0, 0))
            for x in spectra
        ]
        + [ly_spec, ly_spec, rz_spec, rz_spec],
        out_specs=pl.BlockSpec((1, plane_step, size, size), lambda s, i: (s, i, 0, 0)),
        out_shape=jax.ShapeDtypeStruct((sets, planes, size, size), F32),
    )(*spectra, *[part for t in tables for part in table_parts(t)])


def gather_by_sum(piece, axis_name, dim):
    count = lax.axis_size(axis_name)
    index = lax.axis_index(axis_name)
    width = piece.shape[dim]
    shape = list(piece.shape)
    shape[dim] = width * count
    start = [0] * len(shape)
    start[dim] = index * width
    placed = lax.dynamic_update_slice(jnp.zeros(shape, piece.dtype), piece, start)
    return lax.psum(placed, axis_name)


def gather_pieces(piece, axis_name, dim):
    count = lax.axis_size(axis_name)
    if count & (count - 1):
        return gather_by_sum(piece, axis_name, dim)
    index = lax.axis_index(axis_name)
    held = piece
    step = 1
    while step < count:
        pairs = [(i, i ^ step) for i in range(count)]
        other = lax.ppermute(held, axis_name, perm=pairs)
        low_half = (index // step) % 2 == 0
        held = jnp.where(
            low_half,
            jnp.concatenate([held, other], axis=dim),
            jnp.concatenate([other, held], axis=dim),
        )
        step *= 2
    return held


def gather_direct(piece, axis_name, dim):
    count = lax.axis_size(axis_name)
    index = lax.axis_index(axis_name)
    held = [piece]
    for hop in range(1, count):
        pairs = [(i, (i + hop) % count) for i in range(count)]
        held.append(lax.ppermute(piece, axis_name, perm=pairs))
    stacked = jnp.stack(held, axis=0)
    order = (index - jnp.arange(count)) % count
    ordered = jnp.take(stacked, order, axis=0, mode="clip")
    ordered = jnp.moveaxis(ordered, 0, dim)
    shape = list(piece.shape)
    shape[dim] = shape[dim] * count
    return ordered.reshape(shape)


def score_grids(receptor, ligand_box, channel_weight):
    size = receptor.shape[2]
    slab_count = lax.axis_size("slab")
    part = receptor.shape[1]
    box = ligand_box.shape[4]
    sets = ligand_box.shape[0]
    extra = -(-(box - 1) // part)
    window = part * (1 + extra)
    plane_step = 8
    row_step = 16

    lead = ligand_box.shape[:4]
    dense = ligand_box.reshape(lead + (box * box,))
    full_box = gather_direct(dense, "slab", 3)
    cos_n, sin_n = phase_tables(size, size, size)
    rz = block2(cos_n, -sin_n, sin_n, cos_n)
    ly = block2(cos_n, sin_n, -sin_n, cos_n)
    splits = max(1, min(2, size // (2 * row_step)))
    own = forward_planes(receptor, (rz, ly), plane_step, size, splits)
    own = own if splits > 1 else [own]
    arrived = []
    for hop in range(1, extra + 1):
        pairs = [(i, (i - hop) % slab_count) for i in range(slab_count)]
        arrived.append([lax.ppermute(rows, "slab", perm=pairs) for rows in own])

    lig = jnp.stack(
        [full_box[:, 0, 0] * channel_weight[0], full_box[:, 0, 1] * channel_weight[1]], axis=0
    ).reshape(2, sets * box, box, box)
    cos_b, sin_b = phase_tables(box, size, size)
    rz_box = block2(cos_b, -sin_b, sin_b, cos_b)
    ly_box = block2(cos_b.T, sin_b.T, -sin_b.T, cos_b.T)
    lig_yz = forward_planes(lig, (rz_box, ly_box), 2 * plane_step, size)

    cos_w, sin_w = phase_tables(window, window, window)
    g_tables = []
    for index in range(1 + extra):
        cols = slice(index * part, (index + 1) * part)
        g_tables.append(block2(cos_w[:, cols], sin_w[:, cols], -sin_w[:, cols], cos_w[:, cols]))
    cos_xb, sin_xb = phase_tables(window, box, window)
    gl = block2(cos_xb, sin_xb, -sin_xb, cos_xb)
    cos_t, sin_t = phase_tables(part, window, window)
    scale = 1.0 / float(window * size * size)
    hx = (block2(cos_t, -sin_t, sin_t, cos_t) * scale).astype(np.float32)
    step = size // splits
    back_x = []
    for q in range(splits):
        rec_blocks = [own[q]] + [hop_rows[q] for hop_rows in arrived]
        back_x.append(
            cross_spectra(rec_blocks, lig_yz, g_tables, gl, hx, sets, box, window, row_step, q * step)
        )

    lyi = block2(cos_n, -sin_n, sin_n, cos_n)
    rzi = np.concatenate([cos_n, -sin_n], axis=0).astype(np.float32)
    inverse_tables = (lyi, rzi)
    grids = inverse_planes(back_x, inverse_tables, min(2 * plane_step, part))
    return grids.reshape(sets, 1, part, size, size), lig_yz


def pose_statistics(
    rotation_table,
    ligand_atoms,
    cluster_center,
    pose_rotation,
    pose_translation,
    pose_owner,
    pose_member,
    size,
):
    all_centers = gather_pieces(cluster_center, "rot", 0)
    local_count = cluster_center.shape[0]
    cluster = pose_owner[:, 0] * local_count + pose_member
    rotation = jnp.take(rotation_table, pose_rotation, axis=1, mode="clip").T.reshape(-1, 3, 3)
    coords = jnp.stack(
        [
            pose_translation // (size * size),
            pose_translation // size % size,
            pose_translation % size,
        ],
        axis=1,
    )
    shifts = ((coords + size // 2) % size - size // 2).astype(F32) / size
    center = jnp.take(all_centers, cluster, axis=0, mode="clip")
    moved = jnp.einsum("pjk,ka->pja", rotation, ligand_atoms, precision=PRECISE) + shifts[:, :, None]
    spread = moved - center
    mean_square = jnp.mean(jnp.sum(spread * spread, axis=1), axis=1)
    moved_centred = moved - jnp.mean(moved, axis=2, keepdims=True)
    center_centred = center - jnp.mean(center, axis=2, keepdims=True)
    covariance = jnp.einsum("pja,pka->pjk", moved_centred, center_centred, precision=PRECISE)
    stats = jnp.concatenate([covariance.reshape(-1, 9), mean_square[:, None]], axis=1)
    return stats.T


def local(
    receptor,
    ligand_box,
    channel_weight,
    rotation_table,
    ligand_atoms,
    cluster_center,
    pose_rotation,
    pose_translation,
    pose_owner,
    pose_member,
):
    size = receptor.shape[2]
    scores, first_rows = score_grids(receptor, ligand_box, channel_weight)
    cluster_center, first_rows = lax.optimization_barrier((cluster_center, first_rows))
    pose_stats = pose_statistics(
        rotation_table,
        ligand_atoms,
        cluster_center,
        pose_rotation,
        pose_translation,
        pose_owner,
        pose_member,
        size,
    )
    return (scores, pose_stats)


def solution(mesh):
    return jax.shard_map(
        local,
        mesh=mesh,
        in_specs=(
            P(None, "slab", None, None),
            P(None, "rot", None, "slab", None, None),
            P(),
            P(),
            P(),
            P("rot", None, None),
            P(("slab", "rot")),
            P(("slab", "rot")),
            P(("slab", "rot"), None),
            P(("slab", "rot")),
        ),
        out_specs=(P(None, "rot", "slab", None, None), P(None, ("slab", "rot"))),
        check_vma=False,
    )
```

```python
import functools

import jax
import jax.numpy as jnp
import ml_dtypes
import numpy as np
from jax import lax
from jax.experimental import pallas as pl
from jax.experimental.pallas import tpu as pltpu
from jax.sharding import PartitionSpec as P

PRECISE = lax.Precision.HIGHEST
SPLIT3 = lax.Precision.HIGH
TWO_PI = 6.283185307179586
F32 = jnp.float32
BF16 = jnp.bfloat16


def phase_tables(rows, cols, length):
    turns = np.outer(np.arange(rows), np.arange(cols)) % length
    phase = turns.astype(np.float64) * (TWO_PI / length)
    return (np.cos(phase), np.sin(phase))


def block2(top_left, top_right, bottom_left, bottom_right):
    top = np.concatenate([top_left, top_right], axis=1)
    bottom = np.concatenate([bottom_left, bottom_right], axis=1)
    return np.concatenate([top, bottom], axis=0).astype(np.float32)


def hi_lo(table):
    high = table.astype(BF16)
    low = (table - high.astype(F32)).astype(BF16)
    return high, low


def table_parts(table):
    high = table.astype(ml_dtypes.bfloat16)
    low = (table - high.astype(np.float32)).astype(ml_dtypes.bfloat16)
    return [high, low]


def split_dot(a, b_high, b_low, a_left):
    a_high = a.astype(BF16)
    a_low = (a - a_high.astype(F32)).astype(BF16)
    dot = functools.partial(jnp.dot, preferred_element_type=F32)
    if a_left:
        return dot(a_high, b_high) + (dot(a_low, b_high) + dot(a_high, b_low))
    return dot(b_high, a_high) + (dot(b_high, a_low) + dot(b_low, a_high))


def forward_plane_kernel(in_ref, rz_hi_ref, rz_lo_ref, ly_hi_ref, ly_lo_ref, *out_refs):
    planes, rows, cols = in_ref.shape[1], in_ref.shape[2], in_ref.shape[3]
    size = out_refs[0].shape[3]
    rz_hi, rz_lo = rz_hi_ref[...], rz_lo_ref[...]
    ly_hi, ly_lo = ly_hi_ref[...], ly_lo_ref[...]
    joined = jnp.concatenate(
        [in_ref[0].reshape(planes * rows, cols), in_ref[1].reshape(planes * rows, cols)], axis=1
    )
    along_z = split_dot(joined, rz_hi, rz_lo, True)
    stacked = jnp.concatenate(
        [
            jnp.concatenate(
                [along_z[p * rows : (p + 1) * rows, :size], along_z[p * rows : (p + 1) * rows, size:]],
                axis=0,
            )
            for p in range(planes)
        ],
        axis=1,
    )
    along_y = split_dot(stacked, ly_hi, ly_lo, False)
    step = size // len(out_refs)
    for q, out_ref in enumerate(out_refs):
        for p in range(planes):
            cols = slice(p * size, (p + 1) * size)
            out_ref[0, p] = along_y[q * step : (q + 1) * step, cols]
            out_ref[1, p] = along_y[size + q * step : size + (q + 1) * step, cols]


def inverse_plane_kernel(*refs):
    in_refs = refs[:-5]
    ly_hi_ref, ly_lo_ref, rz_hi_ref, rz_lo_ref, out_ref = refs[-5:]
    planes = in_refs[0].shape[2]
    size = in_refs[0].shape[4]
    ly_hi, ly_lo = ly_hi_ref[...], ly_lo_ref[...]
    rz_hi, rz_lo = rz_hi_ref[...], rz_lo_ref[...]

    def plane(c, p):
        return jnp.concatenate([r[0, c, p] for r in in_refs], axis=0)

    stacked = jnp.concatenate(
        [jnp.concatenate([plane(0, p), plane(1, p)], axis=0) for p in range(planes)], axis=1
    )
    along_y = split_dot(stacked, ly_hi, ly_lo, False)
    joined = jnp.concatenate(
        [
            jnp.concatenate(
                [along_y[:size, p * size : (p + 1) * size], along_y[size:, p * size : (p + 1) * size]],
                axis=1,
            )
            for p in range(planes)
        ],
        axis=0,
    )
    out_ref[0] = split_dot(joined, rz_hi, rz_lo, True).reshape(planes, size, size)


def forward_planes(block, tables, plane_step, size, splits=1):
    planes, rows, cols = block.shape[1], block.shape[2], block.shape[3]
    tables = [part for t in tables for part in table_parts(t)]
    table_specs = [pl.BlockSpec(t.shape, lambda i: (0, 0)) for t in tables]
    step = size // splits
    outs = pl.pallas_call(
        forward_plane_kernel,
        grid=(planes // plane_step,),
        in_specs=[pl.BlockSpec((2, plane_step, rows, cols), lambda i: (0, i, 0, 0))] + table_specs,
        out_specs=[pl.BlockSpec((2, plane_step, step, size), lambda i: (0, i, 0, 0))] * splits,
        out_shape=[jax.ShapeDtypeStruct((2, planes, step, size), F32)] * splits,
    )(block, *tables)
    return outs if splits > 1 else outs[0]


def cross_kernel(*refs, blocks, sets, box, window, part):
    rec_refs = refs[:blocks]
    lig_ref = refs[blocks]
    g_hi, g_lo, gl_hi, gl_lo, h_hi, h_lo = [r[...] for r in refs[blocks + 1 : blocks + 7]]
    out_ref = refs[-1]
    rows = out_ref.shape[3]
    lanes = out_ref.shape[4]

    def gathered(ref, lo, count):
        turned = [jnp.swapaxes(ref[c, lo : lo + count], 0, 1) for c in range(2)]
        return jnp.concatenate(
            [jnp.concatenate([turned[0][r], turned[1][r]], axis=0) for r in range(rows)], axis=1
        )

    rec_in = jnp.concatenate(
        [gathered(rec_refs[b], 0, rec_refs[b].shape[1]) for b in range(blocks)], axis=0
    )
    rec = split_dot(rec_in, g_hi, g_lo, False)
    rec = jnp.concatenate([rec] * sets, axis=1)
    lig_in = jnp.concatenate([gathered(lig_ref, s * box, box) for s in range(sets)], axis=1)
    lig = split_dot(lig_in, gl_hi, gl_lo, False)
    rec_real = rec[:window]
    rec_imag = rec[window:]
    lig_real = lig[:window]
    lig_imag = lig[window:]
    prod = jnp.concatenate(
        [rec_real * lig_real + rec_imag * lig_imag, rec_imag * lig_real - rec_real * lig_imag],
        axis=0,
    )
    back = split_dot(prod, h_hi, h_lo, False)
    width = rows * lanes
    for s in range(sets):
        for c in range(2):
            pieces = jnp.stack(
                [
                    back[c * part : (c + 1) * part, s * width + r * lanes : s * width + (r + 1) * lanes]
                    for r in range(rows)
                ],
                axis=0,
            )
            out_ref[s, c] = jnp.swapaxes(pieces, 0, 1)


def cross_spectra(rec_blocks, lig_yz, g_tables, gl, hx, sets, box, window, row_step, lig_from):
    part = hx.shape[0] // 2
    size = rec_blocks[0].shape[2]
    offset = lig_from // row_step
    lanes = rec_blocks[0].shape[3]
    blocks = len(rec_blocks)
    tables = [np.concatenate(g_tables, axis=1), gl, hx]
    tables = [part for t in tables for part in table_parts(t)]
    kernel = functools.partial(
        cross_kernel, blocks=blocks, sets=sets, box=box, window=window, part=part
    )
    return pl.pallas_call(
        kernel,
        grid=(size // row_step,),
        in_specs=[pl.BlockSpec((2, b.shape[1], row_step, lanes), lambda i: (0, 0, i, 0)) for b in rec_blocks]
        + [pl.BlockSpec((2, sets * box, row_step, lanes), lambda i: (0, 0, i + offset, 0))]
        + [pl.BlockSpec(t.shape, lambda i: (0, 0)) for t in tables],
        out_specs=pl.BlockSpec((sets, 2, part, row_step, lanes), lambda i: (0, 0, 0, i, 0)),
        out_shape=jax.ShapeDtypeStruct((sets, 2, part, size, lanes), F32),
    )(*rec_blocks, lig_yz, *tables)


def inverse_planes(spectra, tables, plane_step):
    sets, planes, size = spectra[0].shape[0], spectra[0].shape[2], spectra[0].shape[4]
    ly_spec = pl.BlockSpec((2 * size, 2 * size), lambda s, i: (0, 0))
    rz_spec = pl.BlockSpec((2 * size, size), lambda s, i: (0, 0))
    return pl.pallas_call(
        inverse_plane_kernel,
        grid=(sets, planes // plane_step),
        in_specs=[
            pl.BlockSpec((1, 2, plane_step, x.shape[3], size), lambda s, i: (s, 0, i, 0, 0))
            for x in spectra
        ]
        + [ly_spec, ly_spec, rz_spec, rz_spec],
        out_specs=pl.BlockSpec((1, plane_step, size, size), lambda s, i: (s, i, 0, 0)),
        out_shape=jax.ShapeDtypeStruct((sets, planes, size, size), F32),
    )(*spectra, *[part for t in tables for part in table_parts(t)])


def gather_by_sum(piece, axis_name, dim):
    count = lax.axis_size(axis_name)
    index = lax.axis_index(axis_name)
    width = piece.shape[dim]
    shape = list(piece.shape)
    shape[dim] = width * count
    start = [0] * len(shape)
    start[dim] = index * width
    placed = lax.dynamic_update_slice(jnp.zeros(shape, piece.dtype), piece, start)
    return lax.psum(placed, axis_name)


def gather_pieces(piece, axis_name, dim):
    count = lax.axis_size(axis_name)
    if count & (count - 1):
        return gather_by_sum(piece, axis_name, dim)
    index = lax.axis_index(axis_name)
    held = piece
    step = 1
    while step < count:
        pairs = [(i, i ^ step) for i in range(count)]
        other = lax.ppermute(held, axis_name, perm=pairs)
        low_half = (index // step) % 2 == 0
        held = jnp.where(
            low_half,
            jnp.concatenate([held, other], axis=dim),
            jnp.concatenate([other, held], axis=dim),
        )
        step *= 2
    return held


def gather_direct(piece, axis_name, dim):
    count = lax.axis_size(axis_name)
    index = lax.axis_index(axis_name)
    held = [piece]
    for hop in range(1, count):
        pairs = [(i, (i + hop) % count) for i in range(count)]
        held.append(lax.ppermute(piece, axis_name, perm=pairs))
    stacked = jnp.stack(held, axis=0)
    order = (index - jnp.arange(count)) % count
    ordered = jnp.take(stacked, order, axis=0, mode="clip")
    ordered = jnp.moveaxis(ordered, 0, dim)
    shape = list(piece.shape)
    shape[dim] = shape[dim] * count
    return ordered.reshape(shape)


def score_grids(receptor, ligand_box, channel_weight):
    size = receptor.shape[2]
    slab_count = lax.axis_size("slab")
    part = receptor.shape[1]
    box = ligand_box.shape[4]
    sets = ligand_box.shape[0]
    extra = -(-(box - 1) // part)
    window = part * (1 + extra)
    plane_step = 8
    row_step = 32

    lead = ligand_box.shape[:4]
    dense = ligand_box.reshape(lead + (box * box,))
    full_box = gather_direct(dense, "slab", 3)
    cos_n, sin_n = phase_tables(size, size, size)
    rz = block2(cos_n, -sin_n, sin_n, cos_n)
    ly = block2(cos_n, sin_n, -sin_n, cos_n)
    splits = max(1, min(2, size // (2 * row_step)))
    own = forward_planes(receptor, (rz, ly), plane_step, size, splits)
    own = own if splits > 1 else [own]
    arrived = []
    for hop in range(1, extra + 1):
        pairs = [(i, (i - hop) % slab_count) for i in range(slab_count)]
        arrived.append([lax.ppermute(rows, "slab", perm=pairs) for rows in own])

    lig = jnp.stack(
        [full_box[:, 0, 0] * channel_weight[0], full_box[:, 0, 1] * channel_weight[1]], axis=0
    ).reshape(2, sets * box, box, box)
    cos_b, sin_b = phase_tables(box, size, size)
    rz_box = block2(cos_b, -sin_b, sin_b, cos_b)
    ly_box = block2(cos_b.T, sin_b.T, -sin_b.T, cos_b.T)
    lig_yz = forward_planes(lig, (rz_box, ly_box), 2 * plane_step, size)

    cos_w, sin_w = phase_tables(window, window, window)
    g_tables = []
    for index in range(1 + extra):
        cols = slice(index * part, (index + 1) * part)
        g_tables.append(block2(cos_w[:, cols], sin_w[:, cols], -sin_w[:, cols], cos_w[:, cols]))
    cos_xb, sin_xb = phase_tables(window, box, window)
    gl = block2(cos_xb, sin_xb, -sin_xb, cos_xb)
    cos_t, sin_t = phase_tables(part, window, window)
    scale = 1.0 / float(window * size * size)
    hx = (block2(cos_t, -sin_t, sin_t, cos_t) * scale).astype(np.float32)
    step = size // splits
    back_x = []
    for q in range(splits):
        rec_blocks = [own[q]] + [hop_rows[q] for hop_rows in arrived]
        back_x.append(
            cross_spectra(rec_blocks, lig_yz, g_tables, gl, hx, sets, box, window, row_step, q * step)
        )

    lyi = block2(cos_n, -sin_n, sin_n, cos_n)
    rzi = np.concatenate([cos_n, -sin_n], axis=0).astype(np.float32)
    inverse_tables = (lyi, rzi)
    grids = inverse_planes(back_x, inverse_tables, min(2 * plane_step, part))
    return grids.reshape(sets, 1, part, size, size), lig_yz


def pose_statistics(
    rotation_table,
    ligand_atoms,
    cluster_center,
    pose_rotation,
    pose_translation,
    pose_owner,
    pose_member,
    size,
):
    all_centers = gather_pieces(cluster_center, "rot", 0)
    local_count = cluster_center.shape[0]
    cluster = pose_owner[:, 0] * local_count + pose_member
    rotation = jnp.take(rotation_table, pose_rotation, axis=1, mode="clip").T.reshape(-1, 3, 3)
    coords = jnp.stack(
        [
            pose_translation // (size * size),
            pose_translation // size % size,
            pose_translation % size,
        ],
        axis=1,
    )
    shifts = ((coords + size // 2) % size - size // 2).astype(F32) / size
    center = jnp.take(all_centers, cluster, axis=0, mode="clip")
    moved = jnp.einsum("pjk,ka->pja", rotation, ligand_atoms, precision=PRECISE) + shifts[:, :, None]
    spread = moved - center
    mean_square = jnp.mean(jnp.sum(spread * spread, axis=1), axis=1)
    moved_centred = moved - jnp.mean(moved, axis=2, keepdims=True)
    center_centred = center - jnp.mean(center, axis=2, keepdims=True)
    covariance = jnp.einsum("pja,pka->pjk", moved_centred, center_centred, precision=PRECISE)
    stats = jnp.concatenate([covariance.reshape(-1, 9), mean_square[:, None]], axis=1)
    return stats.T


def local(
    receptor,
    ligand_box,
    channel_weight,
    rotation_table,
    ligand_atoms,
    cluster_center,
    pose_rotation,
    pose_translation,
    pose_owner,
    pose_member,
):
    size = receptor.shape[2]
    scores, first_rows = score_grids(receptor, ligand_box, channel_weight)
    cluster_center, first_rows = lax.optimization_barrier((cluster_center, first_rows))
    pose_stats = pose_statistics(
        rotation_table,
        ligand_atoms,
        cluster_center,
        pose_rotation,
        pose_translation,
        pose_owner,
        pose_member,
        size,
    )
    return (scores, pose_stats)


def solution(mesh):
    return jax.shard_map(
        local,
        mesh=mesh,
        in_specs=(
            P(None, "slab", None, None),
            P(None, "rot", None, "slab", None, None),
            P(),
            P(),
            P(),
            P("rot", None, None),
            P(("slab", "rot")),
            P(("slab", "rot")),
            P(("slab", "rot"), None),
            P(("slab", "rot")),
        ),
        out_specs=(P(None, "rot", "slab", None, None), P(None, ("slab", "rot"))),
        check_vma=False,
    )
```
